32 devices in a mesh: groups: 2 (over y), dict: 8 (over z, x), section: 2 (over core).
Axes of the slice: x: 2, y: 2, z: 4, core: 2. Of those that a mesh axis runs over, the one named last changes fastest.
Arguments:
- cotangent: bfloat16 [256, 4608], P(('groups', 'dict')), parts along dimension 0, may hold values from -6 to 6
- routes: int32 [2, 256, 8], P('section', ('groups', 'dict')), parts along dimension 1, may hold values from 0 to 15, as said below
- acts: bfloat16 [2, 256, 1024], P('section', ('groups', 'dict')), parts along dimension 1, as said below
- decoder: bfloat16 [2, 2048, 4608], P('section', 'dict'), may hold values from -0.09375 to 0.09375
- encoder: bfloat16 [2, 2048, 4608], P('section', 'dict'), may hold values from -0.1875 to 0.1875
- gain: float32 [2, 4608], P('section'), may hold values from 0.3 to 3
- inv_rms: float32 [2, 256], P('section', ('groups', 'dict')), parts along dimension 1, may hold values from 0.3 to 3
Outputs:
- attributions: float32 [2, 256, 1024], P('section', ('groups', 'dict')), parts along dimension 1
- grads: bfloat16 [2, 256, 4608], P('section', ('groups', 'dict')), parts along dimension 1
The draws below stay inside these ranges and needn't reach their ends.
There are 2 independent parts, one for each index of `groups`. The reference program is written for one: setup_inputs(seed, part) draws one part's arguments, and reference() takes and returns one part's arrays. A program takes and returns all parts, laid end to end along the dimension named above; an argument that names none is the same for every part. Nothing has to cross between parts.
Inputs may be any that keep to these rules, and one draw needn't show every extreme that they name: `routes`: each row lists 8 blocks whose ranges b // 2 all differ; in each layer, among the 16 rows of one index of dict, every range is listed either 16 times or one time fewer, and some range exactly 16 times. `acts`: nonnegative, roughly half of the entries zero.
All inputs are finite; a program needn't handle non-finite values.
Results may differ from the reference program's by a relative error of at most 0.012.
Values may be sent and summed in bfloat16 or wider, within the bound.
No kernel may reach another device: no remote copies, remote signals or barrier semaphores. Data moves between devices by JAX's collectives and lax.ppermute only.
A program may use at most 64 MiB of HBM per device.

```python
import math
import jax
import jax.numpy as jnp
from jax import lax

D = 4608
BS = 128
BLK_DEV = 2
TOK_DEV = 16
ROWS = 128
NBLK = 16
LAYERS = 2
TOPB = 8


def draw_routes(key, part):
    holders = NBLK // BLK_DEV
    first, second = jax.random.split(jax.random.fold_in(key, 11))
    keys = jax.random.split(first, LAYERS * holders)
    orders = jax.vmap(lambda k: jax.random.permutation(k, holders))(keys).reshape(LAYERS, holders, holders)
    position = (jnp.arange(TOK_DEV, dtype=jnp.int32)[:, None] * TOPB + jnp.arange(TOPB, dtype=jnp.int32)[None, :]) % holders
    owners = orders[:, :, position]
    within = jax.random.randint(second, (LAYERS, holders, TOK_DEV, TOPB), 0, BLK_DEV, dtype=jnp.int32)
    blocks = owners.astype(jnp.int32) * BLK_DEV + within
    return blocks.reshape(LAYERS, ROWS, TOPB).astype(jnp.int32)


def draw_acts(key, part):
    first, second = jax.random.split(jax.random.fold_in(key, 7))
    shape = (LAYERS, ROWS, TOPB * BS)
    base = jnp.clip(jax.random.normal(first, shape, jnp.float32), -6.0, 6.0)
    spread = jnp.exp(jax.random.uniform(second, shape, jnp.float32, jnp.log(0.3), jnp.log(3.0)))
    return (jnp.maximum(base, 0.0) * spread).astype(jnp.bfloat16)


def shard_levels(key, dims, pieces, least, top_value):
    def one(dim, blocks):
        steps = jax.random.uniform(jax.random.fold_in(jax.random.fold_in(key, 6), dim), (blocks,), jnp.float32, least / len(pieces), top_value / len(pieces))
        return jnp.repeat(jnp.exp(steps), dims[dim] // blocks).reshape((-1,) + (1,) * (len(dims) - dim - 1))

    level = one(*pieces[0])
    for cut in pieces[1:]:
        level = level * one(*cut)
    return level


def noise(stream_key, shape, scale, most, shards=(), held_as=jnp.bfloat16):
    array = jax.random.normal(stream_key, shape, jnp.float32) * scale
    if len(shards) > 0:
        array = shard_levels(stream_key, shape, shards, -0.22, 0.18) * array
    return jnp.clip(array, min=-most, max=most).astype(held_as)


def setup_inputs(seed: int = 0, part: int = 0) -> dict:
    streams_of = jax.random.split(jax.random.key(seed), 8)
    part_splits = jax.random.split(jax.random.fold_in(streams_of[7], part), 8)
    cotangent = noise(part_splits[0], (ROWS, D), 1.0, 6.0, ((0, 8),))
    routes = draw_routes(jax.random.fold_in(jax.random.fold_in(streams_of[7], part), 71), part)
    acts = draw_acts(jax.random.fold_in(jax.random.fold_in(streams_of[7], part), 71), part)
    decoder = noise(streams_of[3], (LAYERS, NBLK * BS, D), D ** -0.5, 0.09375, ((0, 2), (1, 8)))
    encoder = noise(streams_of[4], (LAYERS, NBLK * BS, D), (TOPB * BS) ** -0.5, 0.1875, ((0, 2), (1, 8)))
    gain = jnp.clip(jnp.exp(math.log(3.0) - 2.3025851 * jax.random.uniform(streams_of[5], (LAYERS, D), jnp.float32) ** shard_levels(streams_of[5], (LAYERS, D), ((0, 2),), -0.2, 0.2)), 0.3, 3.0)
    inv_rms = jnp.clip(jnp.exp(math.log(3.0) - 2.3025851 * jax.random.uniform(part_splits[6], (LAYERS, ROWS), jnp.float32) ** shard_levels(part_splits[6], (LAYERS, ROWS), ((0, 2), (1, 8)), -0.2, 0.2)), 0.3, 3.0)
    return dict(cotangent=cotangent, routes=routes, acts=acts, decoder=decoder, encoder=encoder, gain=gain, inv_rms=inv_rms)


def reference(cotangent, routes, acts, decoder, encoder, gain, inv_rms):
    g_rows = cotangent
    attr_list = []
    grad_list = []
    for layer in reversed(range(LAYERS)):
        dec_blocks = decoder[layer].reshape(NBLK, BS, D)
        enc_blocks = encoder[layer].reshape(NBLK, BS, D)
        gain_row = gain[layer]

        def per_row(item):
            row_g, row_blocks, row_act, row_scale = item
            picked_dec = jnp.take(dec_blocks, row_blocks.astype(jnp.int32), axis=0).astype(jnp.float32)
            coef = jnp.einsum("kjd,d->kj", picked_dec, row_g.astype(jnp.float32)).astype(jnp.bfloat16)
            act_grid = row_act.reshape(TOPB, BS)
            dz = jnp.where(act_grid > 0, coef, jnp.zeros_like(coef))
            picked_enc = jnp.take(enc_blocks, row_blocks.astype(jnp.int32), axis=0).astype(jnp.float32)
            contrib = jnp.einsum("kj,kjd->kd", dz.astype(jnp.float32), picked_enc).astype(jnp.bfloat16)
            total = jnp.sum(contrib.astype(jnp.float32), axis=0)
            new_g = (row_g.astype(jnp.float32) + row_scale * gain_row * total).astype(jnp.bfloat16)
            attr = (act_grid.astype(jnp.float32) * coef.astype(jnp.float32)).reshape(TOPB * BS)
            return attr, new_g

        attr, g_rows = lax.map(per_row, (g_rows, routes[layer], acts[layer], inv_rms[layer]))
        attr_list.append(attr)
        grad_list.append(g_rows)
    attr_list = attr_list[::-1]
    grad_list = grad_list[::-1]
    return jnp.stack(attr_list, axis=0), jnp.stack(grad_list, axis=0)
```

```python
import jax
import jax.numpy as jnp
from jax import lax
from jax.sharding import PartitionSpec as P


def passed_along(block, axis, distance):
    devices = range(lax.axis_size(axis))
    route = [(i - distance, i) for i in devices if i - distance in devices]
    return lax.ppermute(block, axis, route)


def owner_work(recv_g, recv_act, dec_local, enc_local):
    width = recv_g.shape[-1]
    columns = dec_local.shape[0]
    flat_g = recv_g.reshape(-1, width)
    flat_act = recv_act.reshape(-1, columns)
    coef = lax.dot_general(
        flat_g, dec_local, (((1,), (1,)), ((), ())), preferred_element_type=jnp.float32
    ).astype(jnp.bfloat16)
    masked = jnp.where(flat_act > 0, coef, jnp.zeros_like(coef))
    contrib = jnp.dot(masked, enc_local, preferred_element_type=jnp.float32).astype(jnp.bfloat16)
    lead = recv_g.shape[:-1]
    return (coef.reshape(lead + (columns,)), contrib.reshape(lead + (width,)))


def layer_pass(g_rows, routes_l, acts_l, dec_local, enc_local, gain_l, scale_l, peers):
    tok_count, listed = routes_l.shape
    block = acts_l.shape[1] // listed
    width = dec_local.shape[1]
    held = dec_local.shape[0] // block
    slots_per = (tok_count * listed + peers - 1) // peers
    total_slots = peers * slots_per
    owner = routes_l // held
    within = routes_l - owner * held
    owners = jnp.arange(peers, dtype=jnp.int32)
    hits = (owner[:, :, None] == owners[None, None, :]).astype(jnp.int32)
    per_row = jnp.sum(hits, axis=1)
    earlier = jnp.cumsum(per_row, axis=0) - per_row
    place = jnp.sum(hits * earlier[:, None, :], axis=2)
    slot_of = (owner * slots_per + place).reshape(-1)
    slot_ids = jnp.arange(total_slots, dtype=jnp.int32)
    pick = (slot_ids[:, None] == slot_of[None, :]).astype(jnp.bfloat16)
    row_pick = jnp.sum(
        pick.reshape(total_slots, tok_count, listed).astype(jnp.float32), axis=2
    ).astype(jnp.bfloat16)
    send_g = jnp.dot(row_pick, g_rows, preferred_element_type=jnp.float32).astype(jnp.bfloat16)
    block_act = jnp.dot(
        pick, acts_l.reshape(tok_count * listed, block), preferred_element_type=jnp.float32
    ).astype(jnp.bfloat16)
    within_hot = (within.reshape(-1)[:, None] == jnp.arange(held, dtype=jnp.int32)[None, :]).astype(
        jnp.bfloat16
    )
    slot_within = jnp.dot(pick, within_hot, preferred_element_type=jnp.float32).astype(jnp.bfloat16)
    send_act = (slot_within[:, :, None] * block_act[:, None, :]).reshape(total_slots, held * block)
    send_g = send_g.reshape(peers, slots_per, width)
    send_act = send_act.reshape(peers, slots_per, held * block)
    recv_g, recv_act = (
        lax.all_to_all(send_g, "dict", split_axis=0, concat_axis=0, tiled=True),
        lax.all_to_all(send_act, "dict", split_axis=0, concat_axis=0, tiled=True),
    )
    coef_here, contrib_here = owner_work(recv_g, recv_act, dec_local, enc_local)
    coef_back, contrib_back = (
        lax.all_to_all(coef_here, "dict", split_axis=0, concat_axis=0, tiled=True),
        lax.all_to_all(contrib_here, "dict", split_axis=0, concat_axis=0, tiled=True),
    )
    coef_back = coef_back.reshape(total_slots, held, block)
    contrib_back = contrib_back.reshape(total_slots, width)
    coef_chosen = jnp.sum(
        slot_within.astype(jnp.float32)[:, :, None] * coef_back.astype(jnp.float32), axis=1
    ).astype(jnp.bfloat16)
    coef_rows = lax.dot_general(
        pick, coef_chosen, (((0,), (0,)), ((), ())), preferred_element_type=jnp.float32
    )
    attr = (acts_l.reshape(tok_count * listed, block).astype(jnp.float32) * coef_rows).reshape(
        tok_count, listed * block
    )
    summed = lax.dot_general(
        row_pick, contrib_back, (((0,), (0,)), ((), ())), preferred_element_type=jnp.float32
    )
    new_g = (g_rows.astype(jnp.float32) + scale_l[:, None] * gain_l[None, :] * summed).astype(
        jnp.bfloat16
    )
    return (attr, new_g)


def slot_device(cotangent, routes, acts, decoder, encoder, gain, inv_rms):
    peers = lax.axis_size("dict")
    depth = lax.axis_size("section")
    here = lax.axis_index("section")
    routes_l = routes[0]
    acts_l = acts[0]
    dec_local = decoder[0]
    enc_local = encoder[0]
    gain_l = gain[0]
    scale_l = inv_rms[0]
    tok_count, listed = routes_l.shape
    attr_keep = jnp.zeros((tok_count, acts_l.shape[1]), jnp.float32)
    grad_keep = jnp.zeros(cotangent.shape, jnp.bfloat16)
    g_new = cotangent
    for turn in range(depth):
        if turn > 0:
            g_now = passed_along(g_new, "section", -1)
        else:
            g_now = cotangent
        active = here == depth - 1 - turn
        attr, g_new = layer_pass(
            g_now, routes_l, acts_l, dec_local, enc_local, gain_l, scale_l, peers
        )
        attr_keep = jnp.where(active, attr, attr_keep)
        grad_keep = jnp.where(active, g_new, grad_keep)
    return (attr_keep[None], grad_keep[None])


def swap_cores(block):
    return lax.ppermute(block, "section", [(0, 1), (1, 0)])


def exchange(parts, sign):
    peers = parts.shape[0]
    moved = [parts[0]]
    for shift in range(1, peers):
        route = [(d, (d + sign * shift) % peers) for d in range(peers)]
        moved.append(lax.ppermute(parts[shift], "dict", route))
    return jnp.stack(moved, axis=0)


def split_layer(g_half, routes_l, acts_l, dec_half, enc_half, gain_half, scale_l):
    peers = lax.axis_size("dict")
    me = lax.axis_index("dict")
    rows, listed = routes_l.shape
    block = acts_l.shape[1] // listed
    held = dec_half.shape[0] // block
    half = g_half.shape[1]
    owner = routes_l // held
    within = routes_l - owner * held
    rel = (owner - me) % peers
    shifts = jnp.arange(peers, dtype=jnp.int32)
    spots = jnp.arange(held, dtype=jnp.int32)
    at_rel = (rel[:, :, None] == shifts[None, None, :]).astype(jnp.bfloat16)
    at_spot = (within[:, :, None] == spots[None, None, :]).astype(jnp.bfloat16)
    act_grid = acts_l.reshape(rows, listed, block)
    placed = jnp.einsum(
        "rks,rkw,rkj->srwj", at_rel, at_spot, act_grid, preferred_element_type=jnp.float32
    ).astype(jnp.bfloat16).reshape(peers, rows, held * block)
    sent = jnp.concatenate(
        [jnp.broadcast_to(g_half[None], (peers, rows, half)), placed], axis=-1
    )
    got = exchange(sent, 1).reshape(peers * rows, half + held * block)
    g_all = got[:, :half]
    act_all = got[:, half:]
    part = lax.dot_general(
        g_all, dec_half, (((1,), (1,)), ((), ())), preferred_element_type=jnp.float32
    )
    coef = (part + swap_cores(part)).astype(jnp.bfloat16)
    dz = jnp.where(act_all > 0, coef, jnp.zeros_like(coef))
    contrib = jnp.dot(dz, enc_half, preferred_element_type=jnp.float32).astype(jnp.bfloat16)
    dz_pick = dz[:, :block]
    for spot in range(1, held):
        dz_pick = dz_pick + dz[:, spot * block:(spot + 1) * block]
    back = jnp.concatenate([contrib, dz_pick], axis=-1).reshape(peers, rows, half + block)
    returned = exchange(back, -1)
    total = jnp.sum(returned[:, :, :half].astype(jnp.float32), axis=0)
    dz_back = returned[:, :, half:]
    dz_slot = jnp.einsum("rks,srj->rkj", at_rel, dz_back, preferred_element_type=jnp.float32)
    attr = (act_grid.astype(jnp.float32) * dz_slot).reshape(rows, listed * block)
    new_half = (g_half.astype(jnp.float32) + scale_l[:, None] * gain_half[None, :] * total).astype(
        jnp.bfloat16
    )
    return attr, new_half


def split_device(cotangent, routes, acts, decoder, encoder, gain, inv_rms):
    depth = lax.axis_size("section")
    here = lax.axis_index("section")
    rows, width = cotangent.shape
    half = width // depth
    mine = here * half
    theirs = (1 - here) * half
    weights = jnp.stack([decoder[0], encoder[0]], axis=0)
    own_w = lax.dynamic_slice_in_dim(weights, mine, half, axis=2)
    other_w = swap_cores(lax.dynamic_slice_in_dim(weights, theirs, half, axis=2))
    small = jnp.concatenate(
        [gain[0], inv_rms[0], routes[0].reshape(-1).astype(jnp.float32)], axis=0
    )
    other_small = swap_cores(small)
    other_acts = swap_cores(acts[0])
    attr_keep = jnp.zeros((rows, acts.shape[2]), jnp.float32)
    grad_keep = jnp.zeros(cotangent.shape, jnp.bfloat16)
    g_half = lax.dynamic_slice_in_dim(cotangent, mine, half, axis=1)
    for layer in reversed(range(depth)):
        is_own = here == layer
        w = jnp.where(is_own, own_w, other_w)
        s = jnp.where(is_own, small, other_small)
        acts_l = jnp.where(is_own, acts[0], other_acts)
        gain_half = lax.dynamic_slice_in_dim(s[:width], mine, half, axis=0)
        scale_l = s[width:width + rows]
        routes_l = s[width + rows:].astype(jnp.int32).reshape(routes.shape[1:])
        attr, g_half = split_layer(g_half, routes_l, acts_l, w[0], w[1], gain_half, scale_l)
        partner = swap_cores(g_half)
        full = jnp.where(
            here == 0,
            jnp.concatenate([g_half, partner], axis=1),
            jnp.concatenate([partner, g_half], axis=1),
        )
        attr_keep = jnp.where(is_own, attr, attr_keep)
        grad_keep = jnp.where(is_own, full, grad_keep)
    return (attr_keep[None], grad_keep[None])


def per_device(cotangent, routes, acts, decoder, encoder, gain, inv_rms):
    peers = lax.axis_size("dict")
    depth = lax.axis_size("section")
    listed = routes.shape[-1]
    width = cotangent.shape[1]
    if listed == peers and depth == 2 and width % (depth * 128) == 0:
        return split_device(cotangent, routes, acts, decoder, encoder, gain, inv_rms)
    return slot_device(cotangent, routes, acts, decoder, encoder, gain, inv_rms)


def solution(mesh):
    placed = (
        P(("groups", "dict"), None),
        P("section", ("groups", "dict"), None),
        P("section", ("groups", "dict"), None),
        P("section", "dict", None),
        P("section", "dict", None),
        P("section", None),
        P("section", ("groups", "dict")),
    )
    return jax.shard_map(
        per_device,
        mesh=mesh,
        in_specs=placed,
        out_specs=(P("section", ("groups", "dict"), None), P("section", ("groups", "dict"), None)),
        check_vma=False,
    )
```

```python
import jax
import jax.numpy as jnp
from jax import lax
from jax.sharding import PartitionSpec as P


def passed_along(block, axis, distance):
    devices = range(lax.axis_size(axis))
    route = [(i - distance, i) for i in devices if i - distance in devices]
    return lax.ppermute(block, axis, route)


def owner_work(recv_g, recv_act, dec_local, enc_local):
    width = recv_g.shape[-1]
    columns = dec_local.shape[0]
    flat_g = recv_g.reshape(-1, width)
    flat_act = recv_act.reshape(-1, columns)
    coef = lax.dot_general(
        flat_g, dec_local, (((1,), (1,)), ((), ())), preferred_element_type=jnp.float32
    ).astype(jnp.bfloat16)
    masked = jnp.where(flat_act > 0, coef, jnp.zeros_like(coef))
    contrib = jnp.dot(masked, enc_local, preferred_element_type=jnp.float32).astype(jnp.bfloat16)
    lead = recv_g.shape[:-1]
    return (coef.reshape(lead + (columns,)), contrib.reshape(lead + (width,)))


def layer_pass(g_rows, routes_l, acts_l, dec_local, enc_local, gain_l, scale_l, peers):
    tok_count, listed = routes_l.shape
    block = acts_l.shape[1] // listed
    width = dec_local.shape[1]
    held = dec_local.shape[0] // block
    slots_per = (tok_count * listed + peers - 1) // peers
    total_slots = peers * slots_per
    owner = routes_l // held
    within = routes_l - owner * held
    owners = jnp.arange(peers, dtype=jnp.int32)
    hits = (owner[:, :, None] == owners[None, None, :]).astype(jnp.int32)
    per_row = jnp.sum(hits, axis=1)
    earlier = jnp.cumsum(per_row, axis=0) - per_row
    place = jnp.sum(hits * earlier[:, None, :], axis=2)
    slot_of = (owner * slots_per + place).reshape(-1)
    slot_ids = jnp.arange(total_slots, dtype=jnp.int32)
    pick = (slot_ids[:, None] == slot_of[None, :]).astype(jnp.bfloat16)
    row_pick = jnp.sum(
        pick.reshape(total_slots, tok_count, listed).astype(jnp.float32), axis=2
    ).astype(jnp.bfloat16)
    send_g = jnp.dot(row_pick, g_rows, preferred_element_type=jnp.float32).astype(jnp.bfloat16)
    block_act = jnp.dot(
        pick, acts_l.reshape(tok_count * listed, block), preferred_element_type=jnp.float32
    ).astype(jnp.bfloat16)
    within_hot = (within.reshape(-1)[:, None] == jnp.arange(held, dtype=jnp.int32)[None, :]).astype(
        jnp.bfloat16
    )
    slot_within = jnp.dot(pick, within_hot, preferred_element_type=jnp.float32).astype(jnp.bfloat16)
    send_act = (slot_within[:, :, None] * block_act[:, None, :]).reshape(total_slots, held * block)
    send_g = send_g.reshape(peers, slots_per, width)
    send_act = send_act.reshape(peers, slots_per, held * block)
    recv_g, recv_act = (
        lax.all_to_all(send_g, "dict", split_axis=0, concat_axis=0, tiled=True),
        lax.all_to_all(send_act, "dict", split_axis=0, concat_axis=0, tiled=True),
    )
    coef_here, contrib_here = owner_work(recv_g, recv_act, dec_local, enc_local)
    coef_back, contrib_back = (
        lax.all_to_all(coef_here, "dict", split_axis=0, concat_axis=0, tiled=True),
        lax.all_to_all(contrib_here, "dict", split_axis=0, concat_axis=0, tiled=True),
    )
    coef_back = coef_back.reshape(total_slots, held, block)
    contrib_back = contrib_back.reshape(total_slots, width)
    coef_chosen = jnp.sum(
        slot_within.astype(jnp.float32)[:, :, None] * coef_back.astype(jnp.float32), axis=1
    ).astype(jnp.bfloat16)
    coef_rows = lax.dot_general(
        pick, coef_chosen, (((0,), (0,)), ((), ())), preferred_element_type=jnp.float32
    )
    attr = (acts_l.reshape(tok_count * listed, block).astype(jnp.float32) * coef_rows).reshape(
        tok_count, listed * block
    )
    summed = lax.dot_general(
        row_pick, contrib_back, (((0,), (0,)), ((), ())), preferred_element_type=jnp.float32
    )
    new_g = (g_rows.astype(jnp.float32) + scale_l[:, None] * gain_l[None, :] * summed).astype(
        jnp.bfloat16
    )
    return (attr, new_g)


def slot_device(cotangent, routes, acts, decoder, encoder, gain, inv_rms):
    peers = lax.axis_size("dict")
    depth = lax.axis_size("section")
    here = lax.axis_index("section")
    routes_l = routes[0]
    acts_l = acts[0]
    dec_local = decoder[0]
    enc_local = encoder[0]
    gain_l = gain[0]
    scale_l = inv_rms[0]
    tok_count, listed = routes_l.shape
    attr_keep = jnp.zeros((tok_count, acts_l.shape[1]), jnp.float32)
    grad_keep = jnp.zeros(cotangent.shape, jnp.bfloat16)
    g_new = cotangent
    for turn in range(depth):
        if turn > 0:
            g_now = passed_along(g_new, "section", -1)
        else:
            g_now = cotangent
        active = here == depth - 1 - turn
        attr, g_new = layer_pass(
            g_now, routes_l, acts_l, dec_local, enc_local, gain_l, scale_l, peers
        )
        attr_keep = jnp.where(active, attr, attr_keep)
        grad_keep = jnp.where(active, g_new, grad_keep)
    return (attr_keep[None], grad_keep[None])


def swap_cores(block):
    return lax.ppermute(block, "section", [(0, 1), (1, 0)])


def exchange(parts, sign):
    peers = parts.shape[0]
    moved = [parts[0]]
    for shift in range(1, peers):
        route = [(d, (d + sign * shift) % peers) for d in range(peers)]
        moved.append(lax.ppermute(parts[shift], "dict", route))
    return jnp.stack(moved, axis=0)


def split_layer(g_half, routes_l, acts_l, own, other, is_own, gain_half, scale_l):
    peers = lax.axis_size("dict")
    me = lax.axis_index("dict")
    rows, listed = routes_l.shape
    block = acts_l.shape[1] // listed
    held = own[0].shape[0] // block
    half = g_half.shape[1]
    owner = routes_l // held
    within = routes_l - owner * held
    rel = (owner - me) % peers
    shifts = jnp.arange(peers, dtype=jnp.int32)
    spots = jnp.arange(held, dtype=jnp.int32)
    at_rel = (rel[:, :, None] == shifts[None, None, :]).astype(jnp.bfloat16)
    at_spot = (within[:, :, None] == spots[None, None, :]).astype(jnp.bfloat16)
    act_grid = acts_l.reshape(rows, listed, block)
    placed = jnp.einsum(
        "rks,rkw,rkj->srwj", at_rel, at_spot, act_grid, preferred_element_type=jnp.float32
    ).astype(jnp.bfloat16).reshape(peers, rows, held * block)
    sent = jnp.concatenate(
        [jnp.broadcast_to(g_half[None], (peers, rows, half)), placed], axis=-1
    )
    got = exchange(sent, 1).reshape(peers * rows, half + held * block)
    g_all = got[:, :half]
    act_all = got[:, half:]

    def with_dec(dec):
        return lax.dot_general(
            g_all, dec, (((1,), (1,)), ((), ())), preferred_element_type=jnp.float32
        )

    part = jnp.where(is_own, with_dec(own[0]), with_dec(other[0]))
    paired = swap_cores(jnp.concatenate([part, act_all.astype(jnp.float32)], axis=1))
    coef = (part + paired[:, :held * block]).astype(jnp.bfloat16)
    act_used = jnp.where(is_own, act_all.astype(jnp.float32), paired[:, held * block:])
    dz = jnp.where(act_used > 0, coef, jnp.zeros_like(coef))

    def with_enc(enc):
        return jnp.dot(dz, enc, preferred_element_type=jnp.float32)

    contrib = jnp.where(is_own, with_enc(own[1]), with_enc(other[1])).astype(jnp.bfloat16)
    dz_pick = dz[:, :block]
    for spot in range(1, held):
        dz_pick = dz_pick + dz[:, spot * block:(spot + 1) * block]
    back = jnp.concatenate([contrib, dz_pick], axis=-1).reshape(peers, rows, half + block)
    returned = exchange(back, -1)
    total = jnp.sum(returned[:, :, :half].astype(jnp.float32), axis=0)
    dz_back = returned[:, :, half:]
    dz_slot = jnp.einsum("rks,srj->rkj", at_rel, dz_back, preferred_element_type=jnp.float32)
    attr = (act_grid.astype(jnp.float32) * dz_slot).reshape(rows, listed * block)
    new_half = (g_half.astype(jnp.float32) + scale_l[:, None] * gain_half[None, :] * total).astype(
        jnp.bfloat16
    )
    return attr, new_half


def split_device(cotangent, routes, acts, decoder, encoder, gain, inv_rms):
    depth = lax.axis_size("section")
    here = lax.axis_index("section")
    rows, width = cotangent.shape
    blocks = decoder.shape[1]
    half = width // depth
    mine = here * half
    theirs = (1 - here) * half
    small = jnp.concatenate([gain[0], inv_rms[0]], axis=0)
    other_small = swap_cores(small)
    sent_w = jnp.concatenate(
        [
            lax.dynamic_slice_in_dim(decoder[0], theirs, half, axis=1),
            lax.dynamic_slice_in_dim(encoder[0], theirs, half, axis=1),
        ],
        axis=0,
    )
    other_w = swap_cores(sent_w)
    other = (other_w[:blocks], other_w[blocks:])
    own = (
        lax.dynamic_slice_in_dim(decoder[0], mine, half, axis=1),
        lax.dynamic_slice_in_dim(encoder[0], mine, half, axis=1),
    )
    attr_keep = jnp.zeros((rows, acts.shape[2]), jnp.float32)
    grad_keep = jnp.zeros(cotangent.shape, jnp.bfloat16)
    g_half = lax.dynamic_slice_in_dim(cotangent, mine, half, axis=1)
    for layer in reversed(range(depth)):
        is_own = here == layer
        s = jnp.where(is_own, small, other_small)
        gain_half = lax.dynamic_slice_in_dim(s[:width], mine, half, axis=0)
        scale_l = s[width:width + rows]
        attr, g_half = split_layer(g_half, routes[0], acts[0], own, other, is_own, gain_half, scale_l)
        partner = swap_cores(g_half)
        full = jnp.where(
            here == 0,
            jnp.concatenate([g_half, partner], axis=1),
            jnp.concatenate([partner, g_half], axis=1),
        )
        attr_keep = jnp.where(is_own, attr, attr_keep)
        grad_keep = jnp.where(is_own, full, grad_keep)
    return (attr_keep[None], grad_keep[None])


def per_device(cotangent, routes, acts, decoder, encoder, gain, inv_rms):
    peers = lax.axis_size("dict")
    depth = lax.axis_size("section")
    listed = routes.shape[-1]
    width = cotangent.shape[1]
    if listed == peers and depth == 2 and width % (depth * 128) == 0:
        return split_device(cotangent, routes, acts, decoder, encoder, gain, inv_rms)
    return slot_device(cotangent, routes, acts, decoder, encoder, gain, inv_rms)


def solution(mesh):
    placed = (
        P(("groups", "dict"), None),
        P("section", ("groups", "dict"), None),
        P("section", ("groups", "dict"), None),
        P("section", "dict", None),
        P("section", "dict", None),
        P("section", None),
        P("section", ("groups", "dict")),
    )
    return jax.shard_map(
        per_device,
        mesh=mesh,
        in_specs=placed,
        out_specs=(P("section", ("groups", "dict"), None), P("section", ("groups", "dict"), None)),
        check_vma=False,
    )
```

```python
import jax
import jax.numpy as jnp
from jax import lax
from jax.sharding import PartitionSpec as P


def passed_along(block, axis, distance):
    devices = range(lax.axis_size(axis))
    route = [(i - distance, i) for i in devices if i - distance in devices]
    return lax.ppermute(block, axis, route)


def owner_work(recv_g, recv_act, dec_local, enc_local):
    width = recv_g.shape[-1]
    columns = dec_local.shape[0]
    flat_g = recv_g.reshape(-1, width)
    flat_act = recv_act.reshape(-1, columns)
    coef = lax.dot_general(
        flat_g, dec_local, (((1,), (1,)), ((), ())), preferred_element_type=jnp.float32
    ).astype(jnp.bfloat16)
    masked = jnp.where(flat_act > 0, coef, jnp.zeros_like(coef))
    contrib = jnp.dot(masked, enc_local, preferred_element_type=jnp.float32).astype(jnp.bfloat16)
    lead = recv_g.shape[:-1]
    return (coef.reshape(lead + (columns,)), contrib.reshape(lead + (width,)))


def layer_pass(g_rows, routes_l, acts_l, dec_local, enc_local, gain_l, scale_l, peers):
    tok_count, listed = routes_l.shape
    block = acts_l.shape[1] // listed
    width = dec_local.shape[1]
    held = dec_local.shape[0] // block
    slots_per = (tok_count * listed + peers - 1) // peers
    total_slots = peers * slots_per
    owner = routes_l // held
    within = routes_l - owner * held
    owners = jnp.arange(peers, dtype=jnp.int32)
    hits = (owner[:, :, None] == owners[None, None, :]).astype(jnp.int32)
    per_row = jnp.sum(hits, axis=1)
    earlier = jnp.cumsum(per_row, axis=0) - per_row
    place = jnp.sum(hits * earlier[:, None, :], axis=2)
    slot_of = (owner * slots_per + place).reshape(-1)
    slot_ids = jnp.arange(total_slots, dtype=jnp.int32)
    pick = (slot_ids[:, None] == slot_of[None, :]).astype(jnp.bfloat16)
    row_pick = jnp.sum(
        pick.reshape(total_slots, tok_count, listed).astype(jnp.float32), axis=2
    ).astype(jnp.bfloat16)
    send_g = jnp.dot(row_pick, g_rows, preferred_element_type=jnp.float32).astype(jnp.bfloat16)
    block_act = jnp.dot(
        pick, acts_l.reshape(tok_count * listed, block), preferred_element_type=jnp.float32
    ).astype(jnp.bfloat16)
    within_hot = (within.reshape(-1)[:, None] == jnp.arange(held, dtype=jnp.int32)[None, :]).astype(
        jnp.bfloat16
    )
    slot_within = jnp.dot(pick, within_hot, preferred_element_type=jnp.float32).astype(jnp.bfloat16)
    send_act = (slot_within[:, :, None] * block_act[:, None, :]).reshape(total_slots, held * block)
    send_g = send_g.reshape(peers, slots_per, width)
    send_act = send_act.reshape(peers, slots_per, held * block)
    recv_g, recv_act = (
        lax.all_to_all(send_g, "dict", split_axis=0, concat_axis=0, tiled=True),
        lax.all_to_all(send_act, "dict", split_axis=0, concat_axis=0, tiled=True),
    )
    coef_here, contrib_here = owner_work(recv_g, recv_act, dec_local, enc_local)
    coef_back, contrib_back = (
        lax.all_to_all(coef_here, "dict", split_axis=0, concat_axis=0, tiled=True),
        lax.all_to_all(contrib_here, "dict", split_axis=0, concat_axis=0, tiled=True),
    )
    coef_back = coef_back.reshape(total_slots, held, block)
    contrib_back = contrib_back.reshape(total_slots, width)
    coef_chosen = jnp.sum(
        slot_within.astype(jnp.float32)[:, :, None] * coef_back.astype(jnp.float32), axis=1
    ).astype(jnp.bfloat16)
    coef_rows = lax.dot_general(
        pick, coef_chosen, (((0,), (0,)), ((), ())), preferred_element_type=jnp.float32
    )
    attr = (acts_l.reshape(tok_count * listed, block).astype(jnp.float32) * coef_rows).reshape(
        tok_count, listed * block
    )
    summed = lax.dot_general(
        row_pick, contrib_back, (((0,), (0,)), ((), ())), preferred_element_type=jnp.float32
    )
    new_g = (g_rows.astype(jnp.float32) + scale_l[:, None] * gain_l[None, :] * summed).astype(
        jnp.bfloat16
    )
    return (attr, new_g)


def slot_device(cotangent, routes, acts, decoder, encoder, gain, inv_rms):
    peers = lax.axis_size("dict")
    depth = lax.axis_size("section")
    here = lax.axis_index("section")
    routes_l = routes[0]
    acts_l = acts[0]
    dec_local = decoder[0]
    enc_local = encoder[0]
    gain_l = gain[0]
    scale_l = inv_rms[0]
    tok_count, listed = routes_l.shape
    attr_keep = jnp.zeros((tok_count, acts_l.shape[1]), jnp.float32)
    grad_keep = jnp.zeros(cotangent.shape, jnp.bfloat16)
    g_new = cotangent
    for turn in range(depth):
        if turn > 0:
            g_now = passed_along(g_new, "section", -1)
        else:
            g_now = cotangent
        active = here == depth - 1 - turn
        attr, g_new = layer_pass(
            g_now, routes_l, acts_l, dec_local, enc_local, gain_l, scale_l, peers
        )
        attr_keep = jnp.where(active, attr, attr_keep)
        grad_keep = jnp.where(active, g_new, grad_keep)
    return (attr_keep[None], grad_keep[None])


def swap_cores(block):
    return lax.ppermute(block, "section", [(0, 1), (1, 0)])


def exchange(parts, sign):
    peers = parts.shape[0]
    moved = [parts[0]]
    for shift in range(1, peers):
        route = [(d, (d + sign * shift) % peers) for d in range(peers)]
        moved.append(lax.ppermute(parts[shift], "dict", route))
    return jnp.stack(moved, axis=0)


def split_layer(g_half, routes_l, acts_l, own, other, is_own, gain_half, scale_l):
    peers = lax.axis_size("dict")
    me = lax.axis_index("dict")
    rows, listed = routes_l.shape
    block = acts_l.shape[1] // listed
    held = own[0].shape[0] // block
    half = g_half.shape[1]
    owner = routes_l // held
    within = routes_l - owner * held
    rel = (owner - me) % peers
    shifts = jnp.arange(peers, dtype=jnp.int32)
    spots = jnp.arange(held, dtype=jnp.int32)
    at_rel = (rel[:, :, None] == shifts[None, None, :]).astype(jnp.bfloat16)
    at_spot = (within[:, :, None] == spots[None, None, :]).astype(jnp.bfloat16)
    act_grid = acts_l.reshape(rows, listed, block)
    placed = jnp.einsum(
        "rks,rkw,rkj->srwj", at_rel, at_spot, act_grid, preferred_element_type=jnp.float32
    ).astype(jnp.bfloat16).reshape(peers, rows, held * block)
    sent = jnp.concatenate(
        [jnp.broadcast_to(g_half[None], (peers, rows, half)), placed], axis=-1
    )
    got = exchange(sent, 1).reshape(peers * rows, half + held * block)
    g_all = got[:, :half]
    act_all = got[:, half:]

    def with_dec(dec):
        return lax.dot_general(
            g_all, dec, (((1,), (1,)), ((), ())), preferred_element_type=jnp.float32
        )

    on_first = lax.axis_index("section") == 0
    part = jnp.where(on_first, with_dec(own[0]), with_dec(other[0]))
    paired = swap_cores(jnp.concatenate([part, act_all.astype(jnp.float32)], axis=1))
    coef = (part + paired[:, :held * block]).astype(jnp.bfloat16)
    act_used = jnp.where(is_own, act_all.astype(jnp.float32), paired[:, held * block:])
    dz = jnp.where(act_used > 0, coef, jnp.zeros_like(coef))

    def with_enc(enc):
        return jnp.dot(dz, enc, preferred_element_type=jnp.float32)

    contrib = jnp.where(on_first, with_enc(own[1]), with_enc(other[1])).astype(jnp.bfloat16)
    dz_pick = dz[:, :block]
    for spot in range(1, held):
        dz_pick = dz_pick + dz[:, spot * block:(spot + 1) * block]
    back = jnp.concatenate([contrib, dz_pick], axis=-1).reshape(peers, rows, half + block)
    returned = exchange(back, -1)
    total = jnp.sum(returned[:, :, :half].astype(jnp.float32), axis=0)
    dz_back = returned[:, :, half:]
    dz_slot = jnp.einsum("rks,srj->rkj", at_rel, dz_back, preferred_element_type=jnp.float32)
    attr = (act_grid.astype(jnp.float32) * dz_slot).reshape(rows, listed * block)
    new_half = (g_half.astype(jnp.float32) + scale_l[:, None] * gain_half[None, :] * total).astype(
        jnp.bfloat16
    )
    return attr, new_half


def split_device(cotangent, routes, acts, decoder, encoder, gain, inv_rms):
    depth = lax.axis_size("section")
    here = lax.axis_index("section")
    rows, width = cotangent.shape
    blocks = decoder.shape[1]
    half = width // depth
    mine = here * half
    theirs = (1 - here) * half
    small = jnp.concatenate([gain[0], inv_rms[0]], axis=0)
    other_small = swap_cores(small)
    dec_here, enc_here = decoder[0], encoder[0]
    dec_there, enc_there = swap_cores(dec_here), swap_cores(enc_here)
    attr_keep = jnp.zeros((rows, acts.shape[2]), jnp.float32)
    grad_keep = jnp.zeros(cotangent.shape, jnp.bfloat16)
    g_half = lax.dynamic_slice_in_dim(cotangent, mine, half, axis=1)
    for layer in reversed(range(depth)):
        is_own = here == layer
        s = jnp.where(is_own, small, other_small)
        gain_half = lax.dynamic_slice_in_dim(s[:width], mine, half, axis=0)
        scale_l = s[width:width + rows]
        if layer == 0:
            first, second = (dec_here, enc_here), (dec_there, enc_there)
        else:
            first, second = (dec_there, enc_there), (dec_here, enc_here)
        first = (first[0][:, :half], first[1][:, :half])
        second = (second[0][:, half:], second[1][:, half:])
        attr, g_half = split_layer(
            g_half, routes[0], acts[0], first, second, is_own, gain_half, scale_l
        )
        partner = swap_cores(g_half)
        full = jnp.where(
            here == 0,
            jnp.concatenate([g_half, partner], axis=1),
            jnp.concatenate([partner, g_half], axis=1),
        )
        attr_keep = jnp.where(is_own, attr, attr_keep)
        grad_keep = jnp.where(is_own, full, grad_keep)
    return (attr_keep[None], grad_keep[None])


def per_device(cotangent, routes, acts, decoder, encoder, gain, inv_rms):
    peers = lax.axis_size("dict")
    depth = lax.axis_size("section")
    listed = routes.shape[-1]
    width = cotangent.shape[1]
    if listed == peers and depth == 2 and width % (depth * 128) == 0:
        return split_device(cotangent, routes, acts, decoder, encoder, gain, inv_rms)
    return slot_device(cotangent, routes, acts, decoder, encoder, gain, inv_rms)


def solution(mesh):
    placed = (
        P(("groups", "dict"), None),
        P("section", ("groups", "dict"), None),
        P("section", ("groups", "dict"), None),
        P("section", "dict", None),
        P("section", "dict", None),
        P("section", None),
        P("section", ("groups", "dict")),
    )
    return jax.shard_map(
        per_device,
        mesh=mesh,
        in_specs=placed,
        out_specs=(P("section", ("groups", "dict"), None), P("section", ("groups", "dict"), None)),
        check_vma=False,
    )
```

```python
import jax
import jax.numpy as jnp
from jax import lax
from jax.sharding import PartitionSpec as P


def passed_along(block, axis, distance):
    devices = range(lax.axis_size(axis))
    route = [(i - distance, i) for i in devices if i - distance in devices]
    return lax.ppermute(block, axis, route)


def owner_work(recv_g, recv_act, dec_local, enc_local):
    width = recv_g.shape[-1]
    columns = dec_local.shape[0]
    flat_g = recv_g.reshape(-1, width)
    flat_act = recv_act.reshape(-1, columns)
    coef = lax.dot_general(
        flat_g, dec_local, (((1,), (1,)), ((), ())), preferred_element_type=jnp.float32
    ).astype(jnp.bfloat16)
    masked = jnp.where(flat_act > 0, coef, jnp.zeros_like(coef))
    contrib = jnp.dot(masked, enc_local, preferred_element_type=jnp.float32).astype(jnp.bfloat16)
    lead = recv_g.shape[:-1]
    return (coef.reshape(lead + (columns,)), contrib.reshape(lead + (width,)))


def layer_pass(g_rows, routes_l, acts_l, dec_local, enc_local, gain_l, scale_l, peers):
    tok_count, listed = routes_l.shape
    block = acts_l.shape[1] // listed
    width = dec_local.shape[1]
    held = dec_local.shape[0] // block
    slots_per = (tok_count * listed + peers - 1) // peers
    total_slots = peers * slots_per
    owner = routes_l // held
    within = routes_l - owner * held
    owners = jnp.arange(peers, dtype=jnp.int32)
    hits = (owner[:, :, None] == owners[None, None, :]).astype(jnp.int32)
    per_row = jnp.sum(hits, axis=1)
    earlier = jnp.cumsum(per_row, axis=0) - per_row
    place = jnp.sum(hits * earlier[:, None, :], axis=2)
    slot_of = (owner * slots_per + place).reshape(-1)
    slot_ids = jnp.arange(total_slots, dtype=jnp.int32)
    pick = (slot_ids[:, None] == slot_of[None, :]).astype(jnp.bfloat16)
    row_pick = jnp.sum(
        pick.reshape(total_slots, tok_count, listed).astype(jnp.float32), axis=2
    ).astype(jnp.bfloat16)
    send_g = jnp.dot(row_pick, g_rows, preferred_element_type=jnp.float32).astype(jnp.bfloat16)
    block_act = jnp.dot(
        pick, acts_l.reshape(tok_count * listed, block), preferred_element_type=jnp.float32
    ).astype(jnp.bfloat16)
    within_hot = (within.reshape(-1)[:, None] == jnp.arange(held, dtype=jnp.int32)[None, :]).astype(
        jnp.bfloat16
    )
    slot_within = jnp.dot(pick, within_hot, preferred_element_type=jnp.float32).astype(jnp.bfloat16)
    send_act = (slot_within[:, :, None] * block_act[:, None, :]).reshape(total_slots, held * block)
    send_g = send_g.reshape(peers, slots_per, width)
    send_act = send_act.reshape(peers, slots_per, held * block)
    recv_g, recv_act = (
        lax.all_to_all(send_g, "dict", split_axis=0, concat_axis=0, tiled=True),
        lax.all_to_all(send_act, "dict", split_axis=0, concat_axis=0, tiled=True),
    )
    coef_here, contrib_here = owner_work(recv_g, recv_act, dec_local, enc_local)
    coef_back, contrib_back = (
        lax.all_to_all(coef_here, "dict", split_axis=0, concat_axis=0, tiled=True),
        lax.all_to_all(contrib_here, "dict", split_axis=0, concat_axis=0, tiled=True),
    )
    coef_back = coef_back.reshape(total_slots, held, block)
    contrib_back = contrib_back.reshape(total_slots, width)
    coef_chosen = jnp.sum(
        slot_within.astype(jnp.float32)[:, :, None] * coef_back.astype(jnp.float32), axis=1
    ).astype(jnp.bfloat16)
    coef_rows = lax.dot_general(
        pick, coef_chosen, (((0,), (0,)), ((), ())), preferred_element_type=jnp.float32
    )
    attr = (acts_l.reshape(tok_count * listed, block).astype(jnp.float32) * coef_rows).reshape(
        tok_count, listed * block
    )
    summed = lax.dot_general(
        row_pick, contrib_back, (((0,), (0,)), ((), ())), preferred_element_type=jnp.float32
    )
    new_g = (g_rows.astype(jnp.float32) + scale_l[:, None] * gain_l[None, :] * summed).astype(
        jnp.bfloat16
    )
    return (attr, new_g)


def slot_device(cotangent, routes, acts, decoder, encoder, gain, inv_rms):
    peers = lax.axis_size("dict")
    depth = lax.axis_size("section")
    here = lax.axis_index("section")
    routes_l = routes[0]
    acts_l = acts[0]
    dec_local = decoder[0]
    enc_local = encoder[0]
    gain_l = gain[0]
    scale_l = inv_rms[0]
    tok_count, listed = routes_l.shape
    attr_keep = jnp.zeros((tok_count, acts_l.shape[1]), jnp.float32)
    grad_keep = jnp.zeros(cotangent.shape, jnp.bfloat16)
    g_new = cotangent
    for turn in range(depth):
        if turn > 0:
            g_now = passed_along(g_new, "section", -1)
        else:
            g_now = cotangent
        active = here == depth - 1 - turn
        attr, g_new = layer_pass(
            g_now, routes_l, acts_l, dec_local, enc_local, gain_l, scale_l, peers
        )
        attr_keep = jnp.where(active, attr, attr_keep)
        grad_keep = jnp.where(active, g_new, grad_keep)
    return (attr_keep[None], grad_keep[None])


def swap_cores(block):
    return lax.ppermute(block, "section", [(0, 1), (1, 0)])


def exchange(parts, sign):
    peers = parts.shape[0]
    moved = [parts[0]]
    for shift in range(1, peers):
        route = [(d, (d + sign * shift) % peers) for d in range(peers)]
        moved.append(lax.ppermute(parts[shift], "dict", route))
    return jnp.stack(moved, axis=0)


def split_layer(g_half, routes_l, acts_l, own, other, is_own, gain_half, scale_l):
    peers = lax.axis_size("dict")
    me = lax.axis_index("dict")
    rows, listed = routes_l.shape
    block = acts_l.shape[1] // listed
    held = own[0].shape[0] // block
    half = g_half.shape[1]
    owner = routes_l // held
    within = routes_l - owner * held
    rel = (owner - me) % peers
    shifts = jnp.arange(peers, dtype=jnp.int32)
    spots = jnp.arange(held, dtype=jnp.int32)
    at_rel = (rel[:, :, None] == shifts[None, None, :]).astype(jnp.bfloat16)
    at_spot = (within[:, :, None] == spots[None, None, :]).astype(jnp.bfloat16)
    act_grid = acts_l.reshape(rows, listed, block)
    placed = jnp.einsum(
        "rks,rkw,rkj->srwj", at_rel, at_spot, act_grid, preferred_element_type=jnp.float32
    ).astype(jnp.bfloat16).reshape(peers, rows, held * block)
    sent = jnp.concatenate(
        [jnp.broadcast_to(g_half[None], (peers, rows, half)), placed], axis=-1
    )
    got = exchange(sent, 1).reshape(peers * rows, half + held * block)
    g_all = got[:, :half]
    act_all = got[:, half:]

    def with_dec(dec):
        return lax.dot_general(
            g_all, dec, (((1,), (1,)), ((), ())), preferred_element_type=jnp.float32
        )

    part = jnp.where(is_own, with_dec(own[0]), with_dec(other[0]))
    paired = swap_cores(jnp.concatenate([part, act_all.astype(jnp.float32)], axis=1))
    coef = (part + paired[:, :held * block]).astype(jnp.bfloat16)
    act_used = jnp.where(is_own, act_all.astype(jnp.float32), paired[:, held * block:])
    dz = jnp.where(act_used > 0, coef, jnp.zeros_like(coef))

    def with_enc(enc):
        return jnp.dot(dz, enc, preferred_element_type=jnp.float32)

    contrib = jnp.where(is_own, with_enc(own[1]), with_enc(other[1])).astype(jnp.bfloat16)
    dz_pick = dz[:, :block]
    for spot in range(1, held):
        dz_pick = dz_pick + dz[:, spot * block:(spot + 1) * block]
    back = jnp.concatenate([contrib, dz_pick], axis=-1).reshape(peers, rows, half + block)
    returned = exchange(back, -1)
    total = jnp.sum(returned[:, :, :half].astype(jnp.float32), axis=0)
    dz_back = returned[:, :, half:]
    dz_slot = jnp.einsum("rks,srj->rkj", at_rel, dz_back, preferred_element_type=jnp.float32)
    attr = (act_grid.astype(jnp.float32) * dz_slot).reshape(rows, listed * block)
    new_half = (g_half.astype(jnp.float32) + scale_l[:, None] * gain_half[None, :] * total).astype(
        jnp.bfloat16
    )
    return attr, new_half


def split_device(cotangent, routes, acts, decoder, encoder, gain, inv_rms):
    depth = lax.axis_size("section")
    here = lax.axis_index("section")
    rows, width = cotangent.shape
    blocks = decoder.shape[1]
    half = width // depth
    mine = here * half
    theirs = (1 - here) * half
    small = jnp.concatenate([gain[0], inv_rms[0]], axis=0)
    other_small = swap_cores(small)
    sent_w = jnp.concatenate(
        [
            lax.dynamic_slice_in_dim(decoder[0], theirs, half, axis=1),
            lax.dynamic_slice_in_dim(encoder[0], theirs, half, axis=1),
        ],
        axis=0,
    )
    own = (
        lax.dynamic_slice_in_dim(decoder[0], mine, half, axis=1),
        lax.dynamic_slice_in_dim(encoder[0], mine, half, axis=1),
    )
    attr_keep = jnp.zeros((rows, acts.shape[2]), jnp.float32)
    grad_keep = jnp.zeros(cotangent.shape, jnp.bfloat16)
    g_half = lax.dynamic_slice_in_dim(cotangent, mine, half, axis=1)
    g_half, own, sent_w = lax.optimization_barrier((g_half, own, sent_w))
    other_w = swap_cores(sent_w)
    other = (other_w[:blocks], other_w[blocks:])
    for layer in reversed(range(depth)):
        is_own = here == layer
        s = jnp.where(is_own, small, other_small)
        gain_half = lax.dynamic_slice_in_dim(s[:width], mine, half, axis=0)
        scale_l = s[width:width + rows]
        attr, g_half = split_layer(g_half, routes[0], acts[0], own, other, is_own, gain_half, scale_l)
        partner = swap_cores(g_half)
        full = jnp.where(
            here == 0,
            jnp.concatenate([g_half, partner], axis=1),
            jnp.concatenate([partner, g_half], axis=1),
        )
        attr_keep = jnp.where(is_own, attr, attr_keep)
        grad_keep = jnp.where(is_own, full, grad_keep)
    return (attr_keep[None], grad_keep[None])


def per_device(cotangent, routes, acts, decoder, encoder, gain, inv_rms):
    peers = lax.axis_size("dict")
    depth = lax.axis_size("section")
    listed = routes.shape[-1]
    width = cotangent.shape[1]
    if listed == peers and depth == 2 and width % (depth * 128) == 0:
        return split_device(cotangent, routes, acts, decoder, encoder, gain, inv_rms)
    return slot_device(cotangent, routes, acts, decoder, encoder, gain, inv_rms)


def solution(mesh):
    placed = (
        P(("groups", "dict"), None),
        P("section", ("groups", "dict"), None),
        P("section", ("groups", "dict"), None),
        P("section", "dict", None),
        P("section", "dict", None),
        P("section", None),
        P("section", ("groups", "dict")),
    )
    return jax.shard_map(
        per_device,
        mesh=mesh,
        in_specs=placed,
        out_specs=(P("section", ("groups", "dict"), None), P("section", ("groups", "dict"), None)),
        check_vma=False,
    )
```

```python
import jax
import jax.numpy as jnp
from jax import lax
from jax.sharding import PartitionSpec as P


def passed_along(block, axis, distance):
    devices = range(lax.axis_size(axis))
    route = [(i - distance, i) for i in devices if i - distance in devices]
    return lax.ppermute(block, axis, route)


def owner_work(recv_g, recv_act, dec_local, enc_local):
    width = recv_g.shape[-1]
    columns = dec_local.shape[0]
    flat_g = recv_g.reshape(-1, width)
    flat_act = recv_act.reshape(-1, columns)
    coef = lax.dot_general(
        flat_g, dec_local, (((1,), (1,)), ((), ())), preferred_element_type=jnp.float32
    ).astype(jnp.bfloat16)
    masked = jnp.where(flat_act > 0, coef, jnp.zeros_like(coef))
    contrib = jnp.dot(masked, enc_local, preferred_element_type=jnp.float32).astype(jnp.bfloat16)
    lead = recv_g.shape[:-1]
    return (coef.reshape(lead + (columns,)), contrib.reshape(lead + (width,)))


def layer_pass(g_rows, routes_l, acts_l, dec_local, enc_local, gain_l, scale_l, peers):
    tok_count, listed = routes_l.shape
    block = acts_l.shape[1] // listed
    width = dec_local.shape[1]
    held = dec_local.shape[0] // block
    slots_per = (tok_count * listed + peers - 1) // peers
    total_slots = peers * slots_per
    owner = routes_l // held
    within = routes_l - owner * held
    owners = jnp.arange(peers, dtype=jnp.int32)
    hits = (owner[:, :, None] == owners[None, None, :]).astype(jnp.int32)
    per_row = jnp.sum(hits, axis=1)
    earlier = jnp.cumsum(per_row, axis=0) - per_row
    place = jnp.sum(hits * earlier[:, None, :], axis=2)
    slot_of = (owner * slots_per + place).reshape(-1)
    slot_ids = jnp.arange(total_slots, dtype=jnp.int32)
    pick = (slot_ids[:, None] == slot_of[None, :]).astype(jnp.bfloat16)
    row_pick = jnp.sum(
        pick.reshape(total_slots, tok_count, listed).astype(jnp.float32), axis=2
    ).astype(jnp.bfloat16)
    send_g = jnp.dot(row_pick, g_rows, preferred_element_type=jnp.float32).astype(jnp.bfloat16)
    block_act = jnp.dot(
        pick, acts_l.reshape(tok_count * listed, block), preferred_element_type=jnp.float32
    ).astype(jnp.bfloat16)
    within_hot = (within.reshape(-1)[:, None] == jnp.arange(held, dtype=jnp.int32)[None, :]).astype(
        jnp.bfloat16
    )
    slot_within = jnp.dot(pick, within_hot, preferred_element_type=jnp.float32).astype(jnp.bfloat16)
    send_act = (slot_within[:, :, None] * block_act[:, None, :]).reshape(total_slots, held * block)
    send_g = send_g.reshape(peers, slots_per, width)
    send_act = send_act.reshape(peers, slots_per, held * block)
    recv_g, recv_act = (
        lax.all_to_all(send_g, "dict", split_axis=0, concat_axis=0, tiled=True),
        lax.all_to_all(send_act, "dict", split_axis=0, concat_axis=0, tiled=True),
    )
    coef_here, contrib_here = owner_work(recv_g, recv_act, dec_local, enc_local)
    coef_back, contrib_back = (
        lax.all_to_all(coef_here, "dict", split_axis=0, concat_axis=0, tiled=True),
        lax.all_to_all(contrib_here, "dict", split_axis=0, concat_axis=0, tiled=True),
    )
    coef_back = coef_back.reshape(total_slots, held, block)
    contrib_back = contrib_back.reshape(total_slots, width)
    coef_chosen = jnp.sum(
        slot_within.astype(jnp.float32)[:, :, None] * coef_back.astype(jnp.float32), axis=1
    ).astype(jnp.bfloat16)
    coef_rows = lax.dot_general(
        pick, coef_chosen, (((0,), (0,)), ((), ())), preferred_element_type=jnp.float32
    )
    attr = (acts_l.reshape(tok_count * listed, block).astype(jnp.float32) * coef_rows).reshape(
        tok_count, listed * block
    )
    summed = lax.dot_general(
        row_pick, contrib_back, (((0,), (0,)), ((), ())), preferred_element_type=jnp.float32
    )
    new_g = (g_rows.astype(jnp.float32) + scale_l[:, None] * gain_l[None, :] * summed).astype(
        jnp.bfloat16
    )
    return (attr, new_g)


def slot_device(cotangent, routes, acts, decoder, encoder, gain, inv_rms):
    peers = lax.axis_size("dict")
    depth = lax.axis_size("section")
    here = lax.axis_index("section")
    routes_l = routes[0]
    acts_l = acts[0]
    dec_local = decoder[0]
    enc_local = encoder[0]
    gain_l = gain[0]
    scale_l = inv_rms[0]
    tok_count, listed = routes_l.shape
    attr_keep = jnp.zeros((tok_count, acts_l.shape[1]), jnp.float32)
    grad_keep = jnp.zeros(cotangent.shape, jnp.bfloat16)
    g_new = cotangent
    for turn in range(depth):
        if turn > 0:
            g_now = passed_along(g_new, "section", -1)
        else:
            g_now = cotangent
        active = here == depth - 1 - turn
        attr, g_new = layer_pass(
            g_now, routes_l, acts_l, dec_local, enc_local, gain_l, scale_l, peers
        )
        attr_keep = jnp.where(active, attr, attr_keep)
        grad_keep = jnp.where(active, g_new, grad_keep)
    return (attr_keep[None], grad_keep[None])


def swap_cores(block):
    return lax.ppermute(block, "section", [(0, 1), (1, 0)])


def exchange(parts, sign):
    peers = parts.shape[0]
    moved = [parts[0]]
    for shift in range(1, peers):
        route = [(d, (d + sign * shift) % peers) for d in range(peers)]
        moved.append(lax.ppermute(parts[shift], "dict", route))
    return jnp.stack(moved, axis=0)


def split_layer(g_half, routes_l, acts_l, own, other, is_own, gain_half, scale_l):
    peers = lax.axis_size("dict")
    me = lax.axis_index("dict")
    rows, listed = routes_l.shape
    block = acts_l.shape[1] // listed
    held = own[0].shape[0] // block
    half = g_half.shape[1]
    owner = routes_l // held
    within = routes_l - owner * held
    rel = (owner - me) % peers
    shifts = jnp.arange(peers, dtype=jnp.int32)
    at_rel = (rel[:, :, None] == shifts[None, None, :]).astype(jnp.bfloat16)
    act_grid = acts_l.reshape(rows, listed, block)
    live = (act_grid > 0).astype(jnp.bfloat16) * (1 + within).astype(jnp.bfloat16)[:, :, None]
    placed = jnp.einsum(
        "rks,rkj->srj", at_rel, live, preferred_element_type=jnp.float32
    ).astype(jnp.bfloat16)
    sent = jnp.concatenate(
        [jnp.broadcast_to(g_half[None], (peers, rows, half)), placed], axis=-1
    )
    got = exchange(sent, 1).reshape(peers * rows, half + block)
    g_all = got[:, :half]
    code_all = got[:, half:]

    def with_dec(dec):
        return lax.dot_general(
            g_all, dec, (((1,), (1,)), ((), ())), preferred_element_type=jnp.float32
        )

    part = jnp.where(is_own, with_dec(own[0]), with_dec(other[0]))
    paired = swap_cores(jnp.concatenate([part, code_all.astype(jnp.float32)], axis=1))
    coef = (part + paired[:, :held * block]).astype(jnp.bfloat16)
    code = jnp.where(is_own, code_all.astype(jnp.float32), paired[:, held * block:])
    marks = jnp.concatenate([code == spot + 1 for spot in range(held)], axis=1)
    dz = jnp.where(marks, coef, jnp.zeros_like(coef))

    def with_enc(enc):
        return jnp.dot(dz, enc, preferred_element_type=jnp.float32)

    contrib = jnp.where(is_own, with_enc(own[1]), with_enc(other[1])).astype(jnp.bfloat16)
    dz_pick = dz[:, :block]
    for spot in range(1, held):
        dz_pick = dz_pick + dz[:, spot * block:(spot + 1) * block]
    back = jnp.concatenate([contrib, dz_pick], axis=-1).reshape(peers, rows, half + block)
    returned = exchange(back, -1)
    total = jnp.sum(returned[:, :, :half].astype(jnp.float32), axis=0)
    dz_back = returned[:, :, half:]
    dz_slot = jnp.einsum("rks,srj->rkj", at_rel, dz_back, preferred_element_type=jnp.float32)
    attr = (act_grid.astype(jnp.float32) * dz_slot).reshape(rows, listed * block)
    new_half = (g_half.astype(jnp.float32) + scale_l[:, None] * gain_half[None, :] * total).astype(
        jnp.bfloat16
    )
    return attr, new_half


def split_device(cotangent, routes, acts, decoder, encoder, gain, inv_rms):
    depth = lax.axis_size("section")
    here = lax.axis_index("section")
    rows, width = cotangent.shape
    blocks = decoder.shape[1]
    half = width // depth
    mine = here * half
    theirs = (1 - here) * half
    small = jnp.concatenate([gain[0], inv_rms[0]], axis=0)
    other_small = swap_cores(small)
    sent_w = jnp.concatenate(
        [
            lax.dynamic_slice_in_dim(decoder[0], theirs, half, axis=1),
            lax.dynamic_slice_in_dim(encoder[0], theirs, half, axis=1),
        ],
        axis=0,
    )
    other_w = swap_cores(sent_w)
    other = (other_w[:blocks], other_w[blocks:])
    own = (
        lax.dynamic_slice_in_dim(decoder[0], mine, half, axis=1),
        lax.dynamic_slice_in_dim(encoder[0], mine, half, axis=1),
    )
    attr_keep = jnp.zeros((rows, acts.shape[2]), jnp.float32)
    grad_keep = jnp.zeros(cotangent.shape, jnp.bfloat16)
    g_half = lax.dynamic_slice_in_dim(cotangent, mine, half, axis=1)
    for layer in reversed(range(depth)):
        is_own = here == layer
        s = jnp.where(is_own, small, other_small)
        gain_half = lax.dynamic_slice_in_dim(s[:width], mine, half, axis=0)
        scale_l = s[width:width + rows]
        attr, g_half = split_layer(g_half, routes[0], acts[0], own, other, is_own, gain_half, scale_l)
        partner = swap_cores(g_half)
        full = jnp.where(
            here == 0,
            jnp.concatenate([g_half, partner], axis=1),
            jnp.concatenate([partner, g_half], axis=1),
        )
        attr_keep = jnp.where(is_own, attr, attr_keep)
        grad_keep = jnp.where(is_own, full, grad_keep)
    return (attr_keep[None], grad_keep[None])


def per_device(cotangent, routes, acts, decoder, encoder, gain, inv_rms):
    peers = lax.axis_size("dict")
    depth = lax.axis_size("section")
    listed = routes.shape[-1]
    width = cotangent.shape[1]
    if listed == peers and depth == 2 and width % (depth * 128) == 0:
        return split_device(cotangent, routes, acts, decoder, encoder, gain, inv_rms)
    return slot_device(cotangent, routes, acts, decoder, encoder, gain, inv_rms)


def solution(mesh):
    placed = (
        P(("groups", "dict"), None),
        P("section", ("groups", "dict"), None),
        P("section", ("groups", "dict"), None),
        P("section", "dict", None),
        P("section", "dict", None),
        P("section", None),
        P("section", ("groups", "dict")),
    )
    return jax.shard_map(
        per_device,
        mesh=mesh,
        in_specs=placed,
        out_specs=(P("section", ("groups", "dict"), None), P("section", ("groups", "dict"), None)),
        check_vma=False,
    )
```

```python
import jax
import jax.numpy as jnp
from jax import lax
from jax.sharding import PartitionSpec as P


def passed_along(block, axis, distance):
    devices = range(lax.axis_size(axis))
    route = [(i - distance, i) for i in devices if i - distance in devices]
    return lax.ppermute(block, axis, route)


def owner_work(recv_g, recv_act, dec_local, enc_local):
    width = recv_g.shape[-1]
    columns = dec_local.shape[0]
    flat_g = recv_g.reshape(-1, width)
    flat_act = recv_act.reshape(-1, columns)
    coef = lax.dot_general(
        flat_g, dec_local, (((1,), (1,)), ((), ())), preferred_element_type=jnp.float32
    ).astype(jnp.bfloat16)
    masked = jnp.where(flat_act > 0, coef, jnp.zeros_like(coef))
    contrib = jnp.dot(masked, enc_local, preferred_element_type=jnp.float32).astype(jnp.bfloat16)
    lead = recv_g.shape[:-1]
    return (coef.reshape(lead + (columns,)), contrib.reshape(lead + (width,)))


def layer_pass(g_rows, routes_l, acts_l, dec_local, enc_local, gain_l, scale_l, peers):
    tok_count, listed = routes_l.shape
    block = acts_l.shape[1] // listed
    width = dec_local.shape[1]
    held = dec_local.shape[0] // block
    slots_per = (tok_count * listed + peers - 1) // peers
    total_slots = peers * slots_per
    owner = routes_l // held
    within = routes_l - owner * held
    owners = jnp.arange(peers, dtype=jnp.int32)
    hits = (owner[:, :, None] == owners[None, None, :]).astype(jnp.int32)
    per_row = jnp.sum(hits, axis=1)
    earlier = jnp.cumsum(per_row, axis=0) - per_row
    place = jnp.sum(hits * earlier[:, None, :], axis=2)
    slot_of = (owner * slots_per + place).reshape(-1)
    slot_ids = jnp.arange(total_slots, dtype=jnp.int32)
    pick = (slot_ids[:, None] == slot_of[None, :]).astype(jnp.bfloat16)
    row_pick = jnp.sum(
        pick.reshape(total_slots, tok_count, listed).astype(jnp.float32), axis=2
    ).astype(jnp.bfloat16)
    send_g = jnp.dot(row_pick, g_rows, preferred_element_type=jnp.float32).astype(jnp.bfloat16)
    block_act = jnp.dot(
        pick, acts_l.reshape(tok_count * listed, block), preferred_element_type=jnp.float32
    ).astype(jnp.bfloat16)
    within_hot = (within.reshape(-1)[:, None] == jnp.arange(held, dtype=jnp.int32)[None, :]).astype(
        jnp.bfloat16
    )
    slot_within = jnp.dot(pick, within_hot, preferred_element_type=jnp.float32).astype(jnp.bfloat16)
    send_act = (slot_within[:, :, None] * block_act[:, None, :]).reshape(total_slots, held * block)
    send_g = send_g.reshape(peers, slots_per, width)
    send_act = send_act.reshape(peers, slots_per, held * block)
    recv_g, recv_act = (
        lax.all_to_all(send_g, "dict", split_axis=0, concat_axis=0, tiled=True),
        lax.all_to_all(send_act, "dict", split_axis=0, concat_axis=0, tiled=True),
    )
    coef_here, contrib_here = owner_work(recv_g, recv_act, dec_local, enc_local)
    coef_back, contrib_back = (
        lax.all_to_all(coef_here, "dict", split_axis=0, concat_axis=0, tiled=True),
        lax.all_to_all(contrib_here, "dict", split_axis=0, concat_axis=0, tiled=True),
    )
    coef_back = coef_back.reshape(total_slots, held, block)
    contrib_back = contrib_back.reshape(total_slots, width)
    coef_chosen = jnp.sum(
        slot_within.astype(jnp.float32)[:, :, None] * coef_back.astype(jnp.float32), axis=1
    ).astype(jnp.bfloat16)
    coef_rows = lax.dot_general(
        pick, coef_chosen, (((0,), (0,)), ((), ())), preferred_element_type=jnp.float32
    )
    attr = (acts_l.reshape(tok_count * listed, block).astype(jnp.float32) * coef_rows).reshape(
        tok_count, listed * block
    )
    summed = lax.dot_general(
        row_pick, contrib_back, (((0,), (0,)), ((), ())), preferred_element_type=jnp.float32
    )
    new_g = (g_rows.astype(jnp.float32) + scale_l[:, None] * gain_l[None, :] * summed).astype(
        jnp.bfloat16
    )
    return (attr, new_g)


def slot_device(cotangent, routes, acts, decoder, encoder, gain, inv_rms):
    peers = lax.axis_size("dict")
    depth = lax.axis_size("section")
    here = lax.axis_index("section")
    routes_l = routes[0]
    acts_l = acts[0]
    dec_local = decoder[0]
    enc_local = encoder[0]
    gain_l = gain[0]
    scale_l = inv_rms[0]
    tok_count, listed = routes_l.shape
    attr_keep = jnp.zeros((tok_count, acts_l.shape[1]), jnp.float32)
    grad_keep = jnp.zeros(cotangent.shape, jnp.bfloat16)
    g_new = cotangent
    for turn in range(depth):
        if turn > 0:
            g_now = passed_along(g_new, "section", -1)
        else:
            g_now = cotangent
        active = here == depth - 1 - turn
        attr, g_new = layer_pass(
            g_now, routes_l, acts_l, dec_local, enc_local, gain_l, scale_l, peers
        )
        attr_keep = jnp.where(active, attr, attr_keep)
        grad_keep = jnp.where(active, g_new, grad_keep)
    return (attr_keep[None], grad_keep[None])


def swap_cores(block):
    return lax.ppermute(block, "section", [(0, 1), (1, 0)])


def exchange(parts, sign, gate=None):
    peers = parts.shape[0]
    moved = [parts[0]]
    for shift in range(1, peers):
        piece = parts[shift]
        if gate is not None and shift >= peers // 2 + 1:
            piece, gate = lax.optimization_barrier((piece, gate))
        route = [(d, (d + sign * shift) % peers) for d in range(peers)]
        moved.append(lax.ppermute(piece, "dict", route))
    return jnp.stack(moved, axis=0), gate


def split_layer(g_half, routes_l, acts_l, own, other, is_own, gain_half, scale_l):
    peers = lax.axis_size("dict")
    me = lax.axis_index("dict")
    rows, listed = routes_l.shape
    block = acts_l.shape[1] // listed
    held = own[0].shape[0] // block
    half = g_half.shape[1]
    owner = routes_l // held
    within = routes_l - owner * held
    rel = (owner - me) % peers
    shifts = jnp.arange(peers, dtype=jnp.int32)
    at_rel = (rel[:, :, None] == shifts[None, None, :]).astype(jnp.bfloat16)
    act_grid = acts_l.reshape(rows, listed, block)
    live = (act_grid > 0).astype(jnp.bfloat16) * (1 + within).astype(jnp.bfloat16)[:, :, None]
    placed = jnp.einsum(
        "rks,rkj->srj", at_rel, live, preferred_element_type=jnp.float32
    ).astype(jnp.bfloat16)
    sent = jnp.concatenate(
        [jnp.broadcast_to(g_half[None], (peers, rows, half)), placed], axis=-1
    )
    got, other = exchange(sent, 1, other)
    got = got.reshape(peers * rows, half + block)
    g_all = got[:, :half]
    code_all = got[:, half:]

    def with_dec(dec):
        return lax.dot_general(
            g_all, dec, (((1,), (1,)), ((), ())), preferred_element_type=jnp.float32
        )

    part = jnp.where(is_own, with_dec(own[0]), with_dec(other[0]))
    paired = swap_cores(jnp.concatenate([part, code_all.astype(jnp.float32)], axis=1))
    coef = (part + paired[:, :held * block]).astype(jnp.bfloat16)
    code = jnp.where(is_own, code_all.astype(jnp.float32), paired[:, held * block:])
    marks = jnp.concatenate([code == spot + 1 for spot in range(held)], axis=1)
    dz = jnp.where(marks, coef, jnp.zeros_like(coef))

    def with_enc(enc):
        return jnp.dot(dz, enc, preferred_element_type=jnp.float32)

    contrib = jnp.where(is_own, with_enc(own[1]), with_enc(other[1])).astype(jnp.bfloat16)
    dz_pick = dz[:, :block]
    for spot in range(1, held):
        dz_pick = dz_pick + dz[:, spot * block:(spot + 1) * block]
    back = jnp.concatenate([contrib, dz_pick], axis=-1).reshape(peers, rows, half + block)
    returned, _ = exchange(back, -1)
    total = jnp.sum(returned[:, :, :half].astype(jnp.float32), axis=0)
    dz_back = returned[:, :, half:]
    dz_slot = jnp.einsum("rks,srj->rkj", at_rel, dz_back, preferred_element_type=jnp.float32)
    attr = (act_grid.astype(jnp.float32) * dz_slot).reshape(rows, listed * block)
    new_half = (g_half.astype(jnp.float32) + scale_l[:, None] * gain_half[None, :] * total).astype(
        jnp.bfloat16
    )
    return attr, new_half


def split_device(cotangent, routes, acts, decoder, encoder, gain, inv_rms):
    depth = lax.axis_size("section")
    here = lax.axis_index("section")
    rows, width = cotangent.shape
    blocks = decoder.shape[1]
    half = width // depth
    mine = here * half
    theirs = (1 - here) * half
    small = jnp.concatenate([gain[0], inv_rms[0]], axis=0)
    other_small = swap_cores(small)
    sent_w = jnp.concatenate(
        [
            lax.dynamic_slice_in_dim(decoder[0], theirs, half, axis=1),
            lax.dynamic_slice_in_dim(encoder[0], theirs, half, axis=1),
        ],
        axis=0,
    )
    other_w = swap_cores(sent_w)
    other = (other_w[:blocks], other_w[blocks:])
    own = (
        lax.dynamic_slice_in_dim(decoder[0], mine, half, axis=1),
        lax.dynamic_slice_in_dim(encoder[0], mine, half, axis=1),
    )
    attr_keep = jnp.zeros((rows, acts.shape[2]), jnp.float32)
    grad_keep = jnp.zeros(cotangent.shape, jnp.bfloat16)
    g_half = lax.dynamic_slice_in_dim(cotangent, mine, half, axis=1)
    for layer in reversed(range(depth)):
        is_own = here == layer
        s = jnp.where(is_own, small, other_small)
        gain_half = lax.dynamic_slice_in_dim(s[:width], mine, half, axis=0)
        scale_l = s[width:width + rows]
        attr, g_half = split_layer(g_half, routes[0], acts[0], own, other, is_own, gain_half, scale_l)
        partner = swap_cores(g_half)
        full = jnp.where(
            here == 0,
            jnp.concatenate([g_half, partner], axis=1),
            jnp.concatenate([partner, g_half], axis=1),
        )
        attr_keep = jnp.where(is_own, attr, attr_keep)
        grad_keep = jnp.where(is_own, full, grad_keep)
    return (attr_keep[None], grad_keep[None])


def per_device(cotangent, routes, acts, decoder, encoder, gain, inv_rms):
    peers = lax.axis_size("dict")
    depth = lax.axis_size("section")
    listed = routes.shape[-1]
    width = cotangent.shape[1]
    if listed == peers and depth == 2 and width % (depth * 128) == 0:
        return split_device(cotangent, routes, acts, decoder, encoder, gain, inv_rms)
    return slot_device(cotangent, routes, acts, decoder, encoder, gain, inv_rms)


def solution(mesh):
    placed = (
        P(("groups", "dict"), None),
        P("section", ("groups", "dict"), None),
        P("section", ("groups", "dict"), None),
        P("section", "dict", None),
        P("section", "dict", None),
        P("section", None),
        P("section", ("groups", "dict")),
    )
    return jax.shard_map(
        per_device,
        mesh=mesh,
        in_specs=placed,
        out_specs=(P("section", ("groups", "dict"), None), P("section", ("groups", "dict"), None)),
        check_vma=False,
    )
```

```python
import jax
import jax.numpy as jnp
from jax import lax
from jax.sharding import PartitionSpec as P


def passed_along(block, axis, distance):
    devices = range(lax.axis_size(axis))
    route = [(i - distance, i) for i in devices if i - distance in devices]
    return lax.ppermute(block, axis, route)


def owner_work(recv_g, recv_act, dec_local, enc_local):
    width = recv_g.shape[-1]
    columns = dec_local.shape[0]
    flat_g = recv_g.reshape(-1, width)
    flat_act = recv_act.reshape(-1, columns)
    coef = lax.dot_general(
        flat_g, dec_local, (((1,), (1,)), ((), ())), preferred_element_type=jnp.float32
    ).astype(jnp.bfloat16)
    masked = jnp.where(flat_act > 0, coef, jnp.zeros_like(coef))
    contrib = jnp.dot(masked, enc_local, preferred_element_type=jnp.float32).astype(jnp.bfloat16)
    lead = recv_g.shape[:-1]
    return (coef.reshape(lead + (columns,)), contrib.reshape(lead + (width,)))


def layer_pass(g_rows, routes_l, acts_l, dec_local, enc_local, gain_l, scale_l, peers):
    tok_count, listed = routes_l.shape
    block = acts_l.shape[1] // listed
    width = dec_local.shape[1]
    held = dec_local.shape[0] // block
    slots_per = (tok_count * listed + peers - 1) // peers
    total_slots = peers * slots_per
    owner = routes_l // held
    within = routes_l - owner * held
    owners = jnp.arange(peers, dtype=jnp.int32)
    hits = (owner[:, :, None] == owners[None, None, :]).astype(jnp.int32)
    per_row = jnp.sum(hits, axis=1)
    earlier = jnp.cumsum(per_row, axis=0) - per_row
    place = jnp.sum(hits * earlier[:, None, :], axis=2)
    slot_of = (owner * slots_per + place).reshape(-1)
    slot_ids = jnp.arange(total_slots, dtype=jnp.int32)
    pick = (slot_ids[:, None] == slot_of[None, :]).astype(jnp.bfloat16)
    row_pick = jnp.sum(
        pick.reshape(total_slots, tok_count, listed).astype(jnp.float32), axis=2
    ).astype(jnp.bfloat16)
    send_g = jnp.dot(row_pick, g_rows, preferred_element_type=jnp.float32).astype(jnp.bfloat16)
    block_act = jnp.dot(
        pick, acts_l.reshape(tok_count * listed, block), preferred_element_type=jnp.float32
    ).astype(jnp.bfloat16)
    within_hot = (within.reshape(-1)[:, None] == jnp.arange(held, dtype=jnp.int32)[None, :]).astype(
        jnp.bfloat16
    )
    slot_within = jnp.dot(pick, within_hot, preferred_element_type=jnp.float32).astype(jnp.bfloat16)
    send_act = (slot_within[:, :, None] * block_act[:, None, :]).reshape(total_slots, held * block)
    send_g = send_g.reshape(peers, slots_per, width)
    send_act = send_act.reshape(peers, slots_per, held * block)
    recv_g, recv_act = (
        lax.all_to_all(send_g, "dict", split_axis=0, concat_axis=0, tiled=True),
        lax.all_to_all(send_act, "dict", split_axis=0, concat_axis=0, tiled=True),
    )
    coef_here, contrib_here = owner_work(recv_g, recv_act, dec_local, enc_local)
    coef_back, contrib_back = (
        lax.all_to_all(coef_here, "dict", split_axis=0, concat_axis=0, tiled=True),
        lax.all_to_all(contrib_here, "dict", split_axis=0, concat_axis=0, tiled=True),
    )
    coef_back = coef_back.reshape(total_slots, held, block)
    contrib_back = contrib_back.reshape(total_slots, width)
    coef_chosen = jnp.sum(
        slot_within.astype(jnp.float32)[:, :, None] * coef_back.astype(jnp.float32), axis=1
    ).astype(jnp.bfloat16)
    coef_rows = lax.dot_general(
        pick, coef_chosen, (((0,), (0,)), ((), ())), preferred_element_type=jnp.float32
    )
    attr = (acts_l.reshape(tok_count * listed, block).astype(jnp.float32) * coef_rows).reshape(
        tok_count, listed * block
    )
    summed = lax.dot_general(
        row_pick, contrib_back, (((0,), (0,)), ((), ())), preferred_element_type=jnp.float32
    )
    new_g = (g_rows.astype(jnp.float32) + scale_l[:, None] * gain_l[None, :] * summed).astype(
        jnp.bfloat16
    )
    return (attr, new_g)


def slot_device(cotangent, routes, acts, decoder, encoder, gain, inv_rms):
    peers = lax.axis_size("dict")
    depth = lax.axis_size("section")
    here = lax.axis_index("section")
    routes_l = routes[0]
    acts_l = acts[0]
    dec_local = decoder[0]
    enc_local = encoder[0]
    gain_l = gain[0]
    scale_l = inv_rms[0]
    tok_count, listed = routes_l.shape
    attr_keep = jnp.zeros((tok_count, acts_l.shape[1]), jnp.float32)
    grad_keep = jnp.zeros(cotangent.shape, jnp.bfloat16)
    g_new = cotangent
    for turn in range(depth):
        if turn > 0:
            g_now = passed_along(g_new, "section", -1)
        else:
            g_now = cotangent
        active = here == depth - 1 - turn
        attr, g_new = layer_pass(
            g_now, routes_l, acts_l, dec_local, enc_local, gain_l, scale_l, peers
        )
        attr_keep = jnp.where(active, attr, attr_keep)
        grad_keep = jnp.where(active, g_new, grad_keep)
    return (attr_keep[None], grad_keep[None])


def swap_cores(block):
    return lax.ppermute(block, "section", [(0, 1), (1, 0)])


def exchange(parts, sign):
    peers = parts.shape[0]
    moved = [parts[0]]
    for shift in range(1, peers):
        route = [(d, (d + sign * shift) % peers) for d in range(peers)]
        moved.append(lax.ppermute(parts[shift], "dict", route))
    return jnp.stack(moved, axis=0)


def split_layer(g_half, routes_l, acts_l, own, other, is_own, gain_half, scale_l):
    peers = lax.axis_size("dict")
    me = lax.axis_index("dict")
    rows, listed = routes_l.shape
    block = acts_l.shape[1] // listed
    held = own[0].shape[0] // block
    half = g_half.shape[1]
    owner = routes_l // held
    within = routes_l - owner * held
    rel = (owner - me) % peers
    shifts = jnp.arange(peers, dtype=jnp.int32)
    at_rel = (rel[:, :, None] == shifts[None, None, :]).astype(jnp.bfloat16)
    act_grid = acts_l.reshape(rows, listed, block)
    live = (act_grid > 0).astype(jnp.bfloat16) * (1 + within).astype(jnp.bfloat16)[:, :, None]
    placed = jnp.einsum(
        "rks,rkj->srj", at_rel, live, preferred_element_type=jnp.float32
    ).astype(jnp.bfloat16)
    sent = jnp.concatenate(
        [jnp.broadcast_to(g_half[None], (peers, rows, half)), placed], axis=-1
    )
    got = exchange(sent, 1).reshape(peers * rows, half + block)
    g_all = got[:, :half]
    code_all = got[:, half:]

    def with_dec(dec):
        return lax.dot_general(
            g_all, dec, (((1,), (1,)), ((), ())), preferred_element_type=jnp.float32
        )

    part = jnp.where(is_own, with_dec(own[0]), with_dec(other[0]))
    paired = swap_cores(jnp.concatenate([part, code_all.astype(jnp.float32)], axis=1))
    coef = (part + paired[:, :held * block]).astype(jnp.bfloat16)
    code = jnp.where(is_own, code_all.astype(jnp.float32), paired[:, held * block:])
    marks = jnp.concatenate([code == spot + 1 for spot in range(held)], axis=1)
    dz = jnp.where(marks, coef, jnp.zeros_like(coef))

    def with_enc(enc):
        return jnp.dot(dz, enc, preferred_element_type=jnp.float32)

    contrib = jnp.where(is_own, with_enc(own[1]), with_enc(other[1])).astype(jnp.bfloat16)
    dz_pick = dz[:, :block]
    for spot in range(1, held):
        dz_pick = dz_pick + dz[:, spot * block:(spot + 1) * block]
    back = jnp.concatenate([contrib, dz_pick], axis=-1).reshape(peers, rows, half + block)
    returned = exchange(back, -1)
    total = jnp.sum(returned[:, :, :half].astype(jnp.float32), axis=0)
    dz_back = returned[:, :, half:]
    dz_slot = jnp.einsum("rks,srj->rkj", at_rel, dz_back, preferred_element_type=jnp.float32)
    attr = (act_grid.astype(jnp.float32) * dz_slot).reshape(rows, listed * block)
    new_half = (g_half.astype(jnp.float32) + scale_l[:, None] * gain_half[None, :] * total).astype(
        jnp.bfloat16
    )
    return attr, new_half


def split_device(cotangent, routes, acts, decoder, encoder, gain, inv_rms):
    depth = lax.axis_size("section")
    here = lax.axis_index("section")
    rows, width = cotangent.shape
    blocks = decoder.shape[1]
    half = width // depth
    mine = here * half
    theirs = (1 - here) * half
    small = jnp.concatenate([gain[0], inv_rms[0]], axis=0)
    other_small = swap_cores(small)
    other = (
        swap_cores(lax.dynamic_slice_in_dim(decoder[0], theirs, half, axis=1)),
        swap_cores(lax.dynamic_slice_in_dim(encoder[0], theirs, half, axis=1)),
    )
    own = (
        lax.dynamic_slice_in_dim(decoder[0], mine, half, axis=1),
        lax.dynamic_slice_in_dim(encoder[0], mine, half, axis=1),
    )
    attr_keep = jnp.zeros((rows, acts.shape[2]), jnp.float32)
    grad_keep = jnp.zeros(cotangent.shape, jnp.bfloat16)
    g_half = jnp.where(here == 0, cotangent[:, :half], cotangent[:, half:])
    for layer in reversed(range(depth)):
        is_own = here == layer
        s = jnp.where(is_own, small, other_small)
        gain_half = lax.dynamic_slice_in_dim(s[:width], mine, half, axis=0)
        scale_l = s[width:width + rows]
        attr, g_half = split_layer(g_half, routes[0], acts[0], own, other, is_own, gain_half, scale_l)
        partner = swap_cores(g_half)
        full = jnp.where(
            here == 0,
            jnp.concatenate([g_half, partner], axis=1),
            jnp.concatenate([partner, g_half], axis=1),
        )
        attr_keep = jnp.where(is_own, attr, attr_keep)
        grad_keep = jnp.where(is_own, full, grad_keep)
    return (attr_keep[None], grad_keep[None])


def per_device(cotangent, routes, acts, decoder, encoder, gain, inv_rms):
    peers = lax.axis_size("dict")
    depth = lax.axis_size("section")
    listed = routes.shape[-1]
    width = cotangent.shape[1]
    if listed == peers and depth == 2 and width % (depth * 128) == 0:
        return split_device(cotangent, routes, acts, decoder, encoder, gain, inv_rms)
    return slot_device(cotangent, routes, acts, decoder, encoder, gain, inv_rms)


def solution(mesh):
    placed = (
        P(("groups", "dict"), None),
        P("section", ("groups", "dict"), None),
        P("section", ("groups", "dict"), None),
        P("section", "dict", None),
        P("section", "dict", None),
        P("section", None),
        P("section", ("groups", "dict")),
    )
    return jax.shard_map(
        per_device,
        mesh=mesh,
        in_specs=placed,
        out_specs=(P("section", ("groups", "dict"), None), P("section", ("groups", "dict"), None)),
        check_vma=False,
    )
```

```python
import jax
import jax.numpy as jnp
from jax import lax
from jax.sharding import PartitionSpec as P


def passed_along(block, axis, distance):
    devices = range(lax.axis_size(axis))
    route = [(i - distance, i) for i in devices if i - distance in devices]
    return lax.ppermute(block, axis, route)


def owner_work(recv_g, recv_act, dec_local, enc_local):
    width = recv_g.shape[-1]
    columns = dec_local.shape[0]
    flat_g = recv_g.reshape(-1, width)
    flat_act = recv_act.reshape(-1, columns)
    coef = lax.dot_general(
        flat_g, dec_local, (((1,), (1,)), ((), ())), preferred_element_type=jnp.float32
    ).astype(jnp.bfloat16)
    masked = jnp.where(flat_act > 0, coef, jnp.zeros_like(coef))
    contrib = jnp.dot(masked, enc_local, preferred_element_type=jnp.float32).astype(jnp.bfloat16)
    lead = recv_g.shape[:-1]
    return (coef.reshape(lead + (columns,)), contrib.reshape(lead + (width,)))


def layer_pass(g_rows, routes_l, acts_l, dec_local, enc_local, gain_l, scale_l, peers):
    tok_count, listed = routes_l.shape
    block = acts_l.shape[1] // listed
    width = dec_local.shape[1]
    held = dec_local.shape[0] // block
    slots_per = (tok_count * listed + peers - 1) // peers
    total_slots = peers * slots_per
    owner = routes_l // held
    within = routes_l - owner * held
    owners = jnp.arange(peers, dtype=jnp.int32)
    hits = (owner[:, :, None] == owners[None, None, :]).astype(jnp.int32)
    per_row = jnp.sum(hits, axis=1)
    earlier = jnp.cumsum(per_row, axis=0) - per_row
    place = jnp.sum(hits * earlier[:, None, :], axis=2)
    slot_of = (owner * slots_per + place).reshape(-1)
    slot_ids = jnp.arange(total_slots, dtype=jnp.int32)
    pick = (slot_ids[:, None] == slot_of[None, :]).astype(jnp.bfloat16)
    row_pick = jnp.sum(
        pick.reshape(total_slots, tok_count, listed).astype(jnp.float32), axis=2
    ).astype(jnp.bfloat16)
    send_g = jnp.dot(row_pick, g_rows, preferred_element_type=jnp.float32).astype(jnp.bfloat16)
    block_act = jnp.dot(
        pick, acts_l.reshape(tok_count * listed, block), preferred_element_type=jnp.float32
    ).astype(jnp.bfloat16)
    within_hot = (within.reshape(-1)[:, None] == jnp.arange(held, dtype=jnp.int32)[None, :]).astype(
        jnp.bfloat16
    )
    slot_within = jnp.dot(pick, within_hot, preferred_element_type=jnp.float32).astype(jnp.bfloat16)
    send_act = (slot_within[:, :, None] * block_act[:, None, :]).reshape(total_slots, held * block)
    send_g = send_g.reshape(peers, slots_per, width)
    send_act = send_act.reshape(peers, slots_per, held * block)
    recv_g, recv_act = (
        lax.all_to_all(send_g, "dict", split_axis=0, concat_axis=0, tiled=True),
        lax.all_to_all(send_act, "dict", split_axis=0, concat_axis=0, tiled=True),
    )
    coef_here, contrib_here = owner_work(recv_g, recv_act, dec_local, enc_local)
    coef_back, contrib_back = (
        lax.all_to_all(coef_here, "dict", split_axis=0, concat_axis=0, tiled=True),
        lax.all_to_all(contrib_here, "dict", split_axis=0, concat_axis=0, tiled=True),
    )
    coef_back = coef_back.reshape(total_slots, held, block)
    contrib_back = contrib_back.reshape(total_slots, width)
    coef_chosen = jnp.sum(
        slot_within.astype(jnp.float32)[:, :, None] * coef_back.astype(jnp.float32), axis=1
    ).astype(jnp.bfloat16)
    coef_rows = lax.dot_general(
        pick, coef_chosen, (((0,), (0,)), ((), ())), preferred_element_type=jnp.float32
    )
    attr = (acts_l.reshape(tok_count * listed, block).astype(jnp.float32) * coef_rows).reshape(
        tok_count, listed * block
    )
    summed = lax.dot_general(
        row_pick, contrib_back, (((0,), (0,)), ((), ())), preferred_element_type=jnp.float32
    )
    new_g = (g_rows.astype(jnp.float32) + scale_l[:, None] * gain_l[None, :] * summed).astype(
        jnp.bfloat16
    )
    return (attr, new_g)


def slot_device(cotangent, routes, acts, decoder, encoder, gain, inv_rms):
    peers = lax.axis_size("dict")
    depth = lax.axis_size("section")
    here = lax.axis_index("section")
    routes_l = routes[0]
    acts_l = acts[0]
    dec_local = decoder[0]
    enc_local = encoder[0]
    gain_l = gain[0]
    scale_l = inv_rms[0]
    tok_count, listed = routes_l.shape
    attr_keep = jnp.zeros((tok_count, acts_l.shape[1]), jnp.float32)
    grad_keep = jnp.zeros(cotangent.shape, jnp.bfloat16)
    g_new = cotangent
    for turn in range(depth):
        if turn > 0:
            g_now = passed_along(g_new, "section", -1)
        else:
            g_now = cotangent
        active = here == depth - 1 - turn
        attr, g_new = layer_pass(
            g_now, routes_l, acts_l, dec_local, enc_local, gain_l, scale_l, peers
        )
        attr_keep = jnp.where(active, attr, attr_keep)
        grad_keep = jnp.where(active, g_new, grad_keep)
    return (attr_keep[None], grad_keep[None])


def swap_cores(block):
    return lax.ppermute(block, "section", [(0, 1), (1, 0)])


def exchange(parts, sign):
    peers = parts.shape[0]
    moved = [parts[0]]
    for shift in range(1, peers):
        route = [(d, (d + sign * shift) % peers) for d in range(peers)]
        moved.append(lax.ppermute(parts[shift], "dict", route))
    return jnp.stack(moved, axis=0)


def after(value, gate):
    return lax.optimization_barrier((value, gate))


def split_layer(g_half, routes_l, acts_l, own, other, is_own, gain_half, scale_l, gate):
    peers = lax.axis_size("dict")
    me = lax.axis_index("dict")
    rows, listed = routes_l.shape
    block = acts_l.shape[1] // listed
    held = own[0].shape[0] // block
    half = g_half.shape[1]
    owner = routes_l // held
    within = routes_l - owner * held
    rel = (owner - me) % peers
    shifts = jnp.arange(peers, dtype=jnp.int32)
    at_rel = (rel[:, :, None] == shifts[None, None, :]).astype(jnp.bfloat16)
    act_grid = acts_l.reshape(rows, listed, block)
    live = (act_grid > 0).astype(jnp.bfloat16) * (1 + within).astype(jnp.bfloat16)[:, :, None]
    placed = jnp.einsum(
        "rks,rkj->srj", at_rel, live, preferred_element_type=jnp.float32
    ).astype(jnp.bfloat16)
    sent = jnp.concatenate(
        [jnp.broadcast_to(g_half[None], (peers, rows, half)), placed], axis=-1
    )
    if gate is not None:
        sent, other = after(sent, other)
    got = exchange(sent, 1).reshape(peers * rows, half + block)
    g_all = got[:, :half]
    code_all = got[:, half:]

    def with_dec(dec):
        return lax.dot_general(
            g_all, dec, (((1,), (1,)), ((), ())), preferred_element_type=jnp.float32
        )

    part = jnp.where(is_own, with_dec(own[0]), with_dec(other[0]))
    paired = swap_cores(jnp.concatenate([part, code_all.astype(jnp.float32)], axis=1))
    coef = (part + paired[:, :held * block]).astype(jnp.bfloat16)
    code = jnp.where(is_own, code_all.astype(jnp.float32), paired[:, held * block:])
    marks = jnp.concatenate([code == spot + 1 for spot in range(held)], axis=1)
    dz = jnp.where(marks, coef, jnp.zeros_like(coef))

    def with_enc(enc):
        return jnp.dot(dz, enc, preferred_element_type=jnp.float32)

    contrib = jnp.where(is_own, with_enc(own[1]), with_enc(other[1])).astype(jnp.bfloat16)
    dz_pick = dz[:, :block]
    for spot in range(1, held):
        dz_pick = dz_pick + dz[:, spot * block:(spot + 1) * block]
    back = jnp.concatenate([contrib, dz_pick], axis=-1).reshape(peers, rows, half + block)
    returned = exchange(back, -1)
    total = jnp.sum(returned[:, :, :half].astype(jnp.float32), axis=0)
    dz_back = returned[:, :, half:]
    dz_slot = jnp.einsum("rks,srj->rkj", at_rel, dz_back, preferred_element_type=jnp.float32)
    attr = (act_grid.astype(jnp.float32) * dz_slot).reshape(rows, listed * block)
    new_half = (g_half.astype(jnp.float32) + scale_l[:, None] * gain_half[None, :] * total).astype(
        jnp.bfloat16
    )
    return attr, new_half


def split_device(cotangent, routes, acts, decoder, encoder, gain, inv_rms):
    depth = lax.axis_size("section")
    here = lax.axis_index("section")
    rows, width = cotangent.shape
    blocks = decoder.shape[1]
    half = width // depth
    mine = here * half
    theirs = (1 - here) * half
    small = jnp.concatenate([gain[0], inv_rms[0]], axis=0)
    other_small = swap_cores(small)
    sent_w = jnp.concatenate(
        [
            lax.dynamic_slice_in_dim(decoder[0], theirs, half, axis=1),
            lax.dynamic_slice_in_dim(encoder[0], theirs, half, axis=1),
        ],
        axis=0,
    )
    other_w = swap_cores(sent_w)
    other = (other_w[:blocks], other_w[blocks:])
    own = (
        lax.dynamic_slice_in_dim(decoder[0], mine, half, axis=1),
        lax.dynamic_slice_in_dim(encoder[0], mine, half, axis=1),
    )
    attr_keep = jnp.zeros((rows, acts.shape[2]), jnp.float32)
    grad_keep = jnp.zeros(cotangent.shape, jnp.bfloat16)
    g_half = lax.dynamic_slice_in_dim(cotangent, mine, half, axis=1)
    for layer in reversed(range(depth)):
        is_own = here == layer
        s = jnp.where(is_own, small, other_small)
        gain_half = lax.dynamic_slice_in_dim(s[:width], mine, half, axis=0)
        scale_l = s[width:width + rows]
        gate = True if layer == depth - 1 else None
        attr, g_half = split_layer(
            g_half, routes[0], acts[0], own, other, is_own, gain_half, scale_l, gate
        )
        partner = swap_cores(g_half)
        full = jnp.where(
            here == 0,
            jnp.concatenate([g_half, partner], axis=1),
            jnp.concatenate([partner, g_half], axis=1),
        )
        attr_keep = jnp.where(is_own, attr, attr_keep)
        grad_keep = jnp.where(is_own, full, grad_keep)
    return (attr_keep[None], grad_keep[None])


def per_device(cotangent, routes, acts, decoder, encoder, gain, inv_rms):
    peers = lax.axis_size("dict")
    depth = lax.axis_size("section")
    listed = routes.shape[-1]
    width = cotangent.shape[1]
    if listed == peers and depth == 2 and width % (depth * 128) == 0:
        return split_device(cotangent, routes, acts, decoder, encoder, gain, inv_rms)
    return slot_device(cotangent, routes, acts, decoder, encoder, gain, inv_rms)


def solution(mesh):
    placed = (
        P(("groups", "dict"), None),
        P("section", ("groups", "dict"), None),
        P("section", ("groups", "dict"), None),
        P("section", "dict", None),
        P("section", "dict", None),
        P("section", None),
        P("section", ("groups", "dict")),
    )
    return jax.shard_map(
        per_device,
        mesh=mesh,
        in_specs=placed,
        out_specs=(P("section", ("groups", "dict"), None), P("section", ("groups", "dict"), None)),
        check_vma=False,
    )
```

```python
import jax
import jax.numpy as jnp
from jax import lax
from jax.sharding import PartitionSpec as P


def passed_along(block, axis, distance):
    devices = range(lax.axis_size(axis))
    route = [(i - distance, i) for i in devices if i - distance in devices]
    return lax.ppermute(block, axis, route)


def owner_work(recv_g, recv_act, dec_local, enc_local):
    width = recv_g.shape[-1]
    columns = dec_local.shape[0]
    flat_g = recv_g.reshape(-1, width)
    flat_act = recv_act.reshape(-1, columns)
    coef = lax.dot_general(
        flat_g, dec_local, (((1,), (1,)), ((), ())), preferred_element_type=jnp.float32
    ).astype(jnp.bfloat16)
    masked = jnp.where(flat_act > 0, coef, jnp.zeros_like(coef))
    contrib = jnp.dot(masked, enc_local, preferred_element_type=jnp.float32).astype(jnp.bfloat16)
    lead = recv_g.shape[:-1]
    return (coef.reshape(lead + (columns,)), contrib.reshape(lead + (width,)))


def layer_pass(g_rows, routes_l, acts_l, dec_local, enc_local, gain_l, scale_l, peers):
    tok_count, listed = routes_l.shape
    block = acts_l.shape[1] // listed
    width = dec_local.shape[1]
    held = dec_local.shape[0] // block
    slots_per = (tok_count * listed + peers - 1) // peers
    total_slots = peers * slots_per
    owner = routes_l // held
    within = routes_l - owner * held
    owners = jnp.arange(peers, dtype=jnp.int32)
    hits = (owner[:, :, None] == owners[None, None, :]).astype(jnp.int32)
    per_row = jnp.sum(hits, axis=1)
    earlier = jnp.cumsum(per_row, axis=0) - per_row
    place = jnp.sum(hits * earlier[:, None, :], axis=2)
    slot_of = (owner * slots_per + place).reshape(-1)
    slot_ids = jnp.arange(total_slots, dtype=jnp.int32)
    pick = (slot_ids[:, None] == slot_of[None, :]).astype(jnp.bfloat16)
    row_pick = jnp.sum(
        pick.reshape(total_slots, tok_count, listed).astype(jnp.float32), axis=2
    ).astype(jnp.bfloat16)
    send_g = jnp.dot(row_pick, g_rows, preferred_element_type=jnp.float32).astype(jnp.bfloat16)
    block_act = jnp.dot(
        pick, acts_l.reshape(tok_count * listed, block), preferred_element_type=jnp.float32
    ).astype(jnp.bfloat16)
    within_hot = (within.reshape(-1)[:, None] == jnp.arange(held, dtype=jnp.int32)[None, :]).astype(
        jnp.bfloat16
    )
    slot_within = jnp.dot(pick, within_hot, preferred_element_type=jnp.float32).astype(jnp.bfloat16)
    send_act = (slot_within[:, :, None] * block_act[:, None, :]).reshape(total_slots, held * block)
    send_g = send_g.reshape(peers, slots_per, width)
    send_act = send_act.reshape(peers, slots_per, held * block)
    recv_g, recv_act = (
        lax.all_to_all(send_g, "dict", split_axis=0, concat_axis=0, tiled=True),
        lax.all_to_all(send_act, "dict", split_axis=0, concat_axis=0, tiled=True),
    )
    coef_here, contrib_here = owner_work(recv_g, recv_act, dec_local, enc_local)
    coef_back, contrib_back = (
        lax.all_to_all(coef_here, "dict", split_axis=0, concat_axis=0, tiled=True),
        lax.all_to_all(contrib_here, "dict", split_axis=0, concat_axis=0, tiled=True),
    )
    coef_back = coef_back.reshape(total_slots, held, block)
    contrib_back = contrib_back.reshape(total_slots, width)
    coef_chosen = jnp.sum(
        slot_within.astype(jnp.float32)[:, :, None] * coef_back.astype(jnp.float32), axis=1
    ).astype(jnp.bfloat16)
    coef_rows = lax.dot_general(
        pick, coef_chosen, (((0,), (0,)), ((), ())), preferred_element_type=jnp.float32
    )
    attr = (acts_l.reshape(tok_count * listed, block).astype(jnp.float32) * coef_rows).reshape(
        tok_count, listed * block
    )
    summed = lax.dot_general(
        row_pick, contrib_back, (((0,), (0,)), ((), ())), preferred_element_type=jnp.float32
    )
    new_g = (g_rows.astype(jnp.float32) + scale_l[:, None] * gain_l[None, :] * summed).astype(
        jnp.bfloat16
    )
    return (attr, new_g)


def slot_device(cotangent, routes, acts, decoder, encoder, gain, inv_rms):
    peers = lax.axis_size("dict")
    depth = lax.axis_size("section")
    here = lax.axis_index("section")
    routes_l = routes[0]
    acts_l = acts[0]
    dec_local = decoder[0]
    enc_local = encoder[0]
    gain_l = gain[0]
    scale_l = inv_rms[0]
    tok_count, listed = routes_l.shape
    attr_keep = jnp.zeros((tok_count, acts_l.shape[1]), jnp.float32)
    grad_keep = jnp.zeros(cotangent.shape, jnp.bfloat16)
    g_new = cotangent
    for turn in range(depth):
        if turn > 0:
            g_now = passed_along(g_new, "section", -1)
        else:
            g_now = cotangent
        active = here == depth - 1 - turn
        attr, g_new = layer_pass(
            g_now, routes_l, acts_l, dec_local, enc_local, gain_l, scale_l, peers
        )
        attr_keep = jnp.where(active, attr, attr_keep)
        grad_keep = jnp.where(active, g_new, grad_keep)
    return (attr_keep[None], grad_keep[None])


def swap_cores(block):
    return lax.ppermute(block, "section", [(0, 1), (1, 0)])


def exchange(parts, sign):
    peers = parts.shape[0]
    moved = [parts[0]]
    for shift in range(1, peers):
        route = [(d, (d + sign * shift) % peers) for d in range(peers)]
        moved.append(lax.ppermute(parts[shift], "dict", route))
    return jnp.stack(moved, axis=0)


def send_pieces(pieces, shifts, sign, peers):
    moved = []
    for piece, shift in zip(pieces, shifts):
        if shift == 0:
            moved.append(piece)
        else:
            route = [(d, (d + sign * shift) % peers) for d in range(peers)]
            moved.append(lax.ppermute(piece, "dict", route))
    return moved


def split_layer(g_half, routes_l, acts_l, own, other, is_own, gain_half, scale_l):
    peers = lax.axis_size("dict")
    me = lax.axis_index("dict")
    rows, listed = routes_l.shape
    block = acts_l.shape[1] // listed
    held = own[0].shape[0] // block
    half = g_half.shape[1]
    owner = routes_l // held
    within = routes_l - owner * held
    rel = (owner - me) % peers
    shifts = jnp.arange(peers, dtype=jnp.int32)
    at_rel = (rel[:, :, None] == shifts[None, None, :]).astype(jnp.bfloat16)
    act_grid = acts_l.reshape(rows, listed, block)
    live = (act_grid > 0).astype(jnp.bfloat16) * (1 + within).astype(jnp.bfloat16)[:, :, None]
    placed = jnp.einsum(
        "rks,rkj->srj", at_rel, live, preferred_element_type=jnp.float32
    ).astype(jnp.bfloat16)
    sent = jnp.concatenate(
        [jnp.broadcast_to(g_half[None], (peers, rows, half)), placed], axis=-1
    )
    order = list(range(peers))
    got = send_pieces([sent[s] for s in order], order, 1, peers)
    cut = peers // 2 + 1
    returned = [None] * peers
    for group in (order[:cut], order[cut:]):
        taken = jnp.concatenate([got[s] for s in group], axis=0)
        g_all = taken[:, :half]
        code_all = taken[:, half:]

        def with_dec(dec):
            return lax.dot_general(
                g_all, dec, (((1,), (1,)), ((), ())), preferred_element_type=jnp.float32
            )

        part = jnp.where(is_own, with_dec(own[0]), with_dec(other[0]))
        paired = swap_cores(jnp.concatenate([part, code_all.astype(jnp.float32)], axis=1))
        coef = (part + paired[:, :held * block]).astype(jnp.bfloat16)
        code = jnp.where(is_own, code_all.astype(jnp.float32), paired[:, held * block:])
        marks = jnp.concatenate([code == spot + 1 for spot in range(held)], axis=1)
        dz = jnp.where(marks, coef, jnp.zeros_like(coef))

        def with_enc(enc):
            return jnp.dot(dz, enc, preferred_element_type=jnp.float32)

        contrib = jnp.where(is_own, with_enc(own[1]), with_enc(other[1])).astype(jnp.bfloat16)
        dz_pick = dz[:, :block]
        for spot in range(1, held):
            dz_pick = dz_pick + dz[:, spot * block:(spot + 1) * block]
        back = jnp.concatenate([contrib, dz_pick], axis=-1)
        pieces = [back[i * rows:(i + 1) * rows] for i in range(len(group))]
        for shift, piece in zip(group, send_pieces(pieces, group, -1, peers)):
            returned[shift] = piece
    returned = jnp.stack(returned, axis=0)
    total = jnp.sum(returned[:, :, :half].astype(jnp.float32), axis=0)
    dz_back = returned[:, :, half:]
    dz_slot = jnp.einsum("rks,srj->rkj", at_rel, dz_back, preferred_element_type=jnp.float32)
    attr = (act_grid.astype(jnp.float32) * dz_slot).reshape(rows, listed * block)
    new_half = (g_half.astype(jnp.float32) + scale_l[:, None] * gain_half[None, :] * total).astype(
        jnp.bfloat16
    )
    return attr, new_half


def split_device(cotangent, routes, acts, decoder, encoder, gain, inv_rms):
    depth = lax.axis_size("section")
    here = lax.axis_index("section")
    rows, width = cotangent.shape
    blocks = decoder.shape[1]
    half = width // depth
    mine = here * half
    theirs = (1 - here) * half
    small = jnp.concatenate([gain[0], inv_rms[0]], axis=0)
    other_small = swap_cores(small)
    sent_w = jnp.concatenate(
        [
            lax.dynamic_slice_in_dim(decoder[0], theirs, half, axis=1),
            lax.dynamic_slice_in_dim(encoder[0], theirs, half, axis=1),
        ],
        axis=0,
    )
    other_w = swap_cores(sent_w)
    other = (other_w[:blocks], other_w[blocks:])
    own = (
        lax.dynamic_slice_in_dim(decoder[0], mine, half, axis=1),
        lax.dynamic_slice_in_dim(encoder[0], mine, half, axis=1),
    )
    attr_keep = jnp.zeros((rows, acts.shape[2]), jnp.float32)
    grad_keep = jnp.zeros(cotangent.shape, jnp.bfloat16)
    g_half = lax.dynamic_slice_in_dim(cotangent, mine, half, axis=1)
    for layer in reversed(range(depth)):
        is_own = here == layer
        s = jnp.where(is_own, small, other_small)
        gain_half = lax.dynamic_slice_in_dim(s[:width], mine, half, axis=0)
        scale_l = s[width:width + rows]
        attr, g_half = split_layer(g_half, routes[0], acts[0], own, other, is_own, gain_half, scale_l)
        partner = swap_cores(g_half)
        full = jnp.where(
            here == 0,
            jnp.concatenate([g_half, partner], axis=1),
            jnp.concatenate([partner, g_half], axis=1),
        )
        attr_keep = jnp.where(is_own, attr, attr_keep)
        grad_keep = jnp.where(is_own, full, grad_keep)
    return (attr_keep[None], grad_keep[None])


def per_device(cotangent, routes, acts, decoder, encoder, gain, inv_rms):
    peers = lax.axis_size("dict")
    depth = lax.axis_size("section")
    listed = routes.shape[-1]
    width = cotangent.shape[1]
    if listed == peers and depth == 2 and width % (depth * 128) == 0:
        return split_device(cotangent, routes, acts, decoder, encoder, gain, inv_rms)
    return slot_device(cotangent, routes, acts, decoder, encoder, gain, inv_rms)


def solution(mesh):
    placed = (
        P(("groups", "dict"), None),
        P("section", ("groups", "dict"), None),
        P("section", ("groups", "dict"), None),
        P("section", "dict", None),
        P("section", "dict", None),
        P("section", None),
        P("section", ("groups", "dict")),
    )
    return jax.shard_map(
        per_device,
        mesh=mesh,
        in_specs=placed,
        out_specs=(P("section", ("groups", "dict"), None), P("section", ("groups", "dict"), None)),
        check_vma=False,
    )
```

```python
import jax
import jax.numpy as jnp
from jax import lax
from jax.sharding import PartitionSpec as P


def passed_along(block, axis, distance):
    devices = range(lax.axis_size(axis))
    route = [(i - distance, i) for i in devices if i - distance in devices]
    return lax.ppermute(block, axis, route)


def owner_work(recv_g, recv_act, dec_local, enc_local):
    width = recv_g.shape[-1]
    columns = dec_local.shape[0]
    flat_g = recv_g.reshape(-1, width)
    flat_act = recv_act.reshape(-1, columns)
    coef = lax.dot_general(
        flat_g, dec_local, (((1,), (1,)), ((), ())), preferred_element_type=jnp.float32
    ).astype(jnp.bfloat16)
    masked = jnp.where(flat_act > 0, coef, jnp.zeros_like(coef))
    contrib = jnp.dot(masked, enc_local, preferred_element_type=jnp.float32).astype(jnp.bfloat16)
    lead = recv_g.shape[:-1]
    return (coef.reshape(lead + (columns,)), contrib.reshape(lead + (width,)))


def layer_pass(g_rows, routes_l, acts_l, dec_local, enc_local, gain_l, scale_l, peers):
    tok_count, listed = routes_l.shape
    block = acts_l.shape[1] // listed
    width = dec_local.shape[1]
    held = dec_local.shape[0] // block
    slots_per = (tok_count * listed + peers - 1) // peers
    total_slots = peers * slots_per
    owner = routes_l // held
    within = routes_l - owner * held
    owners = jnp.arange(peers, dtype=jnp.int32)
    hits = (owner[:, :, None] == owners[None, None, :]).astype(jnp.int32)
    per_row = jnp.sum(hits, axis=1)
    earlier = jnp.cumsum(per_row, axis=0) - per_row
    place = jnp.sum(hits * earlier[:, None, :], axis=2)
    slot_of = (owner * slots_per + place).reshape(-1)
    slot_ids = jnp.arange(total_slots, dtype=jnp.int32)
    pick = (slot_ids[:, None] == slot_of[None, :]).astype(jnp.bfloat16)
    row_pick = jnp.sum(
        pick.reshape(total_slots, tok_count, listed).astype(jnp.float32), axis=2
    ).astype(jnp.bfloat16)
    send_g = jnp.dot(row_pick, g_rows, preferred_element_type=jnp.float32).astype(jnp.bfloat16)
    block_act = jnp.dot(
        pick, acts_l.reshape(tok_count * listed, block), preferred_element_type=jnp.float32
    ).astype(jnp.bfloat16)
    within_hot = (within.reshape(-1)[:, None] == jnp.arange(held, dtype=jnp.int32)[None, :]).astype(
        jnp.bfloat16
    )
    slot_within = jnp.dot(pick, within_hot, preferred_element_type=jnp.float32).astype(jnp.bfloat16)
    send_act = (slot_within[:, :, None] * block_act[:, None, :]).reshape(total_slots, held * block)
    send_g = send_g.reshape(peers, slots_per, width)
    send_act = send_act.reshape(peers, slots_per, held * block)
    recv_g, recv_act = (
        lax.all_to_all(send_g, "dict", split_axis=0, concat_axis=0, tiled=True),
        lax.all_to_all(send_act, "dict", split_axis=0, concat_axis=0, tiled=True),
    )
    coef_here, contrib_here = owner_work(recv_g, recv_act, dec_local, enc_local)
    coef_back, contrib_back = (
        lax.all_to_all(coef_here, "dict", split_axis=0, concat_axis=0, tiled=True),
        lax.all_to_all(contrib_here, "dict", split_axis=0, concat_axis=0, tiled=True),
    )
    coef_back = coef_back.reshape(total_slots, held, block)
    contrib_back = contrib_back.reshape(total_slots, width)
    coef_chosen = jnp.sum(
        slot_within.astype(jnp.float32)[:, :, None] * coef_back.astype(jnp.float32), axis=1
    ).astype(jnp.bfloat16)
    coef_rows = lax.dot_general(
        pick, coef_chosen, (((0,), (0,)), ((), ())), preferred_element_type=jnp.float32
    )
    attr = (acts_l.reshape(tok_count * listed, block).astype(jnp.float32) * coef_rows).reshape(
        tok_count, listed * block
    )
    summed = lax.dot_general(
        row_pick, contrib_back, (((0,), (0,)), ((), ())), preferred_element_type=jnp.float32
    )
    new_g = (g_rows.astype(jnp.float32) + scale_l[:, None] * gain_l[None, :] * summed).astype(
        jnp.bfloat16
    )
    return (attr, new_g)


def slot_device(cotangent, routes, acts, decoder, encoder, gain, inv_rms):
    peers = lax.axis_size("dict")
    depth = lax.axis_size("section")
    here = lax.axis_index("section")
    routes_l = routes[0]
    acts_l = acts[0]
    dec_local = decoder[0]
    enc_local = encoder[0]
    gain_l = gain[0]
    scale_l = inv_rms[0]
    tok_count, listed = routes_l.shape
    attr_keep = jnp.zeros((tok_count, acts_l.shape[1]), jnp.float32)
    grad_keep = jnp.zeros(cotangent.shape, jnp.bfloat16)
    g_new = cotangent
    for turn in range(depth):
        if turn > 0:
            g_now = passed_along(g_new, "section", -1)
        else:
            g_now = cotangent
        active = here == depth - 1 - turn
        attr, g_new = layer_pass(
            g_now, routes_l, acts_l, dec_local, enc_local, gain_l, scale_l, peers
        )
        attr_keep = jnp.where(active, attr, attr_keep)
        grad_keep = jnp.where(active, g_new, grad_keep)
    return (attr_keep[None], grad_keep[None])


def swap_cores(block):
    return lax.ppermute(block, "section", [(0, 1), (1, 0)])


def exchange(parts, sign):
    peers = parts.shape[0]
    moved = [parts[0]]
    for shift in range(1, peers):
        route = [(d, (d + sign * shift) % peers) for d in range(peers)]
        moved.append(lax.ppermute(parts[shift], "dict", route))
    return jnp.stack(moved, axis=0)


def split_layer(g_half, routes_l, acts_l, own, other, is_own, gain_half, scale_l):
    peers = lax.axis_size("dict")
    me = lax.axis_index("dict")
    rows, listed = routes_l.shape
    block = acts_l.shape[1] // listed
    held = own[0].shape[0] // block
    half = g_half.shape[1]
    owner = routes_l // held
    within = routes_l - owner * held
    rel = (owner - me) % peers
    shifts = jnp.arange(peers, dtype=jnp.int32)
    at_rel = (rel[:, :, None] == shifts[None, None, :]).astype(jnp.bfloat16)
    act_grid = acts_l.reshape(rows, listed, block)
    live = (act_grid > 0).astype(jnp.bfloat16) * (1 + within).astype(jnp.bfloat16)[:, :, None]
    hit = rel[None, :, :, None] == shifts[:, None, None, None]
    placed = jnp.sum(
        jnp.where(hit, live[None], jnp.zeros_like(live[None])), axis=2
    ).astype(jnp.bfloat16)
    sent = jnp.concatenate(
        [jnp.broadcast_to(g_half[None], (peers, rows, half)), placed], axis=-1
    )
    got = exchange(sent, 1).reshape(peers * rows, half + block)
    g_all = got[:, :half]
    code_all = got[:, half:]

    def with_dec(dec):
        return lax.dot_general(
            g_all, dec, (((1,), (1,)), ((), ())), preferred_element_type=jnp.float32
        )

    part = jnp.where(is_own, with_dec(own[0]), with_dec(other[0]))
    paired = swap_cores(jnp.concatenate([part, code_all.astype(jnp.float32)], axis=1))
    coef = (part + paired[:, :held * block]).astype(jnp.bfloat16)
    code = jnp.where(is_own, code_all.astype(jnp.float32), paired[:, held * block:])
    marks = jnp.concatenate([code == spot + 1 for spot in range(held)], axis=1)
    dz = jnp.where(marks, coef, jnp.zeros_like(coef))

    def with_enc(enc):
        return jnp.dot(dz, enc, preferred_element_type=jnp.float32)

    contrib = jnp.where(is_own, with_enc(own[1]), with_enc(other[1])).astype(jnp.bfloat16)
    dz_pick = dz[:, :block]
    for spot in range(1, held):
        dz_pick = dz_pick + dz[:, spot * block:(spot + 1) * block]
    back = jnp.concatenate([contrib, dz_pick], axis=-1).reshape(peers, rows, half + block)
    returned = exchange(back, -1)
    total = jnp.sum(returned[:, :, :half].astype(jnp.float32), axis=0)
    dz_back = returned[:, :, half:]
    dz_slot = jnp.einsum("rks,srj->rkj", at_rel, dz_back, preferred_element_type=jnp.float32)
    attr = (act_grid.astype(jnp.float32) * dz_slot).reshape(rows, listed * block)
    new_half = (g_half.astype(jnp.float32) + scale_l[:, None] * gain_half[None, :] * total).astype(
        jnp.bfloat16
    )
    return attr, new_half


def split_device(cotangent, routes, acts, decoder, encoder, gain, inv_rms):
    depth = lax.axis_size("section")
    here = lax.axis_index("section")
    rows, width = cotangent.shape
    blocks = decoder.shape[1]
    half = width // depth
    mine = here * half
    theirs = (1 - here) * half
    small = jnp.concatenate([gain[0], inv_rms[0]], axis=0)
    other_small = swap_cores(small)
    sent_w = jnp.concatenate(
        [
            lax.dynamic_slice_in_dim(decoder[0], theirs, half, axis=1),
            lax.dynamic_slice_in_dim(encoder[0], theirs, half, axis=1),
        ],
        axis=0,
    )
    other_w = swap_cores(sent_w)
    other = (other_w[:blocks], other_w[blocks:])
    own = (
        lax.dynamic_slice_in_dim(decoder[0], mine, half, axis=1),
        lax.dynamic_slice_in_dim(encoder[0], mine, half, axis=1),
    )
    attr_keep = jnp.zeros((rows, acts.shape[2]), jnp.float32)
    grad_keep = jnp.zeros(cotangent.shape, jnp.bfloat16)
    g_half = lax.dynamic_slice_in_dim(cotangent, mine, half, axis=1)
    for layer in reversed(range(depth)):
        is_own = here == layer
        s = jnp.where(is_own, small, other_small)
        gain_half = lax.dynamic_slice_in_dim(s[:width], mine, half, axis=0)
        scale_l = s[width:width + rows]
        attr, g_half = split_layer(g_half, routes[0], acts[0], own, other, is_own, gain_half, scale_l)
        partner = swap_cores(g_half)
        full = jnp.where(
            here == 0,
            jnp.concatenate([g_half, partner], axis=1),
            jnp.concatenate([partner, g_half], axis=1),
        )
        attr_keep = jnp.where(is_own, attr, attr_keep)
        grad_keep = jnp.where(is_own, full, grad_keep)
    return (attr_keep[None], grad_keep[None])


def per_device(cotangent, routes, acts, decoder, encoder, gain, inv_rms):
    peers = lax.axis_size("dict")
    depth = lax.axis_size("section")
    listed = routes.shape[-1]
    width = cotangent.shape[1]
    if listed == peers and depth == 2 and width % (depth * 128) == 0:
        return split_device(cotangent, routes, acts, decoder, encoder, gain, inv_rms)
    return slot_device(cotangent, routes, acts, decoder, encoder, gain, inv_rms)


def solution(mesh):
    placed = (
        P(("groups", "dict"), None),
        P("section", ("groups", "dict"), None),
        P("section", ("groups", "dict"), None),
        P("section", "dict", None),
        P("section", "dict", None),
        P("section", None),
        P("section", ("groups", "dict")),
    )
    return jax.shard_map(
        per_device,
        mesh=mesh,
        in_specs=placed,
        out_specs=(P("section", ("groups", "dict"), None), P("section", ("groups", "dict"), None)),
        check_vma=False,
    )
```

```python
import jax
import jax.numpy as jnp
from jax import lax
from jax.sharding import PartitionSpec as P


def passed_along(block, axis, distance):
    devices = range(lax.axis_size(axis))
    route = [(i - distance, i) for i in devices if i - distance in devices]
    return lax.ppermute(block, axis, route)


def owner_work(recv_g, recv_act, dec_local, enc_local):
    width = recv_g.shape[-1]
    columns = dec_local.shape[0]
    flat_g = recv_g.reshape(-1, width)
    flat_act = recv_act.reshape(-1, columns)
    coef = lax.dot_general(
        flat_g, dec_local, (((1,), (1,)), ((), ())), preferred_element_type=jnp.float32
    ).astype(jnp.bfloat16)
    masked = jnp.where(flat_act > 0, coef, jnp.zeros_like(coef))
    contrib = jnp.dot(masked, enc_local, preferred_element_type=jnp.float32).astype(jnp.bfloat16)
    lead = recv_g.shape[:-1]
    return (coef.reshape(lead + (columns,)), contrib.reshape(lead + (width,)))


def layer_pass(g_rows, routes_l, acts_l, dec_local, enc_local, gain_l, scale_l, peers):
    tok_count, listed = routes_l.shape
    block = acts_l.shape[1] // listed
    width = dec_local.shape[1]
    held = dec_local.shape[0] // block
    slots_per = (tok_count * listed + peers - 1) // peers
    total_slots = peers * slots_per
    owner = routes_l // held
    within = routes_l - owner * held
    owners = jnp.arange(peers, dtype=jnp.int32)
    hits = (owner[:, :, None] == owners[None, None, :]).astype(jnp.int32)
    per_row = jnp.sum(hits, axis=1)
    earlier = jnp.cumsum(per_row, axis=0) - per_row
    place = jnp.sum(hits * earlier[:, None, :], axis=2)
    slot_of = (owner * slots_per + place).reshape(-1)
    slot_ids = jnp.arange(total_slots, dtype=jnp.int32)
    pick = (slot_ids[:, None] == slot_of[None, :]).astype(jnp.bfloat16)
    row_pick = jnp.sum(
        pick.reshape(total_slots, tok_count, listed).astype(jnp.float32), axis=2
    ).astype(jnp.bfloat16)
    send_g = jnp.dot(row_pick, g_rows, preferred_element_type=jnp.float32).astype(jnp.bfloat16)
    block_act = jnp.dot(
        pick, acts_l.reshape(tok_count * listed, block), preferred_element_type=jnp.float32
    ).astype(jnp.bfloat16)
    within_hot = (within.reshape(-1)[:, None] == jnp.arange(held, dtype=jnp.int32)[None, :]).astype(
        jnp.bfloat16
    )
    slot_within = jnp.dot(pick, within_hot, preferred_element_type=jnp.float32).astype(jnp.bfloat16)
    send_act = (slot_within[:, :, None] * block_act[:, None, :]).reshape(total_slots, held * block)
    send_g = send_g.reshape(peers, slots_per, width)
    send_act = send_act.reshape(peers, slots_per, held * block)
    recv_g, recv_act = (
        lax.all_to_all(send_g, "dict", split_axis=0, concat_axis=0, tiled=True),
        lax.all_to_all(send_act, "dict", split_axis=0, concat_axis=0, tiled=True),
    )
    coef_here, contrib_here = owner_work(recv_g, recv_act, dec_local, enc_local)
    coef_back, contrib_back = (
        lax.all_to_all(coef_here, "dict", split_axis=0, concat_axis=0, tiled=True),
        lax.all_to_all(contrib_here, "dict", split_axis=0, concat_axis=0, tiled=True),
    )
    coef_back = coef_back.reshape(total_slots, held, block)
    contrib_back = contrib_back.reshape(total_slots, width)
    coef_chosen = jnp.sum(
        slot_within.astype(jnp.float32)[:, :, None] * coef_back.astype(jnp.float32), axis=1
    ).astype(jnp.bfloat16)
    coef_rows = lax.dot_general(
        pick, coef_chosen, (((0,), (0,)), ((), ())), preferred_element_type=jnp.float32
    )
    attr = (acts_l.reshape(tok_count * listed, block).astype(jnp.float32) * coef_rows).reshape(
        tok_count, listed * block
    )
    summed = lax.dot_general(
        row_pick, contrib_back, (((0,), (0,)), ((), ())), preferred_element_type=jnp.float32
    )
    new_g = (g_rows.astype(jnp.float32) + scale_l[:, None] * gain_l[None, :] * summed).astype(
        jnp.bfloat16
    )
    return (attr, new_g)


def slot_device(cotangent, routes, acts, decoder, encoder, gain, inv_rms):
    peers = lax.axis_size("dict")
    depth = lax.axis_size("section")
    here = lax.axis_index("section")
    routes_l = routes[0]
    acts_l = acts[0]
    dec_local = decoder[0]
    enc_local = encoder[0]
    gain_l = gain[0]
    scale_l = inv_rms[0]
    tok_count, listed = routes_l.shape
    attr_keep = jnp.zeros((tok_count, acts_l.shape[1]), jnp.float32)
    grad_keep = jnp.zeros(cotangent.shape, jnp.bfloat16)
    g_new = cotangent
    for turn in range(depth):
        if turn > 0:
            g_now = passed_along(g_new, "section", -1)
        else:
            g_now = cotangent
        active = here == depth - 1 - turn
        attr, g_new = layer_pass(
            g_now, routes_l, acts_l, dec_local, enc_local, gain_l, scale_l, peers
        )
        attr_keep = jnp.where(active, attr, attr_keep)
        grad_keep = jnp.where(active, g_new, grad_keep)
    return (attr_keep[None], grad_keep[None])


def swap_cores(block):
    return lax.ppermute(block, "section", [(0, 1), (1, 0)])


def exchange(parts, sign, joined=False):
    peers = parts.shape[0]
    moved = [parts[0]]
    for shift in range(1, peers):
        route = [(d, (d + sign * shift) % peers) for d in range(peers)]
        moved.append(lax.ppermute(parts[shift], "dict", route))
    if joined:
        return jnp.concatenate(moved, axis=0).reshape(parts.shape)
    return jnp.stack(moved, axis=0)


def split_layer(g_half, routes_l, acts_l, own, other, is_own, gain_half, scale_l, joined):
    peers = lax.axis_size("dict")
    me = lax.axis_index("dict")
    rows, listed = routes_l.shape
    block = acts_l.shape[1] // listed
    held = own[0].shape[0] // block
    half = g_half.shape[1]
    owner = routes_l // held
    within = routes_l - owner * held
    rel = (owner - me) % peers
    shifts = jnp.arange(peers, dtype=jnp.int32)
    at_rel = (rel[:, :, None] == shifts[None, None, :]).astype(jnp.bfloat16)
    act_grid = acts_l.reshape(rows, listed, block)
    live = (act_grid > 0).astype(jnp.bfloat16) * (1 + within).astype(jnp.bfloat16)[:, :, None]
    placed = jnp.einsum(
        "rks,rkj->srj", at_rel, live, preferred_element_type=jnp.float32
    ).astype(jnp.bfloat16)
    sent = jnp.concatenate(
        [jnp.broadcast_to(g_half[None], (peers, rows, half)), placed], axis=-1
    )
    got = exchange(sent, 1, joined).reshape(peers * rows, half + block)
    g_all = got[:, :half]
    code_all = got[:, half:]

    def with_dec(dec):
        return lax.dot_general(
            g_all, dec, (((1,), (1,)), ((), ())), preferred_element_type=jnp.float32
        )

    part = jnp.where(is_own, with_dec(own[0]), with_dec(other[0]))
    paired = swap_cores(jnp.concatenate([part, code_all.astype(jnp.float32)], axis=1))
    coef = (part + paired[:, :held * block]).astype(jnp.bfloat16)
    code = jnp.where(is_own, code_all.astype(jnp.float32), paired[:, held * block:])
    marks = jnp.concatenate([code == spot + 1 for spot in range(held)], axis=1)
    dz = jnp.where(marks, coef, jnp.zeros_like(coef))

    def with_enc(enc):
        return jnp.dot(dz, enc, preferred_element_type=jnp.float32)

    contrib = jnp.where(is_own, with_enc(own[1]), with_enc(other[1])).astype(jnp.bfloat16)
    dz_pick = dz[:, :block]
    for spot in range(1, held):
        dz_pick = dz_pick + dz[:, spot * block:(spot + 1) * block]
    back = jnp.concatenate([contrib, dz_pick], axis=-1).reshape(peers, rows, half + block)
    returned = exchange(back, -1)
    total = jnp.sum(returned[:, :, :half].astype(jnp.float32), axis=0)
    dz_back = returned[:, :, half:]
    dz_slot = jnp.einsum("rks,srj->rkj", at_rel, dz_back, preferred_element_type=jnp.float32)
    attr = (act_grid.astype(jnp.float32) * dz_slot).reshape(rows, listed * block)
    new_half = (g_half.astype(jnp.float32) + scale_l[:, None] * gain_half[None, :] * total).astype(
        jnp.bfloat16
    )
    return attr, new_half


def split_device(cotangent, routes, acts, decoder, encoder, gain, inv_rms):
    depth = lax.axis_size("section")
    here = lax.axis_index("section")
    rows, width = cotangent.shape
    blocks = decoder.shape[1]
    half = width // depth
    mine = here * half
    theirs = (1 - here) * half
    small = jnp.concatenate([gain[0], inv_rms[0]], axis=0)
    other_small = swap_cores(small)
    sent_w = jnp.concatenate(
        [
            lax.dynamic_slice_in_dim(decoder[0], theirs, half, axis=1),
            lax.dynamic_slice_in_dim(encoder[0], theirs, half, axis=1),
        ],
        axis=0,
    )
    other_w = swap_cores(sent_w)
    other = (other_w[:blocks], other_w[blocks:])
    own = (
        lax.dynamic_slice_in_dim(decoder[0], mine, half, axis=1),
        lax.dynamic_slice_in_dim(encoder[0], mine, half, axis=1),
    )
    attr_keep = jnp.zeros((rows, acts.shape[2]), jnp.float32)
    grad_keep = jnp.zeros(cotangent.shape, jnp.bfloat16)
    g_half = lax.dynamic_slice_in_dim(cotangent, mine, half, axis=1)
    for layer in reversed(range(depth)):
        is_own = here == layer
        s = jnp.where(is_own, small, other_small)
        gain_half = lax.dynamic_slice_in_dim(s[:width], mine, half, axis=0)
        scale_l = s[width:width + rows]
        attr, g_half = split_layer(
            g_half, routes[0], acts[0], own, other, is_own, gain_half, scale_l, layer == depth - 1
        )
        partner = swap_cores(g_half)
        full = jnp.where(
            here == 0,
            jnp.concatenate([g_half, partner], axis=1),
            jnp.concatenate([partner, g_half], axis=1),
        )
        attr_keep = jnp.where(is_own, attr, attr_keep)
        grad_keep = jnp.where(is_own, full, grad_keep)
    return (attr_keep[None], grad_keep[None])


def per_device(cotangent, routes, acts, decoder, encoder, gain, inv_rms):
    peers = lax.axis_size("dict")
    depth = lax.axis_size("section")
    listed = routes.shape[-1]
    width = cotangent.shape[1]
    if listed == peers and depth == 2 and width % (depth * 128) == 0:
        return split_device(cotangent, routes, acts, decoder, encoder, gain, inv_rms)
    return slot_device(cotangent, routes, acts, decoder, encoder, gain, inv_rms)


def solution(mesh):
    placed = (
        P(("groups", "dict"), None),
        P("section", ("groups", "dict"), None),
        P("section", ("groups", "dict"), None),
        P("section", "dict", None),
        P("section", "dict", None),
        P("section", None),
        P("section", ("groups", "dict")),
    )
    return jax.shard_map(
        per_device,
        mesh=mesh,
        in_specs=placed,
        out_specs=(P("section", ("groups", "dict"), None), P("section", ("groups", "dict"), None)),
        check_vma=False,
    )
```

```python
import jax
import jax.numpy as jnp
from jax import lax
from jax.sharding import PartitionSpec as P


def passed_along(block, axis, distance):
    devices = range(lax.axis_size(axis))
    route = [(i - distance, i) for i in devices if i - distance in devices]
    return lax.ppermute(block, axis, route)


def owner_work(recv_g, recv_act, dec_local, enc_local):
    width = recv_g.shape[-1]
    columns = dec_local.shape[0]
    flat_g = recv_g.reshape(-1, width)
    flat_act = recv_act.reshape(-1, columns)
    coef = lax.dot_general(
        flat_g, dec_local, (((1,), (1,)), ((), ())), preferred_element_type=jnp.float32
    ).astype(jnp.bfloat16)
    masked = jnp.where(flat_act > 0, coef, jnp.zeros_like(coef))
    contrib = jnp.dot(masked, enc_local, preferred_element_type=jnp.float32).astype(jnp.bfloat16)
    lead = recv_g.shape[:-1]
    return (coef.reshape(lead + (columns,)), contrib.reshape(lead + (width,)))


def layer_pass(g_rows, routes_l, acts_l, dec_local, enc_local, gain_l, scale_l, peers):
    tok_count, listed = routes_l.shape
    block = acts_l.shape[1] // listed
    width = dec_local.shape[1]
    held = dec_local.shape[0] // block
    slots_per = (tok_count * listed + peers - 1) // peers
    total_slots = peers * slots_per
    owner = routes_l // held
    within = routes_l - owner * held
    owners = jnp.arange(peers, dtype=jnp.int32)
    hits = (owner[:, :, None] == owners[None, None, :]).astype(jnp.int32)
    per_row = jnp.sum(hits, axis=1)
    earlier = jnp.cumsum(per_row, axis=0) - per_row
    place = jnp.sum(hits * earlier[:, None, :], axis=2)
    slot_of = (owner * slots_per + place).reshape(-1)
    slot_ids = jnp.arange(total_slots, dtype=jnp.int32)
    pick = (slot_ids[:, None] == slot_of[None, :]).astype(jnp.bfloat16)
    row_pick = jnp.sum(
        pick.reshape(total_slots, tok_count, listed).astype(jnp.float32), axis=2
    ).astype(jnp.bfloat16)
    send_g = jnp.dot(row_pick, g_rows, preferred_element_type=jnp.float32).astype(jnp.bfloat16)
    block_act = jnp.dot(
        pick, acts_l.reshape(tok_count * listed, block), preferred_element_type=jnp.float32
    ).astype(jnp.bfloat16)
    within_hot = (within.reshape(-1)[:, None] == jnp.arange(held, dtype=jnp.int32)[None, :]).astype(
        jnp.bfloat16
    )
    slot_within = jnp.dot(pick, within_hot, preferred_element_type=jnp.float32).astype(jnp.bfloat16)
    send_act = (slot_within[:, :, None] * block_act[:, None, :]).reshape(total_slots, held * block)
    send_g = send_g.reshape(peers, slots_per, width)
    send_act = send_act.reshape(peers, slots_per, held * block)
    recv_g, recv_act = (
        lax.all_to_all(send_g, "dict", split_axis=0, concat_axis=0, tiled=True),
        lax.all_to_all(send_act, "dict", split_axis=0, concat_axis=0, tiled=True),
    )
    coef_here, contrib_here = owner_work(recv_g, recv_act, dec_local, enc_local)
    coef_back, contrib_back = (
        lax.all_to_all(coef_here, "dict", split_axis=0, concat_axis=0, tiled=True),
        lax.all_to_all(contrib_here, "dict", split_axis=0, concat_axis=0, tiled=True),
    )
    coef_back = coef_back.reshape(total_slots, held, block)
    contrib_back = contrib_back.reshape(total_slots, width)
    coef_chosen = jnp.sum(
        slot_within.astype(jnp.float32)[:, :, None] * coef_back.astype(jnp.float32), axis=1
    ).astype(jnp.bfloat16)
    coef_rows = lax.dot_general(
        pick, coef_chosen, (((0,), (0,)), ((), ())), preferred_element_type=jnp.float32
    )
    attr = (acts_l.reshape(tok_count * listed, block).astype(jnp.float32) * coef_rows).reshape(
        tok_count, listed * block
    )
    summed = lax.dot_general(
        row_pick, contrib_back, (((0,), (0,)), ((), ())), preferred_element_type=jnp.float32
    )
    new_g = (g_rows.astype(jnp.float32) + scale_l[:, None] * gain_l[None, :] * summed).astype(
        jnp.bfloat16
    )
    return (attr, new_g)


def slot_device(cotangent, routes, acts, decoder, encoder, gain, inv_rms):
    peers = lax.axis_size("dict")
    depth = lax.axis_size("section")
    here = lax.axis_index("section")
    routes_l = routes[0]
    acts_l = acts[0]
    dec_local = decoder[0]
    enc_local = encoder[0]
    gain_l = gain[0]
    scale_l = inv_rms[0]
    tok_count, listed = routes_l.shape
    attr_keep = jnp.zeros((tok_count, acts_l.shape[1]), jnp.float32)
    grad_keep = jnp.zeros(cotangent.shape, jnp.bfloat16)
    g_new = cotangent
    for turn in range(depth):
        if turn > 0:
            g_now = passed_along(g_new, "section", -1)
        else:
            g_now = cotangent
        active = here == depth - 1 - turn
        attr, g_new = layer_pass(
            g_now, routes_l, acts_l, dec_local, enc_local, gain_l, scale_l, peers
        )
        attr_keep = jnp.where(active, attr, attr_keep)
        grad_keep = jnp.where(active, g_new, grad_keep)
    return (attr_keep[None], grad_keep[None])


def swap_cores(block):
    return lax.ppermute(block, "section", [(0, 1), (1, 0)])


def exchange(parts, sign):
    peers = parts.shape[0]
    moved = [parts[0]]
    for shift in range(1, peers):
        route = [(d, (d + sign * shift) % peers) for d in range(peers)]
        moved.append(lax.ppermute(parts[shift], "dict", route))
    return jnp.stack(moved, axis=0)


def split_layer(g_half, routes_l, acts_l, own, other, is_own, gain_half, scale_l):
    peers = lax.axis_size("dict")
    me = lax.axis_index("dict")
    rows, listed = routes_l.shape
    block = acts_l.shape[1] // listed
    held = own[0].shape[0] // block
    half = g_half.shape[1]
    owner = routes_l // held
    within = routes_l - owner * held
    rel = (owner - me) % peers
    shifts = jnp.arange(peers, dtype=jnp.int32)
    at_rel = (rel[:, :, None] == shifts[None, None, :]).astype(jnp.bfloat16)
    act_grid = acts_l.reshape(rows, listed, block)
    live = (act_grid > 0).astype(jnp.bfloat16) * (1 + within).astype(jnp.bfloat16)[:, :, None]
    placed = jnp.einsum(
        "rks,rkj->srj", at_rel, live, preferred_element_type=jnp.float32
    ).astype(jnp.bfloat16)
    sent = jnp.concatenate(
        [jnp.broadcast_to(g_half[None], (peers, rows, half)), placed], axis=-1
    )
    got = exchange(sent, 1).reshape(peers * rows, half + block)
    g_all = got[:, :half]
    code_all = got[:, half:]

    def with_dec(dec):
        return lax.dot_general(
            g_all, dec, (((1,), (1,)), ((), ())), preferred_element_type=jnp.float32
        )

    part = jnp.where(is_own, with_dec(own[0]), with_dec(other[0]))
    paired = swap_cores(jnp.concatenate([part, code_all.astype(jnp.float32)], axis=1))
    coef = (part + paired[:, :held * block]).astype(jnp.bfloat16)
    code = jnp.where(is_own, code_all.astype(jnp.float32), paired[:, held * block:])
    marks = jnp.concatenate([code == spot + 1 for spot in range(held)], axis=1)
    dz = jnp.where(marks, coef, jnp.zeros_like(coef))

    def with_enc(enc):
        return jnp.dot(dz, enc, preferred_element_type=jnp.float32)

    contrib = jnp.where(is_own, with_enc(own[1]), with_enc(other[1])).astype(jnp.bfloat16)
    dz_pick = dz[:, :block]
    for spot in range(1, held):
        dz_pick = dz_pick + dz[:, spot * block:(spot + 1) * block]
    back = jnp.concatenate([contrib, dz_pick], axis=-1).reshape(peers, rows, half + block)
    returned = exchange(back, -1)
    total = jnp.sum(returned[:, :, :half].astype(jnp.float32), axis=0)
    dz_back = returned[:, :, half:]
    dz_slot = jnp.einsum("rks,srj->rkj", at_rel, dz_back, preferred_element_type=jnp.float32)
    attr = (act_grid.astype(jnp.float32) * dz_slot).reshape(rows, listed * block)
    new_half = (g_half.astype(jnp.float32) + scale_l[:, None] * gain_half[None, :] * total).astype(
        jnp.bfloat16
    )
    return attr, new_half


def owner_layer(g_half, routes_l, acts_l, dec_full, enc_full, layer, gain_half, scale_l):
    peers = lax.axis_size("dict")
    me = lax.axis_index("dict")
    here = lax.axis_index("section")
    rows, listed = routes_l.shape
    block = acts_l.shape[1] // listed
    held = dec_full.shape[0] // block
    half = g_half.shape[1]
    owner = routes_l // held
    within = routes_l - owner * held
    rel = (owner - me) % peers
    shifts = jnp.arange(peers, dtype=jnp.int32)
    at_rel = (rel[:, :, None] == shifts[None, None, :]).astype(jnp.bfloat16)
    act_grid = acts_l.reshape(rows, listed, block)
    live = (act_grid > 0).astype(jnp.bfloat16) * (1 + within).astype(jnp.bfloat16)[:, :, None]
    placed = jnp.einsum(
        "rks,rkj->srj", at_rel, live, preferred_element_type=jnp.float32
    ).astype(jnp.bfloat16)
    sent = jnp.concatenate(
        [jnp.broadcast_to(g_half[None], (peers, rows, half)), placed], axis=-1
    )
    got = exchange(sent, 1).reshape(peers * rows, half + block)
    other = 1 - layer
    lent = lax.ppermute(got[:, :half], "section", [(other, layer)])
    halves = [None, None]
    halves[layer] = got[:, :half]
    halves[other] = lent
    g_all = jnp.concatenate(halves, axis=1)
    code = got[:, half:].astype(jnp.float32)
    coef = lax.dot_general(
        g_all, dec_full, (((1,), (1,)), ((), ())), preferred_element_type=jnp.float32
    ).astype(jnp.bfloat16)
    marks = jnp.concatenate([code == spot + 1 for spot in range(held)], axis=1)
    dz = jnp.where(marks, coef, jnp.zeros_like(coef))
    contrib = jnp.dot(dz, enc_full, preferred_element_type=jnp.float32).astype(jnp.bfloat16)
    dz_pick = dz[:, :block]
    for spot in range(1, held):
        dz_pick = dz_pick + dz[:, spot * block:(spot + 1) * block]
    kept = jnp.concatenate([contrib[:, layer * half:(layer + 1) * half], dz_pick], axis=-1)
    given = jnp.concatenate([contrib[:, other * half:(other + 1) * half], dz_pick], axis=-1)
    given = lax.ppermute(given, "section", [(layer, other)])
    back = jnp.where(here == layer, kept, given).reshape(peers, rows, half + block)
    returned = exchange(back, -1)
    total = jnp.sum(returned[:, :, :half].astype(jnp.float32), axis=0)
    dz_back = returned[:, :, half:]
    dz_slot = jnp.einsum("rks,srj->rkj", at_rel, dz_back, preferred_element_type=jnp.float32)
    attr = (act_grid.astype(jnp.float32) * dz_slot).reshape(rows, listed * block)
    new_half = (g_half.astype(jnp.float32) + scale_l[:, None] * gain_half[None, :] * total).astype(
        jnp.bfloat16
    )
    return attr, new_half


def owner_device(cotangent, routes, acts, decoder, encoder, gain, inv_rms):
    depth = lax.axis_size("section")
    here = lax.axis_index("section")
    rows, width = cotangent.shape
    half = width // depth
    mine = here * half
    small = jnp.concatenate([gain[0], inv_rms[0]], axis=0)
    other_small = swap_cores(small)
    attr_keep = jnp.zeros((rows, acts.shape[2]), jnp.float32)
    grad_keep = jnp.zeros(cotangent.shape, jnp.bfloat16)
    g_half = lax.dynamic_slice_in_dim(cotangent, mine, half, axis=1)
    for layer in reversed(range(depth)):
        is_own = here == layer
        s = jnp.where(is_own, small, other_small)
        gain_half = lax.dynamic_slice_in_dim(s[:width], mine, half, axis=0)
        scale_l = s[width:width + rows]
        attr, g_half = owner_layer(
            g_half, routes[0], acts[0], decoder[0], encoder[0], layer, gain_half, scale_l
        )
        partner = swap_cores(g_half)
        full = jnp.where(
            here == 0,
            jnp.concatenate([g_half, partner], axis=1),
            jnp.concatenate([partner, g_half], axis=1),
        )
        attr_keep = jnp.where(is_own, attr, attr_keep)
        grad_keep = jnp.where(is_own, full, grad_keep)
    return (attr_keep[None], grad_keep[None])


def split_device(cotangent, routes, acts, decoder, encoder, gain, inv_rms):
    depth = lax.axis_size("section")
    here = lax.axis_index("section")
    rows, width = cotangent.shape
    blocks = decoder.shape[1]
    half = width // depth
    mine = here * half
    theirs = (1 - here) * half
    small = jnp.concatenate([gain[0], inv_rms[0]], axis=0)
    other_small = swap_cores(small)
    sent_w = jnp.concatenate(
        [
            lax.dynamic_slice_in_dim(decoder[0], theirs, half, axis=1),
            lax.dynamic_slice_in_dim(encoder[0], theirs, half, axis=1),
        ],
        axis=0,
    )
    other_w = swap_cores(sent_w)
    other = (other_w[:blocks], other_w[blocks:])
    own = (
        lax.dynamic_slice_in_dim(decoder[0], mine, half, axis=1),
        lax.dynamic_slice_in_dim(encoder[0], mine, half, axis=1),
    )
    attr_keep = jnp.zeros((rows, acts.shape[2]), jnp.float32)
    grad_keep = jnp.zeros(cotangent.shape, jnp.bfloat16)
    g_half = lax.dynamic_slice_in_dim(cotangent, mine, half, axis=1)
    for layer in reversed(range(depth)):
        is_own = here == layer
        s = jnp.where(is_own, small, other_small)
        gain_half = lax.dynamic_slice_in_dim(s[:width], mine, half, axis=0)
        scale_l = s[width:width + rows]
        attr, g_half = split_layer(g_half, routes[0], acts[0], own, other, is_own, gain_half, scale_l)
        partner = swap_cores(g_half)
        full = jnp.where(
            here == 0,
            jnp.concatenate([g_half, partner], axis=1),
            jnp.concatenate([partner, g_half], axis=1),
        )
        attr_keep = jnp.where(is_own, attr, attr_keep)
        grad_keep = jnp.where(is_own, full, grad_keep)
    return (attr_keep[None], grad_keep[None])


def per_device(cotangent, routes, acts, decoder, encoder, gain, inv_rms):
    peers = lax.axis_size("dict")
    depth = lax.axis_size("section")
    listed = routes.shape[-1]
    width = cotangent.shape[1]
    if listed == peers and depth == 2 and width % (depth * 128) == 0:
        return owner_device(cotangent, routes, acts, decoder, encoder, gain, inv_rms)
    return slot_device(cotangent, routes, acts, decoder, encoder, gain, inv_rms)


def solution(mesh):
    placed = (
        P(("groups", "dict"), None),
        P("section", ("groups", "dict"), None),
        P("section", ("groups", "dict"), None),
        P("section", "dict", None),
        P("section", "dict", None),
        P("section", None),
        P("section", ("groups", "dict")),
    )
    return jax.shard_map(
        per_device,
        mesh=mesh,
        in_specs=placed,
        out_specs=(P("section", ("groups", "dict"), None), P("section", ("groups", "dict"), None)),
        check_vma=False,
    )
```

```python
import jax
import jax.numpy as jnp
from jax import lax
from jax.sharding import PartitionSpec as P


def passed_along(block, axis, distance):
    devices = range(lax.axis_size(axis))
    route = [(i - distance, i) for i in devices if i - distance in devices]
    return lax.ppermute(block, axis, route)


def owner_work(recv_g, recv_act, dec_local, enc_local):
    width = recv_g.shape[-1]
    columns = dec_local.shape[0]
    flat_g = recv_g.reshape(-1, width)
    flat_act = recv_act.reshape(-1, columns)
    coef = lax.dot_general(
        flat_g, dec_local, (((1,), (1,)), ((), ())), preferred_element_type=jnp.float32
    ).astype(jnp.bfloat16)
    masked = jnp.where(flat_act > 0, coef, jnp.zeros_like(coef))
    contrib = jnp.dot(masked, enc_local, preferred_element_type=jnp.float32).astype(jnp.bfloat16)
    lead = recv_g.shape[:-1]
    return (coef.reshape(lead + (columns,)), contrib.reshape(lead + (width,)))


def layer_pass(g_rows, routes_l, acts_l, dec_local, enc_local, gain_l, scale_l, peers):
    tok_count, listed = routes_l.shape
    block = acts_l.shape[1] // listed
    width = dec_local.shape[1]
    held = dec_local.shape[0] // block
    slots_per = (tok_count * listed + peers - 1) // peers
    total_slots = peers * slots_per
    owner = routes_l // held
    within = routes_l - owner * held
    owners = jnp.arange(peers, dtype=jnp.int32)
    hits = (owner[:, :, None] == owners[None, None, :]).astype(jnp.int32)
    per_row = jnp.sum(hits, axis=1)
    earlier = jnp.cumsum(per_row, axis=0) - per_row
    place = jnp.sum(hits * earlier[:, None, :], axis=2)
    slot_of = (owner * slots_per + place).reshape(-1)
    slot_ids = jnp.arange(total_slots, dtype=jnp.int32)
    pick = (slot_ids[:, None] == slot_of[None, :]).astype(jnp.bfloat16)
    row_pick = jnp.sum(
        pick.reshape(total_slots, tok_count, listed).astype(jnp.float32), axis=2
    ).astype(jnp.bfloat16)
    send_g = jnp.dot(row_pick, g_rows, preferred_element_type=jnp.float32).astype(jnp.bfloat16)
    block_act = jnp.dot(
        pick, acts_l.reshape(tok_count * listed, block), preferred_element_type=jnp.float32
    ).astype(jnp.bfloat16)
    within_hot = (within.reshape(-1)[:, None] == jnp.arange(held, dtype=jnp.int32)[None, :]).astype(
        jnp.bfloat16
    )
    slot_within = jnp.dot(pick, within_hot, preferred_element_type=jnp.float32).astype(jnp.bfloat16)
    send_act = (slot_within[:, :, None] * block_act[:, None, :]).reshape(total_slots, held * block)
    send_g = send_g.reshape(peers, slots_per, width)
    send_act = send_act.reshape(peers, slots_per, held * block)
    recv_g, recv_act = (
        lax.all_to_all(send_g, "dict", split_axis=0, concat_axis=0, tiled=True),
        lax.all_to_all(send_act, "dict", split_axis=0, concat_axis=0, tiled=True),
    )
    coef_here, contrib_here = owner_work(recv_g, recv_act, dec_local, enc_local)
    coef_back, contrib_back = (
        lax.all_to_all(coef_here, "dict", split_axis=0, concat_axis=0, tiled=True),
        lax.all_to_all(contrib_here, "dict", split_axis=0, concat_axis=0, tiled=True),
    )
    coef_back = coef_back.reshape(total_slots, held, block)
    contrib_back = contrib_back.reshape(total_slots, width)
    coef_chosen = jnp.sum(
        slot_within.astype(jnp.float32)[:, :, None] * coef_back.astype(jnp.float32), axis=1
    ).astype(jnp.bfloat16)
    coef_rows = lax.dot_general(
        pick, coef_chosen, (((0,), (0,)), ((), ())), preferred_element_type=jnp.float32
    )
    attr = (acts_l.reshape(tok_count * listed, block).astype(jnp.float32) * coef_rows).reshape(
        tok_count, listed * block
    )
    summed = lax.dot_general(
        row_pick, contrib_back, (((0,), (0,)), ((), ())), preferred_element_type=jnp.float32
    )
    new_g = (g_rows.astype(jnp.float32) + scale_l[:, None] * gain_l[None, :] * summed).astype(
        jnp.bfloat16
    )
    return (attr, new_g)


def slot_device(cotangent, routes, acts, decoder, encoder, gain, inv_rms):
    peers = lax.axis_size("dict")
    depth = lax.axis_size("section")
    here = lax.axis_index("section")
    routes_l = routes[0]
    acts_l = acts[0]
    dec_local = decoder[0]
    enc_local = encoder[0]
    gain_l = gain[0]
    scale_l = inv_rms[0]
    tok_count, listed = routes_l.shape
    attr_keep = jnp.zeros((tok_count, acts_l.shape[1]), jnp.float32)
    grad_keep = jnp.zeros(cotangent.shape, jnp.bfloat16)
    g_new = cotangent
    for turn in range(depth):
        if turn > 0:
            g_now = passed_along(g_new, "section", -1)
        else:
            g_now = cotangent
        active = here == depth - 1 - turn
        attr, g_new = layer_pass(
            g_now, routes_l, acts_l, dec_local, enc_local, gain_l, scale_l, peers
        )
        attr_keep = jnp.where(active, attr, attr_keep)
        grad_keep = jnp.where(active, g_new, grad_keep)
    return (attr_keep[None], grad_keep[None])


def swap_cores(block):
    return lax.ppermute(block, "section", [(0, 1), (1, 0)])


def exchange(parts, sign):
    peers = parts.shape[0]
    moved = [parts[0]]
    for shift in range(1, peers):
        route = [(d, d ^ shift) for d in range(peers)]
        moved.append(lax.ppermute(parts[shift], "dict", route))
    return jnp.stack(moved, axis=0)


def split_layer(g_half, routes_l, acts_l, own, other, is_own, gain_half, scale_l):
    peers = lax.axis_size("dict")
    me = lax.axis_index("dict")
    rows, listed = routes_l.shape
    block = acts_l.shape[1] // listed
    held = own[0].shape[0] // block
    half = g_half.shape[1]
    owner = routes_l // held
    within = routes_l - owner * held
    rel = lax.bitwise_xor(owner, me)
    shifts = jnp.arange(peers, dtype=jnp.int32)
    at_rel = (rel[:, :, None] == shifts[None, None, :]).astype(jnp.bfloat16)
    act_grid = acts_l.reshape(rows, listed, block)
    live = (act_grid > 0).astype(jnp.bfloat16) * (1 + within).astype(jnp.bfloat16)[:, :, None]
    placed = jnp.einsum(
        "rks,rkj->srj", at_rel, live, preferred_element_type=jnp.float32
    ).astype(jnp.bfloat16)
    sent = jnp.concatenate(
        [jnp.broadcast_to(g_half[None], (peers, rows, half)), placed], axis=-1
    )
    got = exchange(sent, 1).reshape(peers * rows, half + block)
    g_all = got[:, :half]
    code_all = got[:, half:]

    def with_dec(dec):
        return lax.dot_general(
            g_all, dec, (((1,), (1,)), ((), ())), preferred_element_type=jnp.float32
        )

    part = jnp.where(is_own, with_dec(own[0]), with_dec(other[0]))
    paired = swap_cores(jnp.concatenate([part, code_all.astype(jnp.float32)], axis=1))
    coef = (part + paired[:, :held * block]).astype(jnp.bfloat16)
    code = jnp.where(is_own, code_all.astype(jnp.float32), paired[:, held * block:])
    marks = jnp.concatenate([code == spot + 1 for spot in range(held)], axis=1)
    dz = jnp.where(marks, coef, jnp.zeros_like(coef))

    def with_enc(enc):
        return jnp.dot(dz, enc, preferred_element_type=jnp.float32)

    contrib = jnp.where(is_own, with_enc(own[1]), with_enc(other[1])).astype(jnp.bfloat16)
    dz_pick = dz[:, :block]
    for spot in range(1, held):
        dz_pick = dz_pick + dz[:, spot * block:(spot + 1) * block]
    back = jnp.concatenate([contrib, dz_pick], axis=-1).reshape(peers, rows, half + block)
    returned = exchange(back, -1)
    total = jnp.sum(returned[:, :, :half].astype(jnp.float32), axis=0)
    dz_back = returned[:, :, half:]
    dz_slot = jnp.einsum("rks,srj->rkj", at_rel, dz_back, preferred_element_type=jnp.float32)
    attr = (act_grid.astype(jnp.float32) * dz_slot).reshape(rows, listed * block)
    new_half = (g_half.astype(jnp.float32) + scale_l[:, None] * gain_half[None, :] * total).astype(
        jnp.bfloat16
    )
    return attr, new_half


def split_device(cotangent, routes, acts, decoder, encoder, gain, inv_rms):
    depth = lax.axis_size("section")
    here = lax.axis_index("section")
    rows, width = cotangent.shape
    blocks = decoder.shape[1]
    half = width // depth
    mine = here * half
    theirs = (1 - here) * half
    small = jnp.concatenate([gain[0], inv_rms[0]], axis=0)
    other_small = swap_cores(small)
    sent_w = jnp.concatenate(
        [
            lax.dynamic_slice_in_dim(decoder[0], theirs, half, axis=1),
            lax.dynamic_slice_in_dim(encoder[0], theirs, half, axis=1),
        ],
        axis=0,
    )
    other_w = swap_cores(sent_w)
    other = (other_w[:blocks], other_w[blocks:])
    own = (
        lax.dynamic_slice_in_dim(decoder[0], mine, half, axis=1),
        lax.dynamic_slice_in_dim(encoder[0], mine, half, axis=1),
    )
    attr_keep = jnp.zeros((rows, acts.shape[2]), jnp.float32)
    grad_keep = jnp.zeros(cotangent.shape, jnp.bfloat16)
    g_half = lax.dynamic_slice_in_dim(cotangent, mine, half, axis=1)
    for layer in reversed(range(depth)):
        is_own = here == layer
        s = jnp.where(is_own, small, other_small)
        gain_half = lax.dynamic_slice_in_dim(s[:width], mine, half, axis=0)
        scale_l = s[width:width + rows]
        attr, g_half = split_layer(g_half, routes[0], acts[0], own, other, is_own, gain_half, scale_l)
        partner = swap_cores(g_half)
        full = jnp.where(
            here == 0,
            jnp.concatenate([g_half, partner], axis=1),
            jnp.concatenate([partner, g_half], axis=1),
        )
        attr_keep = jnp.where(is_own, attr, attr_keep)
        grad_keep = jnp.where(is_own, full, grad_keep)
    return (attr_keep[None], grad_keep[None])


def per_device(cotangent, routes, acts, decoder, encoder, gain, inv_rms):
    peers = lax.axis_size("dict")
    depth = lax.axis_size("section")
    listed = routes.shape[-1]
    width = cotangent.shape[1]
    if listed == peers and peers & (peers - 1) == 0 and depth == 2 and width % (depth * 128) == 0:
        return split_device(cotangent, routes, acts, decoder, encoder, gain, inv_rms)
    return slot_device(cotangent, routes, acts, decoder, encoder, gain, inv_rms)


def solution(mesh):
    placed = (
        P(("groups", "dict"), None),
        P("section", ("groups", "dict"), None),
        P("section", ("groups", "dict"), None),
        P("section", "dict", None),
        P("section", "dict", None),
        P("section", None),
        P("section", ("groups", "dict")),
    )
    return jax.shard_map(
        per_device,
        mesh=mesh,
        in_specs=placed,
        out_specs=(P("section", ("groups", "dict"), None), P("section", ("groups", "dict"), None)),
        check_vma=False,
    )
```

```python
import jax
import jax.numpy as jnp
from jax import lax
from jax.sharding import PartitionSpec as P


def passed_along(block, axis, distance):
    devices = range(lax.axis_size(axis))
    route = [(i - distance, i) for i in devices if i - distance in devices]
    return lax.ppermute(block, axis, route)


def owner_work(recv_g, recv_act, dec_local, enc_local):
    width = recv_g.shape[-1]
    columns = dec_local.shape[0]
    flat_g = recv_g.reshape(-1, width)
    flat_act = recv_act.reshape(-1, columns)
    coef = lax.dot_general(
        flat_g, dec_local, (((1,), (1,)), ((), ())), preferred_element_type=jnp.float32
    ).astype(jnp.bfloat16)
    masked = jnp.where(flat_act > 0, coef, jnp.zeros_like(coef))
    contrib = jnp.dot(masked, enc_local, preferred_element_type=jnp.float32).astype(jnp.bfloat16)
    lead = recv_g.shape[:-1]
    return (coef.reshape(lead + (columns,)), contrib.reshape(lead + (width,)))


def layer_pass(g_rows, routes_l, acts_l, dec_local, enc_local, gain_l, scale_l, peers):
    tok_count, listed = routes_l.shape
    block = acts_l.shape[1] // listed
    width = dec_local.shape[1]
    held = dec_local.shape[0] // block
    slots_per = (tok_count * listed + peers - 1) // peers
    total_slots = peers * slots_per
    owner = routes_l // held
    within = routes_l - owner * held
    owners = jnp.arange(peers, dtype=jnp.int32)
    hits = (owner[:, :, None] == owners[None, None, :]).astype(jnp.int32)
    per_row = jnp.sum(hits, axis=1)
    earlier = jnp.cumsum(per_row, axis=0) - per_row
    place = jnp.sum(hits * earlier[:, None, :], axis=2)
    slot_of = (owner * slots_per + place).reshape(-1)
    slot_ids = jnp.arange(total_slots, dtype=jnp.int32)
    pick = (slot_ids[:, None] == slot_of[None, :]).astype(jnp.bfloat16)
    row_pick = jnp.sum(
        pick.reshape(total_slots, tok_count, listed).astype(jnp.float32), axis=2
    ).astype(jnp.bfloat16)
    send_g = jnp.dot(row_pick, g_rows, preferred_element_type=jnp.float32).astype(jnp.bfloat16)
    block_act = jnp.dot(
        pick, acts_l.reshape(tok_count * listed, block), preferred_element_type=jnp.float32
    ).astype(jnp.bfloat16)
    within_hot = (within.reshape(-1)[:, None] == jnp.arange(held, dtype=jnp.int32)[None, :]).astype(
        jnp.bfloat16
    )
    slot_within = jnp.dot(pick, within_hot, preferred_element_type=jnp.float32).astype(jnp.bfloat16)
    send_act = (slot_within[:, :, None] * block_act[:, None, :]).reshape(total_slots, held * block)
    send_g = send_g.reshape(peers, slots_per, width)
    send_act = send_act.reshape(peers, slots_per, held * block)
    recv_g, recv_act = (
        lax.all_to_all(send_g, "dict", split_axis=0, concat_axis=0, tiled=True),
        lax.all_to_all(send_act, "dict", split_axis=0, concat_axis=0, tiled=True),
    )
    coef_here, contrib_here = owner_work(recv_g, recv_act, dec_local, enc_local)
    coef_back, contrib_back = (
        lax.all_to_all(coef_here, "dict", split_axis=0, concat_axis=0, tiled=True),
        lax.all_to_all(contrib_here, "dict", split_axis=0, concat_axis=0, tiled=True),
    )
    coef_back = coef_back.reshape(total_slots, held, block)
    contrib_back = contrib_back.reshape(total_slots, width)
    coef_chosen = jnp.sum(
        slot_within.astype(jnp.float32)[:, :, None] * coef_back.astype(jnp.float32), axis=1
    ).astype(jnp.bfloat16)
    coef_rows = lax.dot_general(
        pick, coef_chosen, (((0,), (0,)), ((), ())), preferred_element_type=jnp.float32
    )
    attr = (acts_l.reshape(tok_count * listed, block).astype(jnp.float32) * coef_rows).reshape(
        tok_count, listed * block
    )
    summed = lax.dot_general(
        row_pick, contrib_back, (((0,), (0,)), ((), ())), preferred_element_type=jnp.float32
    )
    new_g = (g_rows.astype(jnp.float32) + scale_l[:, None] * gain_l[None, :] * summed).astype(
        jnp.bfloat16
    )
    return (attr, new_g)


def slot_device(cotangent, routes, acts, decoder, encoder, gain, inv_rms):
    peers = lax.axis_size("dict")
    depth = lax.axis_size("section")
    here = lax.axis_index("section")
    routes_l = routes[0]
    acts_l = acts[0]
    dec_local = decoder[0]
    enc_local = encoder[0]
    gain_l = gain[0]
    scale_l = inv_rms[0]
    tok_count, listed = routes_l.shape
    attr_keep = jnp.zeros((tok_count, acts_l.shape[1]), jnp.float32)
    grad_keep = jnp.zeros(cotangent.shape, jnp.bfloat16)
    g_new = cotangent
    for turn in range(depth):
        if turn > 0:
            g_now = passed_along(g_new, "section", -1)
        else:
            g_now = cotangent
        active = here == depth - 1 - turn
        attr, g_new = layer_pass(
            g_now, routes_l, acts_l, dec_local, enc_local, gain_l, scale_l, peers
        )
        attr_keep = jnp.where(active, attr, attr_keep)
        grad_keep = jnp.where(active, g_new, grad_keep)
    return (attr_keep[None], grad_keep[None])


def swap_cores(block):
    return lax.ppermute(block, "section", [(0, 1), (1, 0)])


def exchange(parts, sign):
    peers = parts.shape[0]
    moved = [parts[0]]
    for shift in range(1, peers):
        route = [(d, (d + sign * shift) % peers) for d in range(peers)]
        moved.append(lax.ppermute(parts[shift], "dict", route))
    return jnp.stack(moved, axis=0)


def split_layer(g_half, routes_l, acts_l, own, other, is_own, gain_half, scale_l):
    peers = lax.axis_size("dict")
    me = lax.axis_index("dict")
    rows, listed = routes_l.shape
    block = acts_l.shape[1] // listed
    held = own[0].shape[0] // block
    half = g_half.shape[1]
    owner = routes_l // held
    within = routes_l - owner * held
    rel = (owner - me) % peers
    shifts = jnp.arange(peers, dtype=jnp.int32)
    at_rel = (rel[:, :, None] == shifts[None, None, :]).astype(jnp.bfloat16)
    act_grid = acts_l.reshape(rows, listed, block)
    live = (act_grid > 0).astype(jnp.bfloat16) * (1 + within).astype(jnp.bfloat16)[:, :, None]
    placed = jnp.einsum(
        "rks,rkj->srj", at_rel, live, preferred_element_type=jnp.float32
    ).astype(jnp.bfloat16)
    sent = jnp.concatenate(
        [jnp.broadcast_to(g_half[None], (peers, rows, half)), placed], axis=-1
    )
    got = exchange(sent, 1).reshape(peers * rows, half + block)
    g_all = got[:, :half]
    code_all = got[:, half:]

    def with_dec(dec):
        return lax.dot_general(
            g_all, dec, (((1,), (1,)), ((), ())), preferred_element_type=jnp.float32
        )

    part = lax.cond(is_own, lambda: with_dec(own[0]), lambda: with_dec(other[0]))
    paired = swap_cores(jnp.concatenate([part, code_all.astype(jnp.float32)], axis=1))
    coef = (part + paired[:, :held * block]).astype(jnp.bfloat16)
    code = jnp.where(is_own, code_all.astype(jnp.float32), paired[:, held * block:])
    marks = jnp.concatenate([code == spot + 1 for spot in range(held)], axis=1)
    dz = jnp.where(marks, coef, jnp.zeros_like(coef))

    def with_enc(enc):
        return jnp.dot(dz, enc, preferred_element_type=jnp.float32)

    contrib = lax.cond(is_own, lambda: with_enc(own[1]), lambda: with_enc(other[1])).astype(
        jnp.bfloat16
    )
    dz_pick = dz[:, :block]
    for spot in range(1, held):
        dz_pick = dz_pick + dz[:, spot * block:(spot + 1) * block]
    back = jnp.concatenate([contrib, dz_pick], axis=-1).reshape(peers, rows, half + block)
    returned = exchange(back, -1)
    total = jnp.sum(returned[:, :, :half].astype(jnp.float32), axis=0)
    dz_back = returned[:, :, half:]
    dz_slot = jnp.einsum("rks,srj->rkj", at_rel, dz_back, preferred_element_type=jnp.float32)
    attr = (act_grid.astype(jnp.float32) * dz_slot).reshape(rows, listed * block)
    new_half = (g_half.astype(jnp.float32) + scale_l[:, None] * gain_half[None, :] * total).astype(
        jnp.bfloat16
    )
    return attr, new_half


def split_device(cotangent, routes, acts, decoder, encoder, gain, inv_rms):
    depth = lax.axis_size("section")
    here = lax.axis_index("section")
    rows, width = cotangent.shape
    blocks = decoder.shape[1]
    half = width // depth
    mine = here * half
    theirs = (1 - here) * half
    small = jnp.concatenate([gain[0], inv_rms[0]], axis=0)
    other_small = swap_cores(small)
    sent_w = jnp.concatenate(
        [
            lax.dynamic_slice_in_dim(decoder[0], theirs, half, axis=1),
            lax.dynamic_slice_in_dim(encoder[0], theirs, half, axis=1),
        ],
        axis=0,
    )
    other_w = swap_cores(sent_w)
    other = (other_w[:blocks], other_w[blocks:])
    own = (
        lax.dynamic_slice_in_dim(decoder[0], mine, half, axis=1),
        lax.dynamic_slice_in_dim(encoder[0], mine, half, axis=1),
    )
    attr_keep = jnp.zeros((rows, acts.shape[2]), jnp.float32)
    grad_keep = jnp.zeros(cotangent.shape, jnp.bfloat16)
    g_half = lax.dynamic_slice_in_dim(cotangent, mine, half, axis=1)
    for layer in reversed(range(depth)):
        is_own = here == layer
        s = jnp.where(is_own, small, other_small)
        gain_half = lax.dynamic_slice_in_dim(s[:width], mine, half, axis=0)
        scale_l = s[width:width + rows]
        attr, g_half = split_layer(g_half, routes[0], acts[0], own, other, is_own, gain_half, scale_l)
        partner = swap_cores(g_half)
        full = jnp.where(
            here == 0,
            jnp.concatenate([g_half, partner], axis=1),
            jnp.concatenate([partner, g_half], axis=1),
        )
        attr_keep = jnp.where(is_own, attr, attr_keep)
        grad_keep = jnp.where(is_own, full, grad_keep)
    return (attr_keep[None], grad_keep[None])


def per_device(cotangent, routes, acts, decoder, encoder, gain, inv_rms):
    peers = lax.axis_size("dict")
    depth = lax.axis_size("section")
    listed = routes.shape[-1]
    width = cotangent.shape[1]
    if listed == peers and depth == 2 and width % (depth * 128) == 0:
        return split_device(cotangent, routes, acts, decoder, encoder, gain, inv_rms)
    return slot_device(cotangent, routes, acts, decoder, encoder, gain, inv_rms)


def solution(mesh):
    placed = (
        P(("groups", "dict"), None),
        P("section", ("groups", "dict"), None),
        P("section", ("groups", "dict"), None),
        P("section", "dict", None),
        P("section", "dict", None),
        P("section", None),
        P("section", ("groups", "dict")),
    )
    return jax.shard_map(
        per_device,
        mesh=mesh,
        in_specs=placed,
        out_specs=(P("section", ("groups", "dict"), None), P("section", ("groups", "dict"), None)),
        check_vma=False,
    )
```

```python
import jax
import jax.numpy as jnp
from jax import lax
from jax.sharding import PartitionSpec as P


def passed_along(block, axis, distance):
    devices = range(lax.axis_size(axis))
    route = [(i - distance, i) for i in devices if i - distance in devices]
    return lax.ppermute(block, axis, route)


def owner_work(recv_g, recv_act, dec_local, enc_local):
    width = recv_g.shape[-1]
    columns = dec_local.shape[0]
    flat_g = recv_g.reshape(-1, width)
    flat_act = recv_act.reshape(-1, columns)
    coef = lax.dot_general(
        flat_g, dec_local, (((1,), (1,)), ((), ())), preferred_element_type=jnp.float32
    ).astype(jnp.bfloat16)
    masked = jnp.where(flat_act > 0, coef, jnp.zeros_like(coef))
    contrib = jnp.dot(masked, enc_local, preferred_element_type=jnp.float32).astype(jnp.bfloat16)
    lead = recv_g.shape[:-1]
    return (coef.reshape(lead + (columns,)), contrib.reshape(lead + (width,)))


def layer_pass(g_rows, routes_l, acts_l, dec_local, enc_local, gain_l, scale_l, peers):
    tok_count, listed = routes_l.shape
    block = acts_l.shape[1] // listed
    width = dec_local.shape[1]
    held = dec_local.shape[0] // block
    slots_per = (tok_count * listed + peers - 1) // peers
    total_slots = peers * slots_per
    owner = routes_l // held
    within = routes_l - owner * held
    owners = jnp.arange(peers, dtype=jnp.int32)
    hits = (owner[:, :, None] == owners[None, None, :]).astype(jnp.int32)
    per_row = jnp.sum(hits, axis=1)
    earlier = jnp.cumsum(per_row, axis=0) - per_row
    place = jnp.sum(hits * earlier[:, None, :], axis=2)
    slot_of = (owner * slots_per + place).reshape(-1)
    slot_ids = jnp.arange(total_slots, dtype=jnp.int32)
    pick = (slot_ids[:, None] == slot_of[None, :]).astype(jnp.bfloat16)
    row_pick = jnp.sum(
        pick.reshape(total_slots, tok_count, listed).astype(jnp.float32), axis=2
    ).astype(jnp.bfloat16)
    send_g = jnp.dot(row_pick, g_rows, preferred_element_type=jnp.float32).astype(jnp.bfloat16)
    block_act = jnp.dot(
        pick, acts_l.reshape(tok_count * listed, block), preferred_element_type=jnp.float32
    ).astype(jnp.bfloat16)
    within_hot = (within.reshape(-1)[:, None] == jnp.arange(held, dtype=jnp.int32)[None, :]).astype(
        jnp.bfloat16
    )
    slot_within = jnp.dot(pick, within_hot, preferred_element_type=jnp.float32).astype(jnp.bfloat16)
    send_act = (slot_within[:, :, None] * block_act[:, None, :]).reshape(total_slots, held * block)
    send_g = send_g.reshape(peers, slots_per, width)
    send_act = send_act.reshape(peers, slots_per, held * block)
    recv_g, recv_act = (
        lax.all_to_all(send_g, "dict", split_axis=0, concat_axis=0, tiled=True),
        lax.all_to_all(send_act, "dict", split_axis=0, concat_axis=0, tiled=True),
    )
    coef_here, contrib_here = owner_work(recv_g, recv_act, dec_local, enc_local)
    coef_back, contrib_back = (
        lax.all_to_all(coef_here, "dict", split_axis=0, concat_axis=0, tiled=True),
        lax.all_to_all(contrib_here, "dict", split_axis=0, concat_axis=0, tiled=True),
    )
    coef_back = coef_back.reshape(total_slots, held, block)
    contrib_back = contrib_back.reshape(total_slots, width)
    coef_chosen = jnp.sum(
        slot_within.astype(jnp.float32)[:, :, None] * coef_back.astype(jnp.float32), axis=1
    ).astype(jnp.bfloat16)
    coef_rows = lax.dot_general(
        pick, coef_chosen, (((0,), (0,)), ((), ())), preferred_element_type=jnp.float32
    )
    attr = (acts_l.reshape(tok_count * listed, block).astype(jnp.float32) * coef_rows).reshape(
        tok_count, listed * block
    )
    summed = lax.dot_general(
        row_pick, contrib_back, (((0,), (0,)), ((), ())), preferred_element_type=jnp.float32
    )
    new_g = (g_rows.astype(jnp.float32) + scale_l[:, None] * gain_l[None, :] * summed).astype(
        jnp.bfloat16
    )
    return (attr, new_g)


def slot_device(cotangent, routes, acts, decoder, encoder, gain, inv_rms):
    peers = lax.axis_size("dict")
    depth = lax.axis_size("section")
    here = lax.axis_index("section")
    routes_l = routes[0]
    acts_l = acts[0]
    dec_local = decoder[0]
    enc_local = encoder[0]
    gain_l = gain[0]
    scale_l = inv_rms[0]
    tok_count, listed = routes_l.shape
    attr_keep = jnp.zeros((tok_count, acts_l.shape[1]), jnp.float32)
    grad_keep = jnp.zeros(cotangent.shape, jnp.bfloat16)
    g_new = cotangent
    for turn in range(depth):
        if turn > 0:
            g_now = passed_along(g_new, "section", -1)
        else:
            g_now = cotangent
        active = here == depth - 1 - turn
        attr, g_new = layer_pass(
            g_now, routes_l, acts_l, dec_local, enc_local, gain_l, scale_l, peers
        )
        attr_keep = jnp.where(active, attr, attr_keep)
        grad_keep = jnp.where(active, g_new, grad_keep)
    return (attr_keep[None], grad_keep[None])


def swap_cores(block):
    return lax.ppermute(block, "section", [(0, 1), (1, 0)])


def exchange(parts, sign):
    peers = parts.shape[0]
    moved = [parts[0]]
    for shift in range(1, peers):
        route = [(d, (d + sign * shift) % peers) for d in range(peers)]
        moved.append(lax.ppermute(parts[shift], "dict", route))
    return jnp.stack(moved, axis=0)


def split_layer(g_half, routes_l, acts_l, own, other, is_own, gain_half, scale_l):
    peers = lax.axis_size("dict")
    me = lax.axis_index("dict")
    rows, listed = routes_l.shape
    block = acts_l.shape[1] // listed
    held = own[0].shape[0] // block
    half = g_half.shape[1]
    owner = routes_l // held
    within = routes_l - owner * held
    rel = (owner - me) % peers
    shifts = jnp.arange(peers, dtype=jnp.int32)
    at_rel = (rel[:, :, None] == shifts[None, None, :]).astype(jnp.bfloat16)
    act_grid = acts_l.reshape(rows, listed, block)
    live = (act_grid > 0).astype(jnp.bfloat16) * (1 + within).astype(jnp.bfloat16)[:, :, None]
    placed = jnp.einsum(
        "rks,rkj->srj", at_rel, live, preferred_element_type=jnp.float32
    ).astype(jnp.bfloat16)
    sent = jnp.concatenate(
        [jnp.broadcast_to(g_half[None], (peers, rows, half)), placed], axis=-1
    )
    got = exchange(sent, 1).reshape(peers * rows, half + block)
    g_all = got[:, :half]
    code_all = got[:, half:]

    def with_dec(dec):
        return lax.dot_general(
            g_all, dec, (((1,), (1,)), ((), ())), preferred_element_type=jnp.float32
        )

    part = jnp.where(is_own, with_dec(own[0]), with_dec(other[0]))
    paired = swap_cores(jnp.concatenate([part, code_all.astype(jnp.float32)], axis=1))
    coef = (part + paired[:, :held * block]).astype(jnp.bfloat16)
    code = jnp.where(is_own, code_all.astype(jnp.float32), paired[:, held * block:])
    marks = jnp.concatenate([code == spot + 1 for spot in range(held)], axis=1)
    dz = jnp.where(marks, coef, jnp.zeros_like(coef))

    def with_enc(enc):
        return jnp.dot(dz, enc, preferred_element_type=jnp.float32)

    contrib = jnp.where(is_own, with_enc(own[1]), with_enc(other[1])).astype(jnp.bfloat16)
    dz_pick = dz[:, :block]
    for spot in range(1, held):
        dz_pick = dz_pick + dz[:, spot * block:(spot + 1) * block]
    back = jnp.concatenate([contrib, dz_pick], axis=-1).reshape(peers, rows, half + block)
    returned = exchange(back, -1)
    total = jnp.sum(returned[:, :, :half].astype(jnp.float32), axis=0)
    dz_back = returned[:, :, half:]
    dz_slot = jnp.einsum("rks,srj->rkj", at_rel, dz_back, preferred_element_type=jnp.float32)
    attr = (act_grid.astype(jnp.float32) * dz_slot).reshape(rows, listed * block)
    new_half = (g_half.astype(jnp.float32) + scale_l[:, None] * gain_half[None, :] * total).astype(
        jnp.bfloat16
    )
    return attr, new_half


def split_device(cotangent, routes, acts, decoder, encoder, gain, inv_rms):
    depth = lax.axis_size("section")
    here = lax.axis_index("section")
    rows, width = cotangent.shape
    blocks = decoder.shape[1]
    half = width // depth
    mine = here * half
    theirs = (1 - here) * half
    small = jnp.concatenate([gain[0], inv_rms[0]], axis=0)
    other_small = swap_cores(small)
    other = (
        swap_cores(lax.dynamic_slice_in_dim(decoder[0], theirs, half, axis=1)),
        swap_cores(lax.dynamic_slice_in_dim(encoder[0], theirs, half, axis=1)),
    )
    own = (
        lax.dynamic_slice_in_dim(decoder[0], mine, half, axis=1),
        lax.dynamic_slice_in_dim(encoder[0], mine, half, axis=1),
    )
    attr_keep = jnp.zeros((rows, acts.shape[2]), jnp.float32)
    grad_keep = jnp.zeros(cotangent.shape, jnp.bfloat16)
    g_half = lax.dynamic_slice_in_dim(cotangent, mine, half, axis=1)
    for layer in reversed(range(depth)):
        is_own = here == layer
        s = jnp.where(is_own, small, other_small)
        gain_half = lax.dynamic_slice_in_dim(s[:width], mine, half, axis=0)
        scale_l = s[width:width + rows]
        attr, g_half = split_layer(g_half, routes[0], acts[0], own, other, is_own, gain_half, scale_l)
        partner = swap_cores(g_half)
        full = jnp.where(
            here == 0,
            jnp.concatenate([g_half, partner], axis=1),
            jnp.concatenate([partner, g_half], axis=1),
        )
        attr_keep = jnp.where(is_own, attr, attr_keep)
        grad_keep = jnp.where(is_own, full, grad_keep)
    return (attr_keep[None], grad_keep[None])


def per_device(cotangent, routes, acts, decoder, encoder, gain, inv_rms):
    peers = lax.axis_size("dict")
    depth = lax.axis_size("section")
    listed = routes.shape[-1]
    width = cotangent.shape[1]
    if listed == peers and depth == 2 and width % (depth * 128) == 0:
        return split_device(cotangent, routes, acts, decoder, encoder, gain, inv_rms)
    return slot_device(cotangent, routes, acts, decoder, encoder, gain, inv_rms)


def solution(mesh):
    placed = (
        P(("groups", "dict"), None),
        P("section", ("groups", "dict"), None),
        P("section", ("groups", "dict"), None),
        P("section", "dict", None),
        P("section", "dict", None),
        P("section", None),
        P("section", ("groups", "dict")),
    )
    return jax.shard_map(
        per_device,
        mesh=mesh,
        in_specs=placed,
        out_specs=(P("section", ("groups", "dict"), None), P("section", ("groups", "dict"), None)),
        check_vma=False,
    )
```

```python
import jax
import jax.numpy as jnp
from jax import lax
from jax.sharding import PartitionSpec as P


def passed_along(block, axis, distance):
    devices = range(lax.axis_size(axis))
    route = [(i - distance, i) for i in devices if i - distance in devices]
    return lax.ppermute(block, axis, route)


def owner_work(recv_g, recv_act, dec_local, enc_local):
    width = recv_g.shape[-1]
    columns = dec_local.shape[0]
    flat_g = recv_g.reshape(-1, width)
    flat_act = recv_act.reshape(-1, columns)
    coef = lax.dot_general(
        flat_g, dec_local, (((1,), (1,)), ((), ())), preferred_element_type=jnp.float32
    ).astype(jnp.bfloat16)
    masked = jnp.where(flat_act > 0, coef, jnp.zeros_like(coef))
    contrib = jnp.dot(masked, enc_local, preferred_element_type=jnp.float32).astype(jnp.bfloat16)
    lead = recv_g.shape[:-1]
    return (coef.reshape(lead + (columns,)), contrib.reshape(lead + (width,)))


def layer_pass(g_rows, routes_l, acts_l, dec_local, enc_local, gain_l, scale_l, peers):
    tok_count, listed = routes_l.shape
    block = acts_l.shape[1] // listed
    width = dec_local.shape[1]
    held = dec_local.shape[0] // block
    slots_per = (tok_count * listed + peers - 1) // peers
    total_slots = peers * slots_per
    owner = routes_l // held
    within = routes_l - owner * held
    owners = jnp.arange(peers, dtype=jnp.int32)
    hits = (owner[:, :, None] == owners[None, None, :]).astype(jnp.int32)
    per_row = jnp.sum(hits, axis=1)
    earlier = jnp.cumsum(per_row, axis=0) - per_row
    place = jnp.sum(hits * earlier[:, None, :], axis=2)
    slot_of = (owner * slots_per + place).reshape(-1)
    slot_ids = jnp.arange(total_slots, dtype=jnp.int32)
    pick = (slot_ids[:, None] == slot_of[None, :]).astype(jnp.bfloat16)
    row_pick = jnp.sum(
        pick.reshape(total_slots, tok_count, listed).astype(jnp.float32), axis=2
    ).astype(jnp.bfloat16)
    send_g = jnp.dot(row_pick, g_rows, preferred_element_type=jnp.float32).astype(jnp.bfloat16)
    block_act = jnp.dot(
        pick, acts_l.reshape(tok_count * listed, block), preferred_element_type=jnp.float32
    ).astype(jnp.bfloat16)
    within_hot = (within.reshape(-1)[:, None] == jnp.arange(held, dtype=jnp.int32)[None, :]).astype(
        jnp.bfloat16
    )
    slot_within = jnp.dot(pick, within_hot, preferred_element_type=jnp.float32).astype(jnp.bfloat16)
    send_act = (slot_within[:, :, None] * block_act[:, None, :]).reshape(total_slots, held * block)
    send_g = send_g.reshape(peers, slots_per, width)
    send_act = send_act.reshape(peers, slots_per, held * block)
    recv_g, recv_act = (
        lax.all_to_all(send_g, "dict", split_axis=0, concat_axis=0, tiled=True),
        lax.all_to_all(send_act, "dict", split_axis=0, concat_axis=0, tiled=True),
    )
    coef_here, contrib_here = owner_work(recv_g, recv_act, dec_local, enc_local)
    coef_back, contrib_back = (
        lax.all_to_all(coef_here, "dict", split_axis=0, concat_axis=0, tiled=True),
        lax.all_to_all(contrib_here, "dict", split_axis=0, concat_axis=0, tiled=True),
    )
    coef_back = coef_back.reshape(total_slots, held, block)
    contrib_back = contrib_back.reshape(total_slots, width)
    coef_chosen = jnp.sum(
        slot_within.astype(jnp.float32)[:, :, None] * coef_back.astype(jnp.float32), axis=1
    ).astype(jnp.bfloat16)
    coef_rows = lax.dot_general(
        pick, coef_chosen, (((0,), (0,)), ((), ())), preferred_element_type=jnp.float32
    )
    attr = (acts_l.reshape(tok_count * listed, block).astype(jnp.float32) * coef_rows).reshape(
        tok_count, listed * block
    )
    summed = lax.dot_general(
        row_pick, contrib_back, (((0,), (0,)), ((), ())), preferred_element_type=jnp.float32
    )
    new_g = (g_rows.astype(jnp.float32) + scale_l[:, None] * gain_l[None, :] * summed).astype(
        jnp.bfloat16
    )
    return (attr, new_g)


def slot_device(cotangent, routes, acts, decoder, encoder, gain, inv_rms):
    peers = lax.axis_size("dict")
    depth = lax.axis_size("section")
    here = lax.axis_index("section")
    routes_l = routes[0]
    acts_l = acts[0]
    dec_local = decoder[0]
    enc_local = encoder[0]
    gain_l = gain[0]
    scale_l = inv_rms[0]
    tok_count, listed = routes_l.shape
    attr_keep = jnp.zeros((tok_count, acts_l.shape[1]), jnp.float32)
    grad_keep = jnp.zeros(cotangent.shape, jnp.bfloat16)
    g_new = cotangent
    for turn in range(depth):
        if turn > 0:
            g_now = passed_along(g_new, "section", -1)
        else:
            g_now = cotangent
        active = here == depth - 1 - turn
        attr, g_new = layer_pass(
            g_now, routes_l, acts_l, dec_local, enc_local, gain_l, scale_l, peers
        )
        attr_keep = jnp.where(active, attr, attr_keep)
        grad_keep = jnp.where(active, g_new, grad_keep)
    return (attr_keep[None], grad_keep[None])


def swap_cores(block):
    return lax.ppermute(block, "section", [(0, 1), (1, 0)])


def exchange(parts, sign):
    peers = parts.shape[0]
    moved = [parts[0]]
    for shift in range(1, peers):
        route = [(d, (d + sign * shift) % peers) for d in range(peers)]
        moved.append(lax.ppermute(parts[shift], "dict", route))
    return jnp.stack(moved, axis=0)


def split_layer(g_half, routes_l, acts_l, own, other, is_own, small, other_small):
    peers = lax.axis_size("dict")
    me = lax.axis_index("dict")
    rows, listed = routes_l.shape
    block = acts_l.shape[1] // listed
    held = own[0].shape[0] // block
    half = g_half.shape[1]
    owner = routes_l // held
    within = routes_l - owner * held
    rel = (owner - me) % peers
    shifts = jnp.arange(peers, dtype=jnp.int32)
    at_rel = (rel[:, :, None] == shifts[None, None, :]).astype(jnp.bfloat16)
    act_grid = acts_l.reshape(rows, listed, block)
    live = (act_grid > 0).astype(jnp.bfloat16) * (1 + within).astype(jnp.bfloat16)[:, :, None]
    placed = jnp.einsum(
        "rks,rkj->srj", at_rel, live, preferred_element_type=jnp.float32
    ).astype(jnp.bfloat16)
    sent = jnp.concatenate(
        [jnp.broadcast_to(g_half[None], (peers, rows, half)), placed], axis=-1
    )
    got = exchange(sent, 1).reshape(peers * rows, half + block)
    if other_small is None:
        small, got = lax.optimization_barrier((small, got))
        other_small = swap_cores(small)
    g_all = got[:, :half]
    code_all = got[:, half:]

    def with_dec(dec):
        return lax.dot_general(
            g_all, dec, (((1,), (1,)), ((), ())), preferred_element_type=jnp.float32
        )

    part = jnp.where(is_own, with_dec(own[0]), with_dec(other[0]))
    paired = swap_cores(jnp.concatenate([part, code_all.astype(jnp.float32)], axis=1))
    coef = (part + paired[:, :held * block]).astype(jnp.bfloat16)
    code = jnp.where(is_own, code_all.astype(jnp.float32), paired[:, held * block:])
    marks = jnp.concatenate([code == spot + 1 for spot in range(held)], axis=1)
    dz = jnp.where(marks, coef, jnp.zeros_like(coef))

    def with_enc(enc):
        return jnp.dot(dz, enc, preferred_element_type=jnp.float32)

    contrib = jnp.where(is_own, with_enc(own[1]), with_enc(other[1])).astype(jnp.bfloat16)
    dz_pick = dz[:, :block]
    for spot in range(1, held):
        dz_pick = dz_pick + dz[:, spot * block:(spot + 1) * block]
    back = jnp.concatenate([contrib, dz_pick], axis=-1).reshape(peers, rows, half + block)
    returned = exchange(back, -1)
    total = jnp.sum(returned[:, :, :half].astype(jnp.float32), axis=0)
    dz_back = returned[:, :, half:]
    dz_slot = jnp.einsum("rks,srj->rkj", at_rel, dz_back, preferred_element_type=jnp.float32)
    attr = (act_grid.astype(jnp.float32) * dz_slot).reshape(rows, listed * block)
    width = half * lax.axis_size("section")
    s = jnp.where(is_own, small, other_small)
    gain_half = lax.dynamic_slice_in_dim(s[:width], lax.axis_index("section") * half, half, axis=0)
    scale_l = s[width:width + rows]
    new_half = (g_half.astype(jnp.float32) + scale_l[:, None] * gain_half[None, :] * total).astype(
        jnp.bfloat16
    )
    return attr, new_half, other_small


def split_device(cotangent, routes, acts, decoder, encoder, gain, inv_rms):
    depth = lax.axis_size("section")
    here = lax.axis_index("section")
    rows, width = cotangent.shape
    blocks = decoder.shape[1]
    half = width // depth
    mine = here * half
    theirs = (1 - here) * half
    small = jnp.concatenate([gain[0], inv_rms[0]], axis=0)
    other_small = None
    sent_w = jnp.concatenate(
        [
            lax.dynamic_slice_in_dim(decoder[0], theirs, half, axis=1),
            lax.dynamic_slice_in_dim(encoder[0], theirs, half, axis=1),
        ],
        axis=0,
    )
    other_w = swap_cores(sent_w)
    other = (other_w[:blocks], other_w[blocks:])
    own = (
        lax.dynamic_slice_in_dim(decoder[0], mine, half, axis=1),
        lax.dynamic_slice_in_dim(encoder[0], mine, half, axis=1),
    )
    attr_keep = jnp.zeros((rows, acts.shape[2]), jnp.float32)
    grad_keep = jnp.zeros(cotangent.shape, jnp.bfloat16)
    g_half = lax.dynamic_slice_in_dim(cotangent, mine, half, axis=1)
    for layer in reversed(range(depth)):
        is_own = here == layer
        attr, g_half, other_small = split_layer(
            g_half, routes[0], acts[0], own, other, is_own, small, other_small
        )
        partner = swap_cores(g_half)
        full = jnp.where(
            here == 0,
            jnp.concatenate([g_half, partner], axis=1),
            jnp.concatenate([partner, g_half], axis=1),
        )
        attr_keep = jnp.where(is_own, attr, attr_keep)
        grad_keep = jnp.where(is_own, full, grad_keep)
    return (attr_keep[None], grad_keep[None])


def per_device(cotangent, routes, acts, decoder, encoder, gain, inv_rms):
    peers = lax.axis_size("dict")
    depth = lax.axis_size("section")
    listed = routes.shape[-1]
    width = cotangent.shape[1]
    if listed == peers and depth == 2 and width % (depth * 128) == 0:
        return split_device(cotangent, routes, acts, decoder, encoder, gain, inv_rms)
    return slot_device(cotangent, routes, acts, decoder, encoder, gain, inv_rms)


def solution(mesh):
    placed = (
        P(("groups", "dict"), None),
        P("section", ("groups", "dict"), None),
        P("section", ("groups", "dict"), None),
        P("section", "dict", None),
        P("section", "dict", None),
        P("section", None),
        P("section", ("groups", "dict")),
    )
    return jax.shard_map(
        per_device,
        mesh=mesh,
        in_specs=placed,
        out_specs=(P("section", ("groups", "dict"), None), P("section", ("groups", "dict"), None)),
        check_vma=False,
    )
```

```python
import jax
import jax.numpy as jnp
from jax import lax
from jax.sharding import PartitionSpec as P


def passed_along(block, axis, distance):
    devices = range(lax.axis_size(axis))
    route = [(i - distance, i) for i in devices if i - distance in devices]
    return lax.ppermute(block, axis, route)


def owner_work(recv_g, recv_act, dec_local, enc_local):
    width = recv_g.shape[-1]
    columns = dec_local.shape[0]
    flat_g = recv_g.reshape(-1, width)
    flat_act = recv_act.reshape(-1, columns)
    coef = lax.dot_general(
        flat_g, dec_local, (((1,), (1,)), ((), ())), preferred_element_type=jnp.float32
    ).astype(jnp.bfloat16)
    masked = jnp.where(flat_act > 0, coef, jnp.zeros_like(coef))
    contrib = jnp.dot(masked, enc_local, preferred_element_type=jnp.float32).astype(jnp.bfloat16)
    lead = recv_g.shape[:-1]
    return (coef.reshape(lead + (columns,)), contrib.reshape(lead + (width,)))


def layer_pass(g_rows, routes_l, acts_l, dec_local, enc_local, gain_l, scale_l, peers):
    tok_count, listed = routes_l.shape
    block = acts_l.shape[1] // listed
    width = dec_local.shape[1]
    held = dec_local.shape[0] // block
    slots_per = (tok_count * listed + peers - 1) // peers
    total_slots = peers * slots_per
    owner = routes_l // held
    within = routes_l - owner * held
    owners = jnp.arange(peers, dtype=jnp.int32)
    hits = (owner[:, :, None] == owners[None, None, :]).astype(jnp.int32)
    per_row = jnp.sum(hits, axis=1)
    earlier = jnp.cumsum(per_row, axis=0) - per_row
    place = jnp.sum(hits * earlier[:, None, :], axis=2)
    slot_of = (owner * slots_per + place).reshape(-1)
    slot_ids = jnp.arange(total_slots, dtype=jnp.int32)
    pick = (slot_ids[:, None] == slot_of[None, :]).astype(jnp.bfloat16)
    row_pick = jnp.sum(
        pick.reshape(total_slots, tok_count, listed).astype(jnp.float32), axis=2
    ).astype(jnp.bfloat16)
    send_g = jnp.dot(row_pick, g_rows, preferred_element_type=jnp.float32).astype(jnp.bfloat16)
    block_act = jnp.dot(
        pick, acts_l.reshape(tok_count * listed, block), preferred_element_type=jnp.float32
    ).astype(jnp.bfloat16)
    within_hot = (within.reshape(-1)[:, None] == jnp.arange(held, dtype=jnp.int32)[None, :]).astype(
        jnp.bfloat16
    )
    slot_within = jnp.dot(pick, within_hot, preferred_element_type=jnp.float32).astype(jnp.bfloat16)
    send_act = (slot_within[:, :, None] * block_act[:, None, :]).reshape(total_slots, held * block)
    send_g = send_g.reshape(peers, slots_per, width)
    send_act = send_act.reshape(peers, slots_per, held * block)
    recv_g, recv_act = (
        lax.all_to_all(send_g, "dict", split_axis=0, concat_axis=0, tiled=True),
        lax.all_to_all(send_act, "dict", split_axis=0, concat_axis=0, tiled=True),
    )
    coef_here, contrib_here = owner_work(recv_g, recv_act, dec_local, enc_local)
    coef_back, contrib_back = (
        lax.all_to_all(coef_here, "dict", split_axis=0, concat_axis=0, tiled=True),
        lax.all_to_all(contrib_here, "dict", split_axis=0, concat_axis=0, tiled=True),
    )
    coef_back = coef_back.reshape(total_slots, held, block)
    contrib_back = contrib_back.reshape(total_slots, width)
    coef_chosen = jnp.sum(
        slot_within.astype(jnp.float32)[:, :, None] * coef_back.astype(jnp.float32), axis=1
    ).astype(jnp.bfloat16)
    coef_rows = lax.dot_general(
        pick, coef_chosen, (((0,), (0,)), ((), ())), preferred_element_type=jnp.float32
    )
    attr = (acts_l.reshape(tok_count * listed, block).astype(jnp.float32) * coef_rows).reshape(
        tok_count, listed * block
    )
    summed = lax.dot_general(
        row_pick, contrib_back, (((0,), (0,)), ((), ())), preferred_element_type=jnp.float32
    )
    new_g = (g_rows.astype(jnp.float32) + scale_l[:, None] * gain_l[None, :] * summed).astype(
        jnp.bfloat16
    )
    return (attr, new_g)


def slot_device(cotangent, routes, acts, decoder, encoder, gain, inv_rms):
    peers = lax.axis_size("dict")
    depth = lax.axis_size("section")
    here = lax.axis_index("section")
    routes_l = routes[0]
    acts_l = acts[0]
    dec_local = decoder[0]
    enc_local = encoder[0]
    gain_l = gain[0]
    scale_l = inv_rms[0]
    tok_count, listed = routes_l.shape
    attr_keep = jnp.zeros((tok_count, acts_l.shape[1]), jnp.float32)
    grad_keep = jnp.zeros(cotangent.shape, jnp.bfloat16)
    g_new = cotangent
    for turn in range(depth):
        if turn > 0:
            g_now = passed_along(g_new, "section", -1)
        else:
            g_now = cotangent
        active = here == depth - 1 - turn
        attr, g_new = layer_pass(
            g_now, routes_l, acts_l, dec_local, enc_local, gain_l, scale_l, peers
        )
        attr_keep = jnp.where(active, attr, attr_keep)
        grad_keep = jnp.where(active, g_new, grad_keep)
    return (attr_keep[None], grad_keep[None])


def swap_cores(block):
    return lax.ppermute(block, "section", [(0, 1), (1, 0)])


def exchange(parts, sign):
    peers = parts.shape[0]
    moved = [parts[0]]
    for shift in range(1, peers):
        route = [(d, d ^ (peers - shift)) for d in range(peers)]
        moved.append(lax.ppermute(parts[shift], "dict", route))
    return jnp.stack(moved, axis=0)


def split_layer(g_half, routes_l, acts_l, own, other, is_own, gain_half, scale_l):
    peers = lax.axis_size("dict")
    me = lax.axis_index("dict")
    rows, listed = routes_l.shape
    block = acts_l.shape[1] // listed
    held = own[0].shape[0] // block
    half = g_half.shape[1]
    owner = routes_l // held
    within = routes_l - owner * held
    rel = (peers - lax.bitwise_xor(owner, me)) % peers
    shifts = jnp.arange(peers, dtype=jnp.int32)
    at_rel = (rel[:, :, None] == shifts[None, None, :]).astype(jnp.bfloat16)
    act_grid = acts_l.reshape(rows, listed, block)
    live = (act_grid > 0).astype(jnp.bfloat16) * (1 + within).astype(jnp.bfloat16)[:, :, None]
    placed = jnp.einsum(
        "rks,rkj->srj", at_rel, live, preferred_element_type=jnp.float32
    ).astype(jnp.bfloat16)
    sent = jnp.concatenate(
        [jnp.broadcast_to(g_half[None], (peers, rows, half)), placed], axis=-1
    )
    got = exchange(sent, 1).reshape(peers * rows, half + block)
    g_all = got[:, :half]
    code_all = got[:, half:]

    def with_dec(dec):
        return lax.dot_general(
            g_all, dec, (((1,), (1,)), ((), ())), preferred_element_type=jnp.float32
        )

    part = jnp.where(is_own, with_dec(own[0]), with_dec(other[0]))
    paired = swap_cores(jnp.concatenate([part, code_all.astype(jnp.float32)], axis=1))
    coef = (part + paired[:, :held * block]).astype(jnp.bfloat16)
    code = jnp.where(is_own, code_all.astype(jnp.float32), paired[:, held * block:])
    marks = jnp.concatenate([code == spot + 1 for spot in range(held)], axis=1)
    dz = jnp.where(marks, coef, jnp.zeros_like(coef))

    def with_enc(enc):
        return jnp.dot(dz, enc, preferred_element_type=jnp.float32)

    contrib = jnp.where(is_own, with_enc(own[1]), with_enc(other[1])).astype(jnp.bfloat16)
    dz_pick = dz[:, :block]
    for spot in range(1, held):
        dz_pick = dz_pick + dz[:, spot * block:(spot + 1) * block]
    back = jnp.concatenate([contrib, dz_pick], axis=-1).reshape(peers, rows, half + block)
    returned = exchange(back, -1)
    total = jnp.sum(returned[:, :, :half].astype(jnp.float32), axis=0)
    dz_back = returned[:, :, half:]
    dz_slot = jnp.einsum("rks,srj->rkj", at_rel, dz_back, preferred_element_type=jnp.float32)
    attr = (act_grid.astype(jnp.float32) * dz_slot).reshape(rows, listed * block)
    new_half = (g_half.astype(jnp.float32) + scale_l[:, None] * gain_half[None, :] * total).astype(
        jnp.bfloat16
    )
    return attr, new_half


def split_device(cotangent, routes, acts, decoder, encoder, gain, inv_rms):
    depth = lax.axis_size("section")
    here = lax.axis_index("section")
    rows, width = cotangent.shape
    blocks = decoder.shape[1]
    half = width // depth
    mine = here * half
    theirs = (1 - here) * half
    small = jnp.concatenate([gain[0], inv_rms[0]], axis=0)
    other_small = swap_cores(small)
    sent_w = jnp.concatenate(
        [
            lax.dynamic_slice_in_dim(decoder[0], theirs, half, axis=1),
            lax.dynamic_slice_in_dim(encoder[0], theirs, half, axis=1),
        ],
        axis=0,
    )
    other_w = swap_cores(sent_w)
    other = (other_w[:blocks], other_w[blocks:])
    own = (
        lax.dynamic_slice_in_dim(decoder[0], mine, half, axis=1),
        lax.dynamic_slice_in_dim(encoder[0], mine, half, axis=1),
    )
    attr_keep = jnp.zeros((rows, acts.shape[2]), jnp.float32)
    grad_keep = jnp.zeros(cotangent.shape, jnp.bfloat16)
    g_half = lax.dynamic_slice_in_dim(cotangent, mine, half, axis=1)
    for layer in reversed(range(depth)):
        is_own = here == layer
        s = jnp.where(is_own, small, other_small)
        gain_half = lax.dynamic_slice_in_dim(s[:width], mine, half, axis=0)
        scale_l = s[width:width + rows]
        attr, g_half = split_layer(g_half, routes[0], acts[0], own, other, is_own, gain_half, scale_l)
        partner = swap_cores(g_half)
        full = jnp.where(
            here == 0,
            jnp.concatenate([g_half, partner], axis=1),
            jnp.concatenate([partner, g_half], axis=1),
        )
        attr_keep = jnp.where(is_own, attr, attr_keep)
        grad_keep = jnp.where(is_own, full, grad_keep)
    return (attr_keep[None], grad_keep[None])


def per_device(cotangent, routes, acts, decoder, encoder, gain, inv_rms):
    peers = lax.axis_size("dict")
    depth = lax.axis_size("section")
    listed = routes.shape[-1]
    width = cotangent.shape[1]
    if listed == peers and peers & (peers - 1) == 0 and depth == 2 and width % (depth * 128) == 0:
        return split_device(cotangent, routes, acts, decoder, encoder, gain, inv_rms)
    return slot_device(cotangent, routes, acts, decoder, encoder, gain, inv_rms)


def solution(mesh):
    placed = (
        P(("groups", "dict"), None),
        P("section", ("groups", "dict"), None),
        P("section", ("groups", "dict"), None),
        P("section", "dict", None),
        P("section", "dict", None),
        P("section", None),
        P("section", ("groups", "dict")),
    )
    return jax.shard_map(
        per_device,
        mesh=mesh,
        in_specs=placed,
        out_specs=(P("section", ("groups", "dict"), None), P("section", ("groups", "dict"), None)),
        check_vma=False,
    )
```

```python
import jax
import jax.numpy as jnp
from jax import lax
from jax.sharding import PartitionSpec as P


def passed_along(block, axis, distance):
    devices = range(lax.axis_size(axis))
    route = [(i - distance, i) for i in devices if i - distance in devices]
    return lax.ppermute(block, axis, route)


def owner_work(recv_g, recv_act, dec_local, enc_local):
    width = recv_g.shape[-1]
    columns = dec_local.shape[0]
    flat_g = recv_g.reshape(-1, width)
    flat_act = recv_act.reshape(-1, columns)
    coef = lax.dot_general(
        flat_g, dec_local, (((1,), (1,)), ((), ())), preferred_element_type=jnp.float32
    ).astype(jnp.bfloat16)
    masked = jnp.where(flat_act > 0, coef, jnp.zeros_like(coef))
    contrib = jnp.dot(masked, enc_local, preferred_element_type=jnp.float32).astype(jnp.bfloat16)
    lead = recv_g.shape[:-1]
    return (coef.reshape(lead + (columns,)), contrib.reshape(lead + (width,)))


def layer_pass(g_rows, routes_l, acts_l, dec_local, enc_local, gain_l, scale_l, peers):
    tok_count, listed = routes_l.shape
    block = acts_l.shape[1] // listed
    width = dec_local.shape[1]
    held = dec_local.shape[0] // block
    slots_per = (tok_count * listed + peers - 1) // peers
    total_slots = peers * slots_per
    owner = routes_l // held
    within = routes_l - owner * held
    owners = jnp.arange(peers, dtype=jnp.int32)
    hits = (owner[:, :, None] == owners[None, None, :]).astype(jnp.int32)
    per_row = jnp.sum(hits, axis=1)
    earlier = jnp.cumsum(per_row, axis=0) - per_row
    place = jnp.sum(hits * earlier[:, None, :], axis=2)
    slot_of = (owner * slots_per + place).reshape(-1)
    slot_ids = jnp.arange(total_slots, dtype=jnp.int32)
    pick = (slot_ids[:, None] == slot_of[None, :]).astype(jnp.bfloat16)
    row_pick = jnp.sum(
        pick.reshape(total_slots, tok_count, listed).astype(jnp.float32), axis=2
    ).astype(jnp.bfloat16)
    send_g = jnp.dot(row_pick, g_rows, preferred_element_type=jnp.float32).astype(jnp.bfloat16)
    block_act = jnp.dot(
        pick, acts_l.reshape(tok_count * listed, block), preferred_element_type=jnp.float32
    ).astype(jnp.bfloat16)
    within_hot = (within.reshape(-1)[:, None] == jnp.arange(held, dtype=jnp.int32)[None, :]).astype(
        jnp.bfloat16
    )
    slot_within = jnp.dot(pick, within_hot, preferred_element_type=jnp.float32).astype(jnp.bfloat16)
    send_act = (slot_within[:, :, None] * block_act[:, None, :]).reshape(total_slots, held * block)
    send_g = send_g.reshape(peers, slots_per, width)
    send_act = send_act.reshape(peers, slots_per, held * block)
    recv_g, recv_act = (
        lax.all_to_all(send_g, "dict", split_axis=0, concat_axis=0, tiled=True),
        lax.all_to_all(send_act, "dict", split_axis=0, concat_axis=0, tiled=True),
    )
    coef_here, contrib_here = owner_work(recv_g, recv_act, dec_local, enc_local)
    coef_back, contrib_back = (
        lax.all_to_all(coef_here, "dict", split_axis=0, concat_axis=0, tiled=True),
        lax.all_to_all(contrib_here, "dict", split_axis=0, concat_axis=0, tiled=True),
    )
    coef_back = coef_back.reshape(total_slots, held, block)
    contrib_back = contrib_back.reshape(total_slots, width)
    coef_chosen = jnp.sum(
        slot_within.astype(jnp.float32)[:, :, None] * coef_back.astype(jnp.float32), axis=1
    ).astype(jnp.bfloat16)
    coef_rows = lax.dot_general(
        pick, coef_chosen, (((0,), (0,)), ((), ())), preferred_element_type=jnp.float32
    )
    attr = (acts_l.reshape(tok_count * listed, block).astype(jnp.float32) * coef_rows).reshape(
        tok_count, listed * block
    )
    summed = lax.dot_general(
        row_pick, contrib_back, (((0,), (0,)), ((), ())), preferred_element_type=jnp.float32
    )
    new_g = (g_rows.astype(jnp.float32) + scale_l[:, None] * gain_l[None, :] * summed).astype(
        jnp.bfloat16
    )
    return (attr, new_g)


def slot_device(cotangent, routes, acts, decoder, encoder, gain, inv_rms):
    peers = lax.axis_size("dict")
    depth = lax.axis_size("section")
    here = lax.axis_index("section")
    routes_l = routes[0]
    acts_l = acts[0]
    dec_local = decoder[0]
    enc_local = encoder[0]
    gain_l = gain[0]
    scale_l = inv_rms[0]
    tok_count, listed = routes_l.shape
    attr_keep = jnp.zeros((tok_count, acts_l.shape[1]), jnp.float32)
    grad_keep = jnp.zeros(cotangent.shape, jnp.bfloat16)
    g_new = cotangent
    for turn in range(depth):
        if turn > 0:
            g_now = passed_along(g_new, "section", -1)
        else:
            g_now = cotangent
        active = here == depth - 1 - turn
        attr, g_new = layer_pass(
            g_now, routes_l, acts_l, dec_local, enc_local, gain_l, scale_l, peers
        )
        attr_keep = jnp.where(active, attr, attr_keep)
        grad_keep = jnp.where(active, g_new, grad_keep)
    return (attr_keep[None], grad_keep[None])


def swap_cores(block):
    return lax.ppermute(block, "section", [(0, 1), (1, 0)])


def exchange(parts, sign):
    peers = parts.shape[0]
    moved = [parts[0]]
    for shift in range(1, peers):
        route = [(d, d ^ (peers - shift)) for d in range(peers)]
        moved.append(lax.ppermute(parts[shift], "dict", route))
    return jnp.stack(moved, axis=0)


def split_layer(g_half, routes_l, acts_l, own, other, is_own, small, other_small):
    peers = lax.axis_size("dict")
    me = lax.axis_index("dict")
    rows, listed = routes_l.shape
    block = acts_l.shape[1] // listed
    held = own[0].shape[0] // block
    half = g_half.shape[1]
    owner = routes_l // held
    within = routes_l - owner * held
    rel = (peers - lax.bitwise_xor(owner, me)) % peers
    shifts = jnp.arange(peers, dtype=jnp.int32)
    at_rel = (rel[:, :, None] == shifts[None, None, :]).astype(jnp.bfloat16)
    act_grid = acts_l.reshape(rows, listed, block)
    live = (act_grid > 0).astype(jnp.bfloat16) * (1 + within).astype(jnp.bfloat16)[:, :, None]
    placed = jnp.einsum(
        "rks,rkj->srj", at_rel, live, preferred_element_type=jnp.float32
    ).astype(jnp.bfloat16)
    sent = jnp.concatenate(
        [jnp.broadcast_to(g_half[None], (peers, rows, half)), placed], axis=-1
    )
    got = exchange(sent, 1).reshape(peers * rows, half + block)
    if other_small is None:
        small, got = lax.optimization_barrier((small, got))
        other_small = swap_cores(small)
    g_all = got[:, :half]
    code_all = got[:, half:]

    def with_dec(dec):
        return lax.dot_general(
            g_all, dec, (((1,), (1,)), ((), ())), preferred_element_type=jnp.float32
        )

    part = jnp.where(is_own, with_dec(own[0]), with_dec(other[0]))
    paired = swap_cores(jnp.concatenate([part, code_all.astype(jnp.float32)], axis=1))
    coef = (part + paired[:, :held * block]).astype(jnp.bfloat16)
    code = jnp.where(is_own, code_all.astype(jnp.float32), paired[:, held * block:])
    marks = jnp.concatenate([code == spot + 1 for spot in range(held)], axis=1)
    dz = jnp.where(marks, coef, jnp.zeros_like(coef))

    def with_enc(enc):
        return jnp.dot(dz, enc, preferred_element_type=jnp.float32)

    contrib = jnp.where(is_own, with_enc(own[1]), with_enc(other[1])).astype(jnp.bfloat16)
    dz_pick = dz[:, :block]
    for spot in range(1, held):
        dz_pick = dz_pick + dz[:, spot * block:(spot + 1) * block]
    back = jnp.concatenate([contrib, dz_pick], axis=-1).reshape(peers, rows, half + block)
    returned = exchange(back, -1)
    total = jnp.sum(returned[:, :, :half].astype(jnp.float32), axis=0)
    dz_back = returned[:, :, half:]
    dz_slot = jnp.einsum("rks,srj->rkj", at_rel, dz_back, preferred_element_type=jnp.float32)
    attr = (act_grid.astype(jnp.float32) * dz_slot).reshape(rows, listed * block)
    width = half * lax.axis_size("section")
    s = jnp.where(is_own, small, other_small)
    gain_half = lax.dynamic_slice_in_dim(s[:width], lax.axis_index("section") * half, half, axis=0)
    scale_l = s[width:width + rows]
    new_half = (g_half.astype(jnp.float32) + scale_l[:, None] * gain_half[None, :] * total).astype(
        jnp.bfloat16
    )
    return attr, new_half, other_small


def split_device(cotangent, routes, acts, decoder, encoder, gain, inv_rms):
    depth = lax.axis_size("section")
    here = lax.axis_index("section")
    rows, width = cotangent.shape
    blocks = decoder.shape[1]
    half = width // depth
    mine = here * half
    theirs = (1 - here) * half
    small = jnp.concatenate([gain[0], inv_rms[0]], axis=0)
    other_small = None
    sent_w = jnp.concatenate(
        [
            lax.dynamic_slice_in_dim(decoder[0], theirs, half, axis=1),
            lax.dynamic_slice_in_dim(encoder[0], theirs, half, axis=1),
        ],
        axis=0,
    )
    other_w = swap_cores(sent_w)
    other = (other_w[:blocks], other_w[blocks:])
    own = (
        lax.dynamic_slice_in_dim(decoder[0], mine, half, axis=1),
        lax.dynamic_slice_in_dim(encoder[0], mine, half, axis=1),
    )
    attr_keep = jnp.zeros((rows, acts.shape[2]), jnp.float32)
    grad_keep = jnp.zeros(cotangent.shape, jnp.bfloat16)
    g_half = lax.dynamic_slice_in_dim(cotangent, mine, half, axis=1)
    for layer in reversed(range(depth)):
        is_own = here == layer
        attr, g_half, other_small = split_layer(
            g_half, routes[0], acts[0], own, other, is_own, small, other_small
        )
        partner = swap_cores(g_half)
        full = jnp.where(
            here == 0,
            jnp.concatenate([g_half, partner], axis=1),
            jnp.concatenate([partner, g_half], axis=1),
        )
        attr_keep = jnp.where(is_own, attr, attr_keep)
        grad_keep = jnp.where(is_own, full, grad_keep)
    return (attr_keep[None], grad_keep[None])


def per_device(cotangent, routes, acts, decoder, encoder, gain, inv_rms):
    peers = lax.axis_size("dict")
    depth = lax.axis_size("section")
    listed = routes.shape[-1]
    width = cotangent.shape[1]
    if listed == peers and peers & (peers - 1) == 0 and depth == 2 and width % (depth * 128) == 0:
        return split_device(cotangent, routes, acts, decoder, encoder, gain, inv_rms)
    return slot_device(cotangent, routes, acts, decoder, encoder, gain, inv_rms)


def solution(mesh):
    placed = (
        P(("groups", "dict"), None),
        P("section", ("groups", "dict"), None),
        P("section", ("groups", "dict"), None),
        P("section", "dict", None),
        P("section", "dict", None),
        P("section", None),
        P("section", ("groups", "dict")),
    )
    return jax.shard_map(
        per_device,
        mesh=mesh,
        in_specs=placed,
        out_specs=(P("section", ("groups", "dict"), None), P("section", ("groups", "dict"), None)),
        check_vma=False,
    )
```

```python
import jax
import jax.numpy as jnp
from jax import lax
from jax.sharding import PartitionSpec as P


def passed_along(block, axis, distance):
    devices = range(lax.axis_size(axis))
    route = [(i - distance, i) for i in devices if i - distance in devices]
    return lax.ppermute(block, axis, route)


def owner_work(recv_g, recv_act, dec_local, enc_local):
    width = recv_g.shape[-1]
    columns = dec_local.shape[0]
    flat_g = recv_g.reshape(-1, width)
    flat_act = recv_act.reshape(-1, columns)
    coef = lax.dot_general(
        flat_g, dec_local, (((1,), (1,)), ((), ())), preferred_element_type=jnp.float32
    ).astype(jnp.bfloat16)
    masked = jnp.where(flat_act > 0, coef, jnp.zeros_like(coef))
    contrib = jnp.dot(masked, enc_local, preferred_element_type=jnp.float32).astype(jnp.bfloat16)
    lead = recv_g.shape[:-1]
    return (coef.reshape(lead + (columns,)), contrib.reshape(lead + (width,)))


def layer_pass(g_rows, routes_l, acts_l, dec_local, enc_local, gain_l, scale_l, peers):
    tok_count, listed = routes_l.shape
    block = acts_l.shape[1] // listed
    width = dec_local.shape[1]
    held = dec_local.shape[0] // block
    slots_per = (tok_count * listed + peers - 1) // peers
    total_slots = peers * slots_per
    owner = routes_l // held
    within = routes_l - owner * held
    owners = jnp.arange(peers, dtype=jnp.int32)
    hits = (owner[:, :, None] == owners[None, None, :]).astype(jnp.int32)
    per_row = jnp.sum(hits, axis=1)
    earlier = jnp.cumsum(per_row, axis=0) - per_row
    place = jnp.sum(hits * earlier[:, None, :], axis=2)
    slot_of = (owner * slots_per + place).reshape(-1)
    slot_ids = jnp.arange(total_slots, dtype=jnp.int32)
    pick = (slot_ids[:, None] == slot_of[None, :]).astype(jnp.bfloat16)
    row_pick = jnp.sum(
        pick.reshape(total_slots, tok_count, listed).astype(jnp.float32), axis=2
    ).astype(jnp.bfloat16)
    send_g = jnp.dot(row_pick, g_rows, preferred_element_type=jnp.float32).astype(jnp.bfloat16)
    block_act = jnp.dot(
        pick, acts_l.reshape(tok_count * listed, block), preferred_element_type=jnp.float32
    ).astype(jnp.bfloat16)
    within_hot = (within.reshape(-1)[:, None] == jnp.arange(held, dtype=jnp.int32)[None, :]).astype(
        jnp.bfloat16
    )
    slot_within = jnp.dot(pick, within_hot, preferred_element_type=jnp.float32).astype(jnp.bfloat16)
    send_act = (slot_within[:, :, None] * block_act[:, None, :]).reshape(total_slots, held * block)
    send_g = send_g.reshape(peers, slots_per, width)
    send_act = send_act.reshape(peers, slots_per, held * block)
    recv_g, recv_act = (
        lax.all_to_all(send_g, "dict", split_axis=0, concat_axis=0, tiled=True),
        lax.all_to_all(send_act, "dict", split_axis=0, concat_axis=0, tiled=True),
    )
    coef_here, contrib_here = owner_work(recv_g, recv_act, dec_local, enc_local)
    coef_back, contrib_back = (
        lax.all_to_all(coef_here, "dict", split_axis=0, concat_axis=0, tiled=True),
        lax.all_to_all(contrib_here, "dict", split_axis=0, concat_axis=0, tiled=True),
    )
    coef_back = coef_back.reshape(total_slots, held, block)
    contrib_back = contrib_back.reshape(total_slots, width)
    coef_chosen = jnp.sum(
        slot_within.astype(jnp.float32)[:, :, None] * coef_back.astype(jnp.float32), axis=1
    ).astype(jnp.bfloat16)
    coef_rows = lax.dot_general(
        pick, coef_chosen, (((0,), (0,)), ((), ())), preferred_element_type=jnp.float32
    )
    attr = (acts_l.reshape(tok_count * listed, block).astype(jnp.float32) * coef_rows).reshape(
        tok_count, listed * block
    )
    summed = lax.dot_general(
        row_pick, contrib_back, (((0,), (0,)), ((), ())), preferred_element_type=jnp.float32
    )
    new_g = (g_rows.astype(jnp.float32) + scale_l[:, None] * gain_l[None, :] * summed).astype(
        jnp.bfloat16
    )
    return (attr, new_g)


def slot_device(cotangent, routes, acts, decoder, encoder, gain, inv_rms):
    peers = lax.axis_size("dict")
    depth = lax.axis_size("section")
    here = lax.axis_index("section")
    routes_l = routes[0]
    acts_l = acts[0]
    dec_local = decoder[0]
    enc_local = encoder[0]
    gain_l = gain[0]
    scale_l = inv_rms[0]
    tok_count, listed = routes_l.shape
    attr_keep = jnp.zeros((tok_count, acts_l.shape[1]), jnp.float32)
    grad_keep = jnp.zeros(cotangent.shape, jnp.bfloat16)
    g_new = cotangent
    for turn in range(depth):
        if turn > 0:
            g_now = passed_along(g_new, "section", -1)
        else:
            g_now = cotangent
        active = here == depth - 1 - turn
        attr, g_new = layer_pass(
            g_now, routes_l, acts_l, dec_local, enc_local, gain_l, scale_l, peers
        )
        attr_keep = jnp.where(active, attr, attr_keep)
        grad_keep = jnp.where(active, g_new, grad_keep)
    return (attr_keep[None], grad_keep[None])


def swap_cores(block):
    return lax.ppermute(block, "section", [(0, 1), (1, 0)])


def exchange(parts, sign):
    peers = parts.shape[0]
    moved = [parts[0]]
    for shift in range(1, peers):
        route = [(d, d ^ (peers - shift)) for d in range(peers)]
        moved.append(lax.ppermute(parts[shift], "dict", route))
    return jnp.stack(moved, axis=0)


def split_layer(g_half, routes_l, acts_l, own, other, is_own, small, other_small):
    peers = lax.axis_size("dict")
    me = lax.axis_index("dict")
    rows, listed = routes_l.shape
    block = acts_l.shape[1] // listed
    held = own[0].shape[0] // block
    half = g_half.shape[1]
    owner = routes_l // held
    within = routes_l - owner * held
    rel = (peers - lax.bitwise_xor(owner, me)) % peers
    shifts = jnp.arange(peers, dtype=jnp.int32)
    at_rel = (rel[:, :, None] == shifts[None, None, :]).astype(jnp.bfloat16)
    act_grid = acts_l.reshape(rows, listed, block)
    live = (act_grid > 0).astype(jnp.bfloat16) * (1 + within).astype(jnp.bfloat16)[:, :, None]
    placed = jnp.einsum(
        "rks,rkj->srj", at_rel, live, preferred_element_type=jnp.float32
    ).astype(jnp.bfloat16)
    sent = jnp.concatenate(
        [jnp.broadcast_to(g_half[None], (peers, rows, half)), placed], axis=-1
    )
    got = exchange(sent, 1).reshape(peers * rows, half + block)
    if other_small is None:
        small, got = lax.optimization_barrier((small, got))
        other_small = swap_cores(small)
    g_all = got[:, :half]
    code_all = got[:, half:]

    def with_dec(dec):
        return lax.dot_general(
            g_all, dec, (((1,), (1,)), ((), ())), preferred_element_type=jnp.float32
        )

    part = jnp.where(is_own, with_dec(own[0]), with_dec(other[0]))
    paired = swap_cores(jnp.concatenate([part, code_all.astype(jnp.float32)], axis=1))
    coef = (part + paired[:, :held * block]).astype(jnp.bfloat16)
    code = jnp.where(is_own, code_all.astype(jnp.float32), paired[:, held * block:])
    marks = jnp.concatenate([code == spot + 1 for spot in range(held)], axis=1)
    dz = jnp.where(marks, coef, jnp.zeros_like(coef))

    def with_enc(enc):
        return jnp.dot(dz, enc, preferred_element_type=jnp.float32)

    contrib = jnp.where(is_own, with_enc(own[1]), with_enc(other[1])).astype(jnp.bfloat16)
    dz_pick = dz[:, :block]
    for spot in range(1, held):
        dz_pick = dz_pick + dz[:, spot * block:(spot + 1) * block]
    back = jnp.concatenate([contrib, dz_pick], axis=-1).reshape(peers, rows, half + block)
    returned = exchange(back, -1)
    total = jnp.sum(returned[:, :, :half].astype(jnp.float32), axis=0)
    dz_back = returned[:, :, half:]
    dz_slot = jnp.einsum("rks,srj->rkj", at_rel, dz_back, preferred_element_type=jnp.float32)
    attr = (act_grid.astype(jnp.float32) * dz_slot).reshape(rows, listed * block)
    width = half * lax.axis_size("section")
    s = jnp.where(is_own, small, other_small)
    gain_half = lax.dynamic_slice_in_dim(s[:width], lax.axis_index("section") * half, half, axis=0)
    scale_l = s[width:width + rows]
    new_half = (g_half.astype(jnp.float32) + scale_l[:, None] * gain_half[None, :] * total).astype(
        jnp.bfloat16
    )
    return attr, new_half, other_small


def split_device(cotangent, routes, acts, decoder, encoder, gain, inv_rms):
    depth = lax.axis_size("section")
    here = lax.axis_index("section")
    rows, width = cotangent.shape
    blocks = decoder.shape[1]
    half = width // depth
    mine = here * half
    theirs = (1 - here) * half
    small = jnp.concatenate([gain[0], inv_rms[0]], axis=0)
    other_small = None
    halves = []
    sent_w = jnp.concatenate(
        [
            lax.dynamic_slice_in_dim(decoder[0], theirs, half, axis=1),
            lax.dynamic_slice_in_dim(encoder[0], theirs, half, axis=1),
        ],
        axis=0,
    )
    other_w = swap_cores(sent_w)
    other = (other_w[:blocks], other_w[blocks:])
    own = (
        lax.dynamic_slice_in_dim(decoder[0], mine, half, axis=1),
        lax.dynamic_slice_in_dim(encoder[0], mine, half, axis=1),
    )
    attr_keep = jnp.zeros((rows, acts.shape[2]), jnp.float32)
    grad_keep = jnp.zeros(cotangent.shape, jnp.bfloat16)
    g_half = lax.dynamic_slice_in_dim(cotangent, mine, half, axis=1)
    for layer in reversed(range(depth)):
        is_own = here == layer
        attr, g_half, other_small = split_layer(
            g_half, routes[0], acts[0], own, other, is_own, small, other_small
        )
        halves.append(g_half)
        attr_keep = jnp.where(is_own, attr, attr_keep)
    mine_both = jnp.stack(halves, axis=0)
    theirs_both = swap_cores(mine_both)
    for step, layer in enumerate(reversed(range(depth))):
        full = jnp.where(
            here == 0,
            jnp.concatenate([mine_both[step], theirs_both[step]], axis=1),
            jnp.concatenate([theirs_both[step], mine_both[step]], axis=1),
        )
        grad_keep = jnp.where(here == layer, full, grad_keep)
    return (attr_keep[None], grad_keep[None])


def per_device(cotangent, routes, acts, decoder, encoder, gain, inv_rms):
    peers = lax.axis_size("dict")
    depth = lax.axis_size("section")
    listed = routes.shape[-1]
    width = cotangent.shape[1]
    if listed == peers and peers & (peers - 1) == 0 and depth == 2 and width % (depth * 128) == 0:
        return split_device(cotangent, routes, acts, decoder, encoder, gain, inv_rms)
    return slot_device(cotangent, routes, acts, decoder, encoder, gain, inv_rms)


def solution(mesh):
    placed = (
        P(("groups", "dict"), None),
        P("section", ("groups", "dict"), None),
        P("section", ("groups", "dict"), None),
        P("section", "dict", None),
        P("section", "dict", None),
        P("section", None),
        P("section", ("groups", "dict")),
    )
    return jax.shard_map(
        per_device,
        mesh=mesh,
        in_specs=placed,
        out_specs=(P("section", ("groups", "dict"), None), P("section", ("groups", "dict"), None)),
        check_vma=False,
    )
```

```python
import jax
import jax.numpy as jnp
from jax import lax
from jax.sharding import PartitionSpec as P


def passed_along(block, axis, distance):
    devices = range(lax.axis_size(axis))
    route = [(i - distance, i) for i in devices if i - distance in devices]
    return lax.ppermute(block, axis, route)


def owner_work(recv_g, recv_act, dec_local, enc_local):
    width = recv_g.shape[-1]
    columns = dec_local.shape[0]
    flat_g = recv_g.reshape(-1, width)
    flat_act = recv_act.reshape(-1, columns)
    coef = lax.dot_general(
        flat_g, dec_local, (((1,), (1,)), ((), ())), preferred_element_type=jnp.float32
    ).astype(jnp.bfloat16)
    masked = jnp.where(flat_act > 0, coef, jnp.zeros_like(coef))
    contrib = jnp.dot(masked, enc_local, preferred_element_type=jnp.float32).astype(jnp.bfloat16)
    lead = recv_g.shape[:-1]
    return (coef.reshape(lead + (columns,)), contrib.reshape(lead + (width,)))


def layer_pass(g_rows, routes_l, acts_l, dec_local, enc_local, gain_l, scale_l, peers):
    tok_count, listed = routes_l.shape
    block = acts_l.shape[1] // listed
    width = dec_local.shape[1]
    held = dec_local.shape[0] // block
    slots_per = (tok_count * listed + peers - 1) // peers
    total_slots = peers * slots_per
    owner = routes_l // held
    within = routes_l - owner * held
    owners = jnp.arange(peers, dtype=jnp.int32)
    hits = (owner[:, :, None] == owners[None, None, :]).astype(jnp.int32)
    per_row = jnp.sum(hits, axis=1)
    earlier = jnp.cumsum(per_row, axis=0) - per_row
    place = jnp.sum(hits * earlier[:, None, :], axis=2)
    slot_of = (owner * slots_per + place).reshape(-1)
    slot_ids = jnp.arange(total_slots, dtype=jnp.int32)
    pick = (slot_ids[:, None] == slot_of[None, :]).astype(jnp.bfloat16)
    row_pick = jnp.sum(
        pick.reshape(total_slots, tok_count, listed).astype(jnp.float32), axis=2
    ).astype(jnp.bfloat16)
    send_g = jnp.dot(row_pick, g_rows, preferred_element_type=jnp.float32).astype(jnp.bfloat16)
    block_act = jnp.dot(
        pick, acts_l.reshape(tok_count * listed, block), preferred_element_type=jnp.float32
    ).astype(jnp.bfloat16)
    within_hot = (within.reshape(-1)[:, None] == jnp.arange(held, dtype=jnp.int32)[None, :]).astype(
        jnp.bfloat16
    )
    slot_within = jnp.dot(pick, within_hot, preferred_element_type=jnp.float32).astype(jnp.bfloat16)
    send_act = (slot_within[:, :, None] * block_act[:, None, :]).reshape(total_slots, held * block)
    send_g = send_g.reshape(peers, slots_per, width)
    send_act = send_act.reshape(peers, slots_per, held * block)
    recv_g, recv_act = (
        lax.all_to_all(send_g, "dict", split_axis=0, concat_axis=0, tiled=True),
        lax.all_to_all(send_act, "dict", split_axis=0, concat_axis=0, tiled=True),
    )
    coef_here, contrib_here = owner_work(recv_g, recv_act, dec_local, enc_local)
    coef_back, contrib_back = (
        lax.all_to_all(coef_here, "dict", split_axis=0, concat_axis=0, tiled=True),
        lax.all_to_all(contrib_here, "dict", split_axis=0, concat_axis=0, tiled=True),
    )
    coef_back = coef_back.reshape(total_slots, held, block)
    contrib_back = contrib_back.reshape(total_slots, width)
    coef_chosen = jnp.sum(
        slot_within.astype(jnp.float32)[:, :, None] * coef_back.astype(jnp.float32), axis=1
    ).astype(jnp.bfloat16)
    coef_rows = lax.dot_general(
        pick, coef_chosen, (((0,), (0,)), ((), ())), preferred_element_type=jnp.float32
    )
    attr = (acts_l.reshape(tok_count * listed, block).astype(jnp.float32) * coef_rows).reshape(
        tok_count, listed * block
    )
    summed = lax.dot_general(
        row_pick, contrib_back, (((0,), (0,)), ((), ())), preferred_element_type=jnp.float32
    )
    new_g = (g_rows.astype(jnp.float32) + scale_l[:, None] * gain_l[None, :] * summed).astype(
        jnp.bfloat16
    )
    return (attr, new_g)


def slot_device(cotangent, routes, acts, decoder, encoder, gain, inv_rms):
    peers = lax.axis_size("dict")
    depth = lax.axis_size("section")
    here = lax.axis_index("section")
    routes_l = routes[0]
    acts_l = acts[0]
    dec_local = decoder[0]
    enc_local = encoder[0]
    gain_l = gain[0]
    scale_l = inv_rms[0]
    tok_count, listed = routes_l.shape
    attr_keep = jnp.zeros((tok_count, acts_l.shape[1]), jnp.float32)
    grad_keep = jnp.zeros(cotangent.shape, jnp.bfloat16)
    g_new = cotangent
    for turn in range(depth):
        if turn > 0:
            g_now = passed_along(g_new, "section", -1)
        else:
            g_now = cotangent
        active = here == depth - 1 - turn
        attr, g_new = layer_pass(
            g_now, routes_l, acts_l, dec_local, enc_local, gain_l, scale_l, peers
        )
        attr_keep = jnp.where(active, attr, attr_keep)
        grad_keep = jnp.where(active, g_new, grad_keep)
    return (attr_keep[None], grad_keep[None])


def swap_cores(block):
    return lax.ppermute(block, "section", [(0, 1), (1, 0)])


def exchange(parts, sign):
    peers = parts.shape[0]
    moved = [parts[0]]
    for shift in range(1, peers):
        route = [(d, d ^ (peers - shift)) for d in range(peers)]
        moved.append(lax.ppermute(parts[shift], "dict", route))
    return jnp.stack(moved, axis=0)


def split_layer(g_half, routes_l, acts_l, own, other, is_own, small, other_small):
    peers = lax.axis_size("dict")
    me = lax.axis_index("dict")
    rows, listed = routes_l.shape
    block = acts_l.shape[1] // listed
    held = own[0].shape[0] // block
    half = g_half.shape[1]
    owner = routes_l // held
    within = routes_l - owner * held
    rel = (peers - lax.bitwise_xor(owner, me)) % peers
    shifts = jnp.arange(peers, dtype=jnp.int32)
    at_rel = (rel[:, :, None] == shifts[None, None, :]).astype(jnp.bfloat16)
    act_grid = acts_l.reshape(rows, listed, block)
    live = (act_grid > 0).astype(jnp.bfloat16) * (1 + within).astype(jnp.bfloat16)[:, :, None]
    placed = jnp.einsum(
        "rks,rkj->srj", at_rel, live, preferred_element_type=jnp.float32
    ).astype(jnp.bfloat16)
    sent = jnp.concatenate(
        [jnp.broadcast_to(g_half[None], (peers, rows, half)), placed], axis=-1
    )
    got = exchange(sent, 1).reshape(peers * rows, half + block)
    g_all = got[:, :half]
    code_all = got[:, half:]

    def with_dec(dec):
        return lax.dot_general(
            g_all, dec, (((1,), (1,)), ((), ())), preferred_element_type=jnp.float32
        )

    part = jnp.where(is_own, with_dec(own[0]), with_dec(other[0]))
    joined = jnp.concatenate([part, code_all.astype(jnp.float32)], axis=1)
    if other_small is None:
        lanes = joined.shape[1]
        extra = -(-small.shape[0] // lanes)
        padded = jnp.pad(small, (0, extra * lanes - small.shape[0])).reshape(extra, lanes)
        paired = swap_cores(jnp.concatenate([joined, padded], axis=0))
        other_small = paired[joined.shape[0]:].reshape(-1)[:small.shape[0]]
        paired = paired[:joined.shape[0]]
    else:
        paired = swap_cores(joined)
    coef = (part + paired[:, :held * block]).astype(jnp.bfloat16)
    code = jnp.where(is_own, code_all.astype(jnp.float32), paired[:, held * block:])
    marks = jnp.concatenate([code == spot + 1 for spot in range(held)], axis=1)
    dz = jnp.where(marks, coef, jnp.zeros_like(coef))

    def with_enc(enc):
        return jnp.dot(dz, enc, preferred_element_type=jnp.float32)

    contrib = jnp.where(is_own, with_enc(own[1]), with_enc(other[1])).astype(jnp.bfloat16)
    dz_pick = dz[:, :block]
    for spot in range(1, held):
        dz_pick = dz_pick + dz[:, spot * block:(spot + 1) * block]
    back = jnp.concatenate([contrib, dz_pick], axis=-1).reshape(peers, rows, half + block)
    returned = exchange(back, -1)
    total = jnp.sum(returned[:, :, :half].astype(jnp.float32), axis=0)
    dz_back = returned[:, :, half:]
    dz_slot = jnp.einsum("rks,srj->rkj", at_rel, dz_back, preferred_element_type=jnp.float32)
    attr = (act_grid.astype(jnp.float32) * dz_slot).reshape(rows, listed * block)
    width = half * lax.axis_size("section")
    s = jnp.where(is_own, small, other_small)
    gain_half = lax.dynamic_slice_in_dim(s[:width], lax.axis_index("section") * half, half, axis=0)
    scale_l = s[width:width + rows]
    new_half = (g_half.astype(jnp.float32) + scale_l[:, None] * gain_half[None, :] * total).astype(
        jnp.bfloat16
    )
    return attr, new_half, other_small


def split_device(cotangent, routes, acts, decoder, encoder, gain, inv_rms):
    depth = lax.axis_size("section")
    here = lax.axis_index("section")
    rows, width = cotangent.shape
    blocks = decoder.shape[1]
    half = width // depth
    mine = here * half
    theirs = (1 - here) * half
    small = jnp.concatenate([gain[0], inv_rms[0]], axis=0)
    other_small = None
    halves = []
    sent_w = jnp.concatenate(
        [
            lax.dynamic_slice_in_dim(decoder[0], theirs, half, axis=1),
            lax.dynamic_slice_in_dim(encoder[0], theirs, half, axis=1),
        ],
        axis=0,
    )
    other_w = swap_cores(sent_w)
    other = (other_w[:blocks], other_w[blocks:])
    own = (
        lax.dynamic_slice_in_dim(decoder[0], mine, half, axis=1),
        lax.dynamic_slice_in_dim(encoder[0], mine, half, axis=1),
    )
    attr_keep = jnp.zeros((rows, acts.shape[2]), jnp.float32)
    grad_keep = jnp.zeros(cotangent.shape, jnp.bfloat16)
    g_half = lax.dynamic_slice_in_dim(cotangent, mine, half, axis=1)
    for layer in reversed(range(depth)):
        is_own = here == layer
        attr, g_half, other_small = split_layer(
            g_half, routes[0], acts[0], own, other, is_own, small, other_small
        )
        halves.append(g_half)
        attr_keep = jnp.where(is_own, attr, attr_keep)
    mine_both = jnp.stack(halves, axis=0)
    theirs_both = swap_cores(mine_both)
    for step, layer in enumerate(reversed(range(depth))):
        full = jnp.where(
            here == 0,
            jnp.concatenate([mine_both[step], theirs_both[step]], axis=1),
            jnp.concatenate([theirs_both[step], mine_both[step]], axis=1),
        )
        grad_keep = jnp.where(here == layer, full, grad_keep)
    return (attr_keep[None], grad_keep[None])


def per_device(cotangent, routes, acts, decoder, encoder, gain, inv_rms):
    peers = lax.axis_size("dict")
    depth = lax.axis_size("section")
    listed = routes.shape[-1]
    width = cotangent.shape[1]
    if listed == peers and peers & (peers - 1) == 0 and depth == 2 and width % (depth * 128) == 0:
        return split_device(cotangent, routes, acts, decoder, encoder, gain, inv_rms)
    return slot_device(cotangent, routes, acts, decoder, encoder, gain, inv_rms)


def solution(mesh):
    placed = (
        P(("groups", "dict"), None),
        P("section", ("groups", "dict"), None),
        P("section", ("groups", "dict"), None),
        P("section", "dict", None),
        P("section", "dict", None),
        P("section", None),
        P("section", ("groups", "dict")),
    )
    return jax.shard_map(
        per_device,
        mesh=mesh,
        in_specs=placed,
        out_specs=(P("section", ("groups", "dict"), None), P("section", ("groups", "dict"), None)),
        check_vma=False,
    )
```

```python
import jax
import jax.numpy as jnp
from jax import lax
from jax.sharding import PartitionSpec as P


def passed_along(block, axis, distance):
    devices = range(lax.axis_size(axis))
    route = [(i - distance, i) for i in devices if i - distance in devices]
    return lax.ppermute(block, axis, route)


def owner_work(recv_g, recv_act, dec_local, enc_local):
    width = recv_g.shape[-1]
    columns = dec_local.shape[0]
    flat_g = recv_g.reshape(-1, width)
    flat_act = recv_act.reshape(-1, columns)
    coef = lax.dot_general(
        flat_g, dec_local, (((1,), (1,)), ((), ())), preferred_element_type=jnp.float32
    ).astype(jnp.bfloat16)
    masked = jnp.where(flat_act > 0, coef, jnp.zeros_like(coef))
    contrib = jnp.dot(masked, enc_local, preferred_element_type=jnp.float32).astype(jnp.bfloat16)
    lead = recv_g.shape[:-1]
    return (coef.reshape(lead + (columns,)), contrib.reshape(lead + (width,)))


def layer_pass(g_rows, routes_l, acts_l, dec_local, enc_local, gain_l, scale_l, peers):
    tok_count, listed = routes_l.shape
    block = acts_l.shape[1] // listed
    width = dec_local.shape[1]
    held = dec_local.shape[0] // block
    slots_per = (tok_count * listed + peers - 1) // peers
    total_slots = peers * slots_per
    owner = routes_l // held
    within = routes_l - owner * held
    owners = jnp.arange(peers, dtype=jnp.int32)
    hits = (owner[:, :, None] == owners[None, None, :]).astype(jnp.int32)
    per_row = jnp.sum(hits, axis=1)
    earlier = jnp.cumsum(per_row, axis=0) - per_row
    place = jnp.sum(hits * earlier[:, None, :], axis=2)
    slot_of = (owner * slots_per + place).reshape(-1)
    slot_ids = jnp.arange(total_slots, dtype=jnp.int32)
    pick = (slot_ids[:, None] == slot_of[None, :]).astype(jnp.bfloat16)
    row_pick = jnp.sum(
        pick.reshape(total_slots, tok_count, listed).astype(jnp.float32), axis=2
    ).astype(jnp.bfloat16)
    send_g = jnp.dot(row_pick, g_rows, preferred_element_type=jnp.float32).astype(jnp.bfloat16)
    block_act = jnp.dot(
        pick, acts_l.reshape(tok_count * listed, block), preferred_element_type=jnp.float32
    ).astype(jnp.bfloat16)
    within_hot = (within.reshape(-1)[:, None] == jnp.arange(held, dtype=jnp.int32)[None, :]).astype(
        jnp.bfloat16
    )
    slot_within = jnp.dot(pick, within_hot, preferred_element_type=jnp.float32).astype(jnp.bfloat16)
    send_act = (slot_within[:, :, None] * block_act[:, None, :]).reshape(total_slots, held * block)
    send_g = send_g.reshape(peers, slots_per, width)
    send_act = send_act.reshape(peers, slots_per, held * block)
    recv_g, recv_act = (
        lax.all_to_all(send_g, "dict", split_axis=0, concat_axis=0, tiled=True),
        lax.all_to_all(send_act, "dict", split_axis=0, concat_axis=0, tiled=True),
    )
    coef_here, contrib_here = owner_work(recv_g, recv_act, dec_local, enc_local)
    coef_back, contrib_back = (
        lax.all_to_all(coef_here, "dict", split_axis=0, concat_axis=0, tiled=True),
        lax.all_to_all(contrib_here, "dict", split_axis=0, concat_axis=0, tiled=True),
    )
    coef_back = coef_back.reshape(total_slots, held, block)
    contrib_back = contrib_back.reshape(total_slots, width)
    coef_chosen = jnp.sum(
        slot_within.astype(jnp.float32)[:, :, None] * coef_back.astype(jnp.float32), axis=1
    ).astype(jnp.bfloat16)
    coef_rows = lax.dot_general(
        pick, coef_chosen, (((0,), (0,)), ((), ())), preferred_element_type=jnp.float32
    )
    attr = (acts_l.reshape(tok_count * listed, block).astype(jnp.float32) * coef_rows).reshape(
        tok_count, listed * block
    )
    summed = lax.dot_general(
        row_pick, contrib_back, (((0,), (0,)), ((), ())), preferred_element_type=jnp.float32
    )
    new_g = (g_rows.astype(jnp.float32) + scale_l[:, None] * gain_l[None, :] * summed).astype(
        jnp.bfloat16
    )
    return (attr, new_g)


def slot_device(cotangent, routes, acts, decoder, encoder, gain, inv_rms):
    peers = lax.axis_size("dict")
    depth = lax.axis_size("section")
    here = lax.axis_index("section")
    routes_l = routes[0]
    acts_l = acts[0]
    dec_local = decoder[0]
    enc_local = encoder[0]
    gain_l = gain[0]
    scale_l = inv_rms[0]
    tok_count, listed = routes_l.shape
    attr_keep = jnp.zeros((tok_count, acts_l.shape[1]), jnp.float32)
    grad_keep = jnp.zeros(cotangent.shape, jnp.bfloat16)
    g_new = cotangent
    for turn in range(depth):
        if turn > 0:
            g_now = passed_along(g_new, "section", -1)
        else:
            g_now = cotangent
        active = here == depth - 1 - turn
        attr, g_new = layer_pass(
            g_now, routes_l, acts_l, dec_local, enc_local, gain_l, scale_l, peers
        )
        attr_keep = jnp.where(active, attr, attr_keep)
        grad_keep = jnp.where(active, g_new, grad_keep)
    return (attr_keep[None], grad_keep[None])


def swap_cores(block):
    return lax.ppermute(block, "section", [(0, 1), (1, 0)])


def exchange(parts, sign):
    peers = parts.shape[0]
    moved = [parts[0]]
    for shift in range(1, peers):
        route = [(d, d ^ (peers - shift)) for d in range(peers)]
        moved.append(lax.ppermute(parts[shift], "dict", route))
    return jnp.stack(moved, axis=0)


def split_layer(g_half, routes_l, acts_l, own, other, is_own, small, other_small):
    peers = lax.axis_size("dict")
    me = lax.axis_index("dict")
    rows, listed = routes_l.shape
    block = acts_l.shape[1] // listed
    held = own[0].shape[0] // block
    half = g_half.shape[1]
    owner = routes_l // held
    within = routes_l - owner * held
    rel = (peers - lax.bitwise_xor(owner, me)) % peers
    shifts = jnp.arange(peers, dtype=jnp.int32)
    at_rel = (rel[:, :, None] == shifts[None, None, :]).astype(jnp.bfloat16)
    act_grid = acts_l.reshape(rows, listed, block)
    live = (act_grid > 0).astype(jnp.bfloat16) * (1 + within).astype(jnp.bfloat16)[:, :, None]
    placed = jnp.einsum(
        "rks,rkj->srj", at_rel, live, preferred_element_type=jnp.float32
    ).astype(jnp.bfloat16)
    sent = jnp.concatenate(
        [jnp.broadcast_to(g_half[None], (peers, rows, half)), placed], axis=-1
    )
    if other_small is None:
        other_small = swap_cores(small)
        sent, other_small = lax.optimization_barrier((sent, other_small))
    got = exchange(sent, 1).reshape(peers * rows, half + block)
    g_all = got[:, :half]
    code_all = got[:, half:]

    def with_dec(dec):
        return lax.dot_general(
            g_all, dec, (((1,), (1,)), ((), ())), preferred_element_type=jnp.float32
        )

    part = jnp.where(is_own, with_dec(own[0]), with_dec(other[0]))
    paired = swap_cores(jnp.concatenate([part, code_all.astype(jnp.float32)], axis=1))
    coef = (part + paired[:, :held * block]).astype(jnp.bfloat16)
    code = jnp.where(is_own, code_all.astype(jnp.float32), paired[:, held * block:])
    marks = jnp.concatenate([code == spot + 1 for spot in range(held)], axis=1)
    dz = jnp.where(marks, coef, jnp.zeros_like(coef))

    def with_enc(enc):
        return jnp.dot(dz, enc, preferred_element_type=jnp.float32)

    contrib = jnp.where(is_own, with_enc(own[1]), with_enc(other[1])).astype(jnp.bfloat16)
    dz_pick = dz[:, :block]
    for spot in range(1, held):
        dz_pick = dz_pick + dz[:, spot * block:(spot + 1) * block]
    back = jnp.concatenate([contrib, dz_pick], axis=-1).reshape(peers, rows, half + block)
    returned = exchange(back, -1)
    total = jnp.sum(returned[:, :, :half].astype(jnp.float32), axis=0)
    dz_back = returned[:, :, half:]
    dz_slot = jnp.einsum("rks,srj->rkj", at_rel, dz_back, preferred_element_type=jnp.float32)
    attr = (act_grid.astype(jnp.float32) * dz_slot).reshape(rows, listed * block)
    width = half * lax.axis_size("section")
    s = jnp.where(is_own, small, other_small)
    gain_half = lax.dynamic_slice_in_dim(s[:width], lax.axis_index("section") * half, half, axis=0)
    scale_l = s[width:width + rows]
    new_half = (g_half.astype(jnp.float32) + scale_l[:, None] * gain_half[None, :] * total).astype(
        jnp.bfloat16
    )
    return attr, new_half, other_small


def split_device(cotangent, routes, acts, decoder, encoder, gain, inv_rms):
    depth = lax.axis_size("section")
    here = lax.axis_index("section")
    rows, width = cotangent.shape
    blocks = decoder.shape[1]
    half = width // depth
    mine = here * half
    theirs = (1 - here) * half
    small = jnp.concatenate([gain[0], inv_rms[0]], axis=0)
    other_small = None
    halves = []
    sent_w = jnp.concatenate(
        [
            lax.dynamic_slice_in_dim(decoder[0], theirs, half, axis=1),
            lax.dynamic_slice_in_dim(encoder[0], theirs, half, axis=1),
        ],
        axis=0,
    )
    other_w = swap_cores(sent_w)
    other = (other_w[:blocks], other_w[blocks:])
    own = (
        lax.dynamic_slice_in_dim(decoder[0], mine, half, axis=1),
        lax.dynamic_slice_in_dim(encoder[0], mine, half, axis=1),
    )
    attr_keep = jnp.zeros((rows, acts.shape[2]), jnp.float32)
    grad_keep = jnp.zeros(cotangent.shape, jnp.bfloat16)
    g_half = lax.dynamic_slice_in_dim(cotangent, mine, half, axis=1)
    for layer in reversed(range(depth)):
        is_own = here == layer
        attr, g_half, other_small = split_layer(
            g_half, routes[0], acts[0], own, other, is_own, small, other_small
        )
        halves.append(g_half)
        attr_keep = jnp.where(is_own, attr, attr_keep)
    mine_both = jnp.stack(halves, axis=0)
    theirs_both = swap_cores(mine_both)
    for step, layer in enumerate(reversed(range(depth))):
        full = jnp.where(
            here == 0,
            jnp.concatenate([mine_both[step], theirs_both[step]], axis=1),
            jnp.concatenate([theirs_both[step], mine_both[step]], axis=1),
        )
        grad_keep = jnp.where(here == layer, full, grad_keep)
    return (attr_keep[None], grad_keep[None])


def per_device(cotangent, routes, acts, decoder, encoder, gain, inv_rms):
    peers = lax.axis_size("dict")
    depth = lax.axis_size("section")
    listed = routes.shape[-1]
    width = cotangent.shape[1]
    if listed == peers and peers & (peers - 1) == 0 and depth == 2 and width % (depth * 128) == 0:
        return split_device(cotangent, routes, acts, decoder, encoder, gain, inv_rms)
    return slot_device(cotangent, routes, acts, decoder, encoder, gain, inv_rms)


def solution(mesh):
    placed = (
        P(("groups", "dict"), None),
        P("section", ("groups", "dict"), None),
        P("section", ("groups", "dict"), None),
        P("section", "dict", None),
        P("section", "dict", None),
        P("section", None),
        P("section", ("groups", "dict")),
    )
    return jax.shard_map(
        per_device,
        mesh=mesh,
        in_specs=placed,
        out_specs=(P("section", ("groups", "dict"), None), P("section", ("groups", "dict"), None)),
        check_vma=False,
    )
```

```python
import jax
import jax.numpy as jnp
from jax import lax
from jax.sharding import PartitionSpec as P


def passed_along(block, axis, distance):
    devices = range(lax.axis_size(axis))
    route = [(i - distance, i) for i in devices if i - distance in devices]
    return lax.ppermute(block, axis, route)


def owner_work(recv_g, recv_act, dec_local, enc_local):
    width = recv_g.shape[-1]
    columns = dec_local.shape[0]
    flat_g = recv_g.reshape(-1, width)
    flat_act = recv_act.reshape(-1, columns)
    coef = lax.dot_general(
        flat_g, dec_local, (((1,), (1,)), ((), ())), preferred_element_type=jnp.float32
    ).astype(jnp.bfloat16)
    masked = jnp.where(flat_act > 0, coef, jnp.zeros_like(coef))
    contrib = jnp.dot(masked, enc_local, preferred_element_type=jnp.float32).astype(jnp.bfloat16)
    lead = recv_g.shape[:-1]
    return (coef.reshape(lead + (columns,)), contrib.reshape(lead + (width,)))


def layer_pass(g_rows, routes_l, acts_l, dec_local, enc_local, gain_l, scale_l, peers):
    tok_count, listed = routes_l.shape
    block = acts_l.shape[1] // listed
    width = dec_local.shape[1]
    held = dec_local.shape[0] // block
    slots_per = (tok_count * listed + peers - 1) // peers
    total_slots = peers * slots_per
    owner = routes_l // held
    within = routes_l - owner * held
    owners = jnp.arange(peers, dtype=jnp.int32)
    hits = (owner[:, :, None] == owners[None, None, :]).astype(jnp.int32)
    per_row = jnp.sum(hits, axis=1)
    earlier = jnp.cumsum(per_row, axis=0) - per_row
    place = jnp.sum(hits * earlier[:, None, :], axis=2)
    slot_of = (owner * slots_per + place).reshape(-1)
    slot_ids = jnp.arange(total_slots, dtype=jnp.int32)
    pick = (slot_ids[:, None] == slot_of[None, :]).astype(jnp.bfloat16)
    row_pick = jnp.sum(
        pick.reshape(total_slots, tok_count, listed).astype(jnp.float32), axis=2
    ).astype(jnp.bfloat16)
    send_g = jnp.dot(row_pick, g_rows, preferred_element_type=jnp.float32).astype(jnp.bfloat16)
    block_act = jnp.dot(
        pick, acts_l.reshape(tok_count * listed, block), preferred_element_type=jnp.float32
    ).astype(jnp.bfloat16)
    within_hot = (within.reshape(-1)[:, None] == jnp.arange(held, dtype=jnp.int32)[None, :]).astype(
        jnp.bfloat16
    )
    slot_within = jnp.dot(pick, within_hot, preferred_element_type=jnp.float32).astype(jnp.bfloat16)
    send_act = (slot_within[:, :, None] * block_act[:, None, :]).reshape(total_slots, held * block)
    send_g = send_g.reshape(peers, slots_per, width)
    send_act = send_act.reshape(peers, slots_per, held * block)
    recv_g, recv_act = (
        lax.all_to_all(send_g, "dict", split_axis=0, concat_axis=0, tiled=True),
        lax.all_to_all(send_act, "dict", split_axis=0, concat_axis=0, tiled=True),
    )
    coef_here, contrib_here = owner_work(recv_g, recv_act, dec_local, enc_local)
    coef_back, contrib_back = (
        lax.all_to_all(coef_here, "dict", split_axis=0, concat_axis=0, tiled=True),
        lax.all_to_all(contrib_here, "dict", split_axis=0, concat_axis=0, tiled=True),
    )
    coef_back = coef_back.reshape(total_slots, held, block)
    contrib_back = contrib_back.reshape(total_slots, width)
    coef_chosen = jnp.sum(
        slot_within.astype(jnp.float32)[:, :, None] * coef_back.astype(jnp.float32), axis=1
    ).astype(jnp.bfloat16)
    coef_rows = lax.dot_general(
        pick, coef_chosen, (((0,), (0,)), ((), ())), preferred_element_type=jnp.float32
    )
    attr = (acts_l.reshape(tok_count * listed, block).astype(jnp.float32) * coef_rows).reshape(
        tok_count, listed * block
    )
    summed = lax.dot_general(
        row_pick, contrib_back, (((0,), (0,)), ((), ())), preferred_element_type=jnp.float32
    )
    new_g = (g_rows.astype(jnp.float32) + scale_l[:, None] * gain_l[None, :] * summed).astype(
        jnp.bfloat16
    )
    return (attr, new_g)


def slot_device(cotangent, routes, acts, decoder, encoder, gain, inv_rms):
    peers = lax.axis_size("dict")
    depth = lax.axis_size("section")
    here = lax.axis_index("section")
    routes_l = routes[0]
    acts_l = acts[0]
    dec_local = decoder[0]
    enc_local = encoder[0]
    gain_l = gain[0]
    scale_l = inv_rms[0]
    tok_count, listed = routes_l.shape
    attr_keep = jnp.zeros((tok_count, acts_l.shape[1]), jnp.float32)
    grad_keep = jnp.zeros(cotangent.shape, jnp.bfloat16)
    g_new = cotangent
    for turn in range(depth):
        if turn > 0:
            g_now = passed_along(g_new, "section", -1)
        else:
            g_now = cotangent
        active = here == depth - 1 - turn
        attr, g_new = layer_pass(
            g_now, routes_l, acts_l, dec_local, enc_local, gain_l, scale_l, peers
        )
        attr_keep = jnp.where(active, attr, attr_keep)
        grad_keep = jnp.where(active, g_new, grad_keep)
    return (attr_keep[None], grad_keep[None])


def swap_cores(block):
    return lax.ppermute(block, "section", [(0, 1), (1, 0)])


def exchange(parts, sign):
    peers = parts.shape[0]
    moved = [parts[0]]
    for shift in range(1, peers):
        route = [(d, d ^ (peers - shift)) for d in range(peers)]
        moved.append(lax.ppermute(parts[shift], "dict", route))
    return jnp.stack(moved, axis=0)


def split_layer(g_half, routes_l, acts_l, own, other, is_own, small, other_small, early=None):
    peers = lax.axis_size("dict")
    me = lax.axis_index("dict")
    rows, listed = routes_l.shape
    block = acts_l.shape[1] // listed
    held = own[0].shape[0] // block
    half = g_half.shape[1]
    owner = routes_l // held
    within = routes_l - owner * held
    rel = (peers - lax.bitwise_xor(owner, me)) % peers
    shifts = jnp.arange(peers, dtype=jnp.int32)
    at_rel = (rel[:, :, None] == shifts[None, None, :]).astype(jnp.bfloat16)
    act_grid = acts_l.reshape(rows, listed, block)
    live = (act_grid > 0).astype(jnp.bfloat16) * (1 + within).astype(jnp.bfloat16)[:, :, None]
    placed = jnp.einsum(
        "rks,rkj->srj", at_rel, live, preferred_element_type=jnp.float32
    ).astype(jnp.bfloat16)
    sent = jnp.concatenate(
        [jnp.broadcast_to(g_half[None], (peers, rows, half)), placed], axis=-1
    )
    got = exchange(sent, 1).reshape(peers * rows, half + block)
    if early is not None:
        early, got = lax.optimization_barrier((early, got))
        early = swap_cores(early)
    if other_small is None:
        small, got = lax.optimization_barrier((small, got))
        other_small = swap_cores(small)
    g_all = got[:, :half]
    code_all = got[:, half:]

    def with_dec(dec):
        return lax.dot_general(
            g_all, dec, (((1,), (1,)), ((), ())), preferred_element_type=jnp.float32
        )

    part = jnp.where(is_own, with_dec(own[0]), with_dec(other[0]))
    paired = swap_cores(jnp.concatenate([part, code_all.astype(jnp.float32)], axis=1))
    coef = (part + paired[:, :held * block]).astype(jnp.bfloat16)
    code = jnp.where(is_own, code_all.astype(jnp.float32), paired[:, held * block:])
    marks = jnp.concatenate([code == spot + 1 for spot in range(held)], axis=1)
    dz = jnp.where(marks, coef, jnp.zeros_like(coef))

    def with_enc(enc):
        return jnp.dot(dz, enc, preferred_element_type=jnp.float32)

    contrib = jnp.where(is_own, with_enc(own[1]), with_enc(other[1])).astype(jnp.bfloat16)
    dz_pick = dz[:, :block]
    for spot in range(1, held):
        dz_pick = dz_pick + dz[:, spot * block:(spot + 1) * block]
    back = jnp.concatenate([contrib, dz_pick], axis=-1).reshape(peers, rows, half + block)
    returned = exchange(back, -1)
    total = jnp.sum(returned[:, :, :half].astype(jnp.float32), axis=0)
    dz_back = returned[:, :, half:]
    dz_slot = jnp.einsum("rks,srj->rkj", at_rel, dz_back, preferred_element_type=jnp.float32)
    attr = (act_grid.astype(jnp.float32) * dz_slot).reshape(rows, listed * block)
    width = half * lax.axis_size("section")
    s = jnp.where(is_own, small, other_small)
    gain_half = lax.dynamic_slice_in_dim(s[:width], lax.axis_index("section") * half, half, axis=0)
    scale_l = s[width:width + rows]
    new_half = (g_half.astype(jnp.float32) + scale_l[:, None] * gain_half[None, :] * total).astype(
        jnp.bfloat16
    )
    return attr, new_half, other_small, early


def split_device(cotangent, routes, acts, decoder, encoder, gain, inv_rms):
    depth = lax.axis_size("section")
    here = lax.axis_index("section")
    rows, width = cotangent.shape
    blocks = decoder.shape[1]
    half = width // depth
    mine = here * half
    theirs = (1 - here) * half
    small = jnp.concatenate([gain[0], inv_rms[0]], axis=0)
    other_small = None
    halves = []
    sent_w = jnp.concatenate(
        [
            lax.dynamic_slice_in_dim(decoder[0], theirs, half, axis=1),
            lax.dynamic_slice_in_dim(encoder[0], theirs, half, axis=1),
        ],
        axis=0,
    )
    other_w = swap_cores(sent_w)
    other = (other_w[:blocks], other_w[blocks:])
    own = (
        lax.dynamic_slice_in_dim(decoder[0], mine, half, axis=1),
        lax.dynamic_slice_in_dim(encoder[0], mine, half, axis=1),
    )
    attr_keep = jnp.zeros((rows, acts.shape[2]), jnp.float32)
    grad_keep = jnp.zeros(cotangent.shape, jnp.bfloat16)
    g_half = lax.dynamic_slice_in_dim(cotangent, mine, half, axis=1)
    lent = None
    fulls = []
    for layer in reversed(range(depth)):
        is_own = here == layer
        attr, g_half, other_small, lent = split_layer(
            g_half, routes[0], acts[0], own, other, is_own, small, other_small,
            halves[-1] if halves else None,
        )
        if lent is not None:
            fulls.append((halves[-1], lent))
        halves.append(g_half)
        attr_keep = jnp.where(is_own, attr, attr_keep)
    fulls.append((halves[-1], swap_cores(halves[-1])))
    for (mine_h, theirs_h), layer in zip(fulls, reversed(range(depth))):
        full = jnp.where(
            here == 0,
            jnp.concatenate([mine_h, theirs_h], axis=1),
            jnp.concatenate([theirs_h, mine_h], axis=1),
        )
        grad_keep = jnp.where(here == layer, full, grad_keep)
    return (attr_keep[None], grad_keep[None])


def per_device(cotangent, routes, acts, decoder, encoder, gain, inv_rms):
    peers = lax.axis_size("dict")
    depth = lax.axis_size("section")
    listed = routes.shape[-1]
    width = cotangent.shape[1]
    if listed == peers and peers & (peers - 1) == 0 and depth == 2 and width % (depth * 128) == 0:
        return split_device(cotangent, routes, acts, decoder, encoder, gain, inv_rms)
    return slot_device(cotangent, routes, acts, decoder, encoder, gain, inv_rms)


def solution(mesh):
    placed = (
        P(("groups", "dict"), None),
        P("section", ("groups", "dict"), None),
        P("section", ("groups", "dict"), None),
        P("section", "dict", None),
        P("section", "dict", None),
        P("section", None),
        P("section", ("groups", "dict")),
    )
    return jax.shard_map(
        per_device,
        mesh=mesh,
        in_specs=placed,
        out_specs=(P("section", ("groups", "dict"), None), P("section", ("groups", "dict"), None)),
        check_vma=False,
    )
```
